32 devices in a mesh: replica: 8 (over z, x), tensor: 4 (over y, core).
Axes of the slice: x: 2, y: 2, z: 4, core: 2. Of those that a mesh axis runs over, the one named last changes fastest.
Arguments:
- hidden: bfloat16 [256, 8192], P('replica', 'tensor'), may hold values from -600 to 600
- input_norm_gain: float32 [8192], replicated, may hold values from 0.1 to 1.9
- key_value_weight: bfloat16 [8192, 2, 1024], P(None, None, 'tensor'), may hold values from -0.0625 to 0.0625
- adapter_down: bfloat16 [128, 8192, 128], P('replica', 'tensor'), may hold values from -0.0625 to 0.0625
- adapter_up: bfloat16 [128, 2, 64, 1024], P('replica', None, None, 'tensor'), may hold values from -0.75 to 0.75
- query: bfloat16 [256, 8192], P('replica', 'tensor'), may hold values from -6 to 6
- key_value_cache: bfloat16 [256, 512, 2, 1024], P('replica', None, None, 'tensor'), may hold values from -6 to 6
- segment_adapter: int32 [8, 16], P('replica'), may hold values from 0 to 127, as said below
- segment_sizes: int32 [8, 16], P('replica'), may hold values from 1 to 4, 32 in all within a row
- cached_length: int32 [256], P('replica'), may hold values from 2 to 512, as said below
Outputs:
- new_kv: bfloat16 [256, 2, 1024], P('replica', None, 'tensor')
- attended: bfloat16 [256, 8192], P('replica', 'tensor')
The draws below stay inside these ranges and needn't reach their ends.
Inputs may be any that keep to these rules, and one draw needn't show every extreme that they name: `segment_adapter`: the segments of one replica name distinct adapters; adapter a is stored at index a // 16 of replica. At most 2 of one replica's segments name adapters stored at one index of replica, and in every replica's list some index of replica is named exactly 2 times. `segment_sizes`: the sizes of one replica's segments sum to 32. The new token takes position cached_length.
All inputs are finite; a program needn't handle non-finite values.
Results may differ from the reference program's by a relative error of at most 0.0058.
Values may be sent and summed in bfloat16 or wider, within the bound.
No kernel may reach another device: no remote copies, remote signals or barrier semaphores. Data moves between devices by JAX's collectives and lax.ppermute only.
A program may use at most 192 MiB of HBM per device.

```python
import math
import jax
import jax.numpy as jnp
import numpy as np
from jax import lax

MODEL_WIDTH = 8192
HEADS = 64
KV_HEADS = 8
HEAD = 128
ADAPTER_RANK = 64
ADP_DEV = 16
SEG_DEV = 16
SLOT = 4
CAP = 2
REPLICA_REQUESTS = 32
CACHE = 512
KEY_VALUE_WIDTH = 1024
REPLICAS = 8
REQUESTS = 256
ADAPTER_COUNT = 128


def draw_hidden(key, part):
    row_scale = 10.0 ** jax.random.uniform(jax.random.fold_in(key, 11), (REQUESTS, 1), jnp.float32)
    col_scale = 10.0 ** jax.random.uniform(jax.random.fold_in(key, 12), (1, MODEL_WIDTH), jnp.float32)
    values = jax.random.truncated_normal(jax.random.fold_in(key, 13), -6.0, 6.0, (REQUESTS, MODEL_WIDTH), jnp.float32)
    return (values * row_scale * col_scale).astype(jnp.bfloat16)


def draw_query(key, part):
    values = jax.random.truncated_normal(jax.random.fold_in(key, 1), -6.0, 6.0, (REQUESTS, HEADS * HEAD), jnp.float32)
    return values.astype(jnp.bfloat16)


def draw_key_value_cache(key, part):
    values = jax.random.truncated_normal(jax.random.fold_in(key, 2), -6.0, 6.0, (REQUESTS, CACHE, 2, KEY_VALUE_WIDTH), jnp.float32)
    return values.astype(jnp.bfloat16)


def draw_cached_length(key, part):
    top_power = int(math.log2(CACHE))
    expo = jax.random.randint(jax.random.fold_in(key, 3), (REQUESTS,), 1, top_power + 1, jnp.int32)
    lower = jnp.left_shift(jnp.ones_like(expo), expo)
    extra = jax.random.randint(jax.random.fold_in(key, 4), (REQUESTS,), 0, 1 << 30, jnp.int32) % lower
    lengths = jnp.minimum(lower + extra, CACHE)
    place = jnp.arange(REQUESTS, dtype=jnp.int32) % REPLICA_REQUESTS
    lengths = jnp.where(place == 0, CACHE, jnp.where(place == 1, 2, lengths))
    return lengths.astype(jnp.int32)


def draw_segment_adapter(key, part):
    hot_owner = jax.random.randint(jax.random.fold_in(key, 5), (), 0, REPLICAS, jnp.int32)

    def one_replica(sub_key):
        spread_ids = jnp.arange((REPLICAS - 1) * CAP, dtype=jnp.int32) // CAP
        others = spread_ids + (spread_ids >= hot_owner).astype(jnp.int32)
        others = jax.random.permutation(jax.random.fold_in(sub_key, 1), others)[:SEG_DEV - CAP]
        owners = jnp.concatenate([jnp.full((CAP,), hot_owner, jnp.int32), others.astype(jnp.int32)])
        owners = jax.random.permutation(jax.random.fold_in(sub_key, 2), owners)
        local_ids = jax.random.permutation(jax.random.fold_in(sub_key, 3), ADP_DEV)[:SEG_DEV].astype(jnp.int32)
        return owners * ADP_DEV + local_ids
    sub_keys = jax.random.split(jax.random.fold_in(key, 6), REPLICAS)
    return jax.vmap(one_replica)(sub_keys).astype(jnp.int32)


def level_of(own_key, shape, cuts, low, largest):
    def one(axis_at, shards_of):
        steps = jax.random.uniform(jax.random.fold_in(jax.random.fold_in(own_key, 6), axis_at), (shards_of,), jnp.float32, low / len(cuts), largest / len(cuts))
        return jnp.repeat(jnp.exp(steps), shape[axis_at] // shards_of).reshape((-1,) + (1,) * (len(shape) - axis_at - 1))

    loudness = one(*cuts[0])
    for cut in cuts[1:]:
        loudness = loudness * one(*cut)
    return loudness


def length_profile(amount, total, reach, lean):
    portions = [(1 << 20) // math.isqrt(grade ** lean) + 1 for grade in range(2, amount + 1)]
    rest, holding = total - reach - (amount - 1), [1] * (amount - 1)
    while rest > 0:
        free = [i for i in range(amount - 1) if holding[i] < reach]
        whole, remaining = sum([portions[i] for i in free]), rest
        for i in free:
            addition = min(reach - holding[i], max(1, remaining * portions[i] // whole), rest)
            holding[i] = holding[i] + addition
            rest = rest - addition
    return np.array([reach] + holding)


def uneven_parts(own_key, count, total, bound, skew):
    if count == 2:
        one = jax.random.randint(own_key, (), max(1, total - bound), min(bound, total - 1) + 1)
        return jnp.stack([one, total - one])
    tallies = jnp.asarray(length_profile(count, total, bound, skew), jnp.int32)
    twos = (count - 1) // 2
    source_of, receiver = tallies[1:1 + 2 * twos:2], tallies[2:2 + 2 * twos:2]
    margin = jnp.minimum(source_of - 1, bound - receiver)
    shifted = jax.random.randint(jax.random.fold_in(own_key, 1), (twos,), 0, 1 << 20) % (margin + 1)
    tallies = tallies.at[1:1 + 2 * twos:2].set(source_of - shifted).at[2:2 + 2 * twos:2].set(receiver + shifted)
    return tallies[jax.random.permutation(jax.random.fold_in(own_key, 2), count)]


def scatter_about(key, dims, deviation, most, cuts=(), held_as=jnp.bfloat16):
    drawn = jax.random.normal(key, dims, jnp.float32) * deviation
    if len(cuts) > 0:
        drawn = level_of(key, dims, cuts, -0.22, 0.18) * drawn
    return jnp.clip(drawn, min=-most, max=most).astype(held_as)


def setup_inputs(seed: int = 0) -> dict:
    key_of = jax.random.split(jax.random.key(seed), 11)
    return {
        "hidden": draw_hidden(jax.random.fold_in(key_of[10], 71), 0),
        "input_norm_gain": jnp.clip(1.0 + 0.18 * jax.random.normal(key_of[1], (MODEL_WIDTH,), jnp.float32), 0.1, 1.9),
        "key_value_weight": scatter_about(key_of[2], (MODEL_WIDTH, 2, KEY_VALUE_WIDTH), MODEL_WIDTH ** -0.5, 0.0625, ((2, 4),)),
        "adapter_down": scatter_about(key_of[3], (ADAPTER_COUNT, MODEL_WIDTH, 2 * ADAPTER_RANK), MODEL_WIDTH ** -0.5, 0.0625, ((0, 8), (1, 4))),
        "adapter_up": scatter_about(key_of[4], (ADAPTER_COUNT, 2, ADAPTER_RANK, KEY_VALUE_WIDTH), ADAPTER_RANK ** -0.5, 0.75, ((0, 8), (3, 4))),
        "query": draw_query(jax.random.fold_in(key_of[10], 71), 0),
        "key_value_cache": draw_key_value_cache(jax.random.fold_in(key_of[10], 71), 0),
        "segment_adapter": draw_segment_adapter(jax.random.fold_in(key_of[10], 71), 0),
        "segment_sizes": jax.vmap(lambda own: uneven_parts(own, SEG_DEV, REPLICA_REQUESTS, SLOT, 2))(jax.random.split(key_of[8], REPLICAS)).reshape((REPLICAS, SEG_DEV)).astype(jnp.int32),
        "cached_length": draw_cached_length(jax.random.fold_in(key_of[10], 71), 0),
    }


ADAPTER_SCALE = 0.5
ROPE_BASE = 500000.0
EPSILON = 1e-05

def rotate(key_heads, token_position):
    half_size = key_heads.shape[-1] // 2
    inv_freq = ROPE_BASE ** (-(jnp.arange(half_size, dtype=jnp.float32) * 2.0) / key_heads.shape[-1])
    angles = token_position.astype(jnp.float32)[:, None] * inv_freq[None, :]
    cosine_term = jnp.cos(angles)[:, None, :]
    sine_term = jnp.sin(angles)[:, None, :]
    first_half = key_heads[..., :half_size]
    second_half = key_heads[..., half_size:]
    return jnp.concatenate([first_half * cosine_term - second_half * sine_term, second_half * cosine_term + first_half * sine_term], axis=-1)

def attend(queries, kv_block, new_kv, lengths):
    row_count = queries.shape[0]
    group_size = HEADS // KV_HEADS
    scale = float(HEAD) ** (-0.5)
    query_heads = queries.astype(jnp.float32).reshape(row_count, KV_HEADS, group_size, HEAD)
    cached_keys = kv_block[:, :, 0].astype(jnp.float32).reshape(row_count, CACHE, KV_HEADS, HEAD)
    cached_values = kv_block[:, :, 1].astype(jnp.float32).reshape(row_count, CACHE, KV_HEADS, HEAD)
    scores = jnp.einsum('bhgd,bthd->bhgt', query_heads, cached_keys) * scale
    is_live = jnp.arange(CACHE, dtype=jnp.int32)[None, :] < lengths[:, None]
    scores = jnp.where(is_live[:, None, None, :], scores, -jnp.inf)
    new_key = new_kv[:, 0].astype(jnp.float32).reshape(row_count, KV_HEADS, HEAD)
    new_value = new_kv[:, 1].astype(jnp.float32).reshape(row_count, KV_HEADS, HEAD)
    own_score = jnp.einsum('bhgd,bhd->bhg', query_heads, new_key) * scale
    top_score = jnp.maximum(lax.optimization_barrier(jnp.max(scores, axis=-1)), own_score)
    weights = jnp.exp(scores - top_score[..., None])
    own_weight = jnp.exp(own_score - top_score)
    total_mass = lax.optimization_barrier(jnp.sum(weights, axis=-1)) + own_weight
    prob_rows = (weights / total_mass[..., None]).astype(jnp.bfloat16)
    own_prob = (own_weight / total_mass).astype(jnp.bfloat16)
    context = jnp.einsum('bhgt,bthd->bhgd', prob_rows.astype(jnp.float32), cached_values)
    context = context + own_prob.astype(jnp.float32)[..., None] * new_value[:, :, None, :]
    return context.reshape(row_count, HEADS * HEAD).astype(jnp.bfloat16)

def reference(hidden, input_norm_gain, key_value_weight, adapter_down, adapter_up, query, key_value_cache, segment_adapter, segment_sizes, cached_length):

    def one_replica(pieces):
        states, seg_counts, adapters, lengths, queries, kv_block = pieces
        widened = states.astype(jnp.float32)
        normed = (widened * lax.rsqrt(lax.optimization_barrier(jnp.mean(widened * widened, axis=1, keepdims=True)) + EPSILON) * input_norm_gain).astype(jnp.bfloat16)
        seg_ends = jnp.cumsum(seg_counts, dtype=jnp.int32)
        row_ids = jnp.arange(REPLICA_REQUESTS, dtype=jnp.int32)
        segment_index = lax.optimization_barrier(jnp.sum((seg_ends[None, :] <= row_ids[:, None]).astype(jnp.int32), axis=1)).astype(jnp.int32)
        adapter_index = adapters[segment_index]
        down_matrix_rows = adapter_down[adapter_index].astype(jnp.float32)
        reduced_features = jnp.einsum('jd,jdr->jr', normed.astype(jnp.float32), down_matrix_rows).astype(jnp.bfloat16)
        up_matrix_rows = adapter_up[adapter_index].astype(jnp.float32)
        adapter_delta = ADAPTER_SCALE * jnp.einsum('vhb,vhbg->vhg', reduced_features.astype(jnp.float32).reshape(REPLICA_REQUESTS, 2, ADAPTER_RANK), up_matrix_rows)
        base_projection = jnp.dot(normed, key_value_weight.reshape(MODEL_WIDTH, 2 * KEY_VALUE_WIDTH), preferred_element_type=jnp.float32).reshape(REPLICA_REQUESTS, 2, KEY_VALUE_WIDTH)
        current_key_value = base_projection + adapter_delta
        rotated = rotate(current_key_value[:, 0].reshape(REPLICA_REQUESTS, KV_HEADS, HEAD), lengths).reshape(REPLICA_REQUESTS, KEY_VALUE_WIDTH)
        new_kv = jnp.stack([rotated, current_key_value[:, 1]], axis=1).astype(jnp.bfloat16)
        return (new_kv, attend(queries, kv_block, new_kv, lengths))
    stacked = (hidden.reshape(REPLICAS, REPLICA_REQUESTS, MODEL_WIDTH), segment_sizes, segment_adapter, cached_length.reshape(REPLICAS, REPLICA_REQUESTS), query.reshape(REPLICAS, REPLICA_REQUESTS, HEADS * HEAD), key_value_cache.reshape(REPLICAS, REPLICA_REQUESTS, CACHE, 2, KEY_VALUE_WIDTH))
    new_kv, attended = lax.map(one_replica, stacked)
    return (new_kv.reshape(REQUESTS, 2, KEY_VALUE_WIDTH), attended.reshape(REQUESTS, HEADS * HEAD))
```

```python
import functools

import jax
import jax.numpy as jnp
from jax import lax
from jax.experimental import pallas as pl
from jax.experimental.pallas import tpu as pltpu
from jax.sharding import PartitionSpec as P

HEAD = 128
ADP_DEV = 16
SLOT = 4
CAP = 2


ADAPTER_SCALE = 0.5
ROPE_BASE = 500000.0
EPSILON = 1e-05


def rotate(key_heads, token_position):
    half_size = key_heads.shape[-1] // 2
    inv_freq = ROPE_BASE ** (
        -(jnp.arange(half_size, dtype=jnp.float32) * 2.0) / key_heads.shape[-1]
    )
    angles = token_position.astype(jnp.float32)[:, None] * inv_freq[None, :]
    cosine_term = jnp.cos(angles)[:, None, :]
    sine_term = jnp.sin(angles)[:, None, :]
    first_half = key_heads[..., :half_size]
    second_half = key_heads[..., half_size:]
    return jnp.concatenate(
        [
            first_half * cosine_term - second_half * sine_term,
            second_half * cosine_term + first_half * sine_term,
        ],
        axis=-1,
    )


def attention_kernel(len_ref, q_ref, kv_ref, nkv_ref, o_ref, *, rows, kv_local, group_size):
    scale = float(HEAD) ** (-0.5)
    step = pl.program_id(0)
    cache_len = kv_ref.shape[1]
    for i in range(rows):
        length = len_ref[step * rows + i]
        keys = kv_ref[i, :, 0, :]
        values = kv_ref[i, :, 1, :]
        live = lax.broadcasted_iota(jnp.int32, (group_size, cache_len), 1) < length
        for h in range(kv_local):
            cols = slice(h * HEAD, (h + 1) * HEAD)
            qrows = slice(h * group_size, (h + 1) * group_size)
            q = q_ref[i, qrows, :]
            scores = lax.dot_general(
                q, keys[:, cols], (((1,), (1,)), ((), ())), preferred_element_type=jnp.float32
            ) * scale
            scores = jnp.where(live, scores, -jnp.inf)
            new_key = nkv_ref[i, 0:1, cols].astype(jnp.float32)
            new_value = nkv_ref[i, 1:2, cols].astype(jnp.float32)
            own = jnp.sum(q.astype(jnp.float32) * new_key, axis=1, keepdims=True) * scale
            top = jnp.maximum(jnp.max(scores, axis=1, keepdims=True), own)
            weights = jnp.exp(scores - top)
            own_weight = jnp.exp(own - top)
            total = jnp.sum(weights, axis=1, keepdims=True) + own_weight
            probs = (weights / total).astype(jnp.bfloat16)
            own_prob = (own_weight / total).astype(jnp.bfloat16).astype(jnp.float32)
            context = jnp.dot(probs, values[:, cols], preferred_element_type=jnp.float32)
            context = context + own_prob * new_value
            o_ref[i, qrows, :] = context.astype(o_ref.dtype)


def attend(query, key_value_cache, new_kv, cached_length, kv_local, group_size):
    row_count = query.shape[0]
    cache_len = key_value_cache.shape[1]
    width = key_value_cache.shape[3]
    heads = kv_local * group_size
    rows = 4
    query_heads = query.reshape(row_count, heads, HEAD)
    kernel = functools.partial(
        attention_kernel, rows=rows, kv_local=kv_local, group_size=group_size
    )
    out = pl.pallas_call(
        kernel,
        out_shape=jax.ShapeDtypeStruct((row_count, heads, HEAD), jnp.bfloat16),
        grid_spec=pltpu.PrefetchScalarGridSpec(
            num_scalar_prefetch=1,
            grid=(row_count // rows,),
            in_specs=[
                pl.BlockSpec((rows, heads, HEAD), lambda b, lens: (b, 0, 0)),
                pl.BlockSpec((rows, cache_len, 2, width), lambda b, lens: (b, 0, 0, 0)),
                pl.BlockSpec((rows, 2, width), lambda b, lens: (b, 0, 0)),
            ],
            out_specs=pl.BlockSpec((rows, heads, HEAD), lambda b, lens: (b, 0, 0)),
        ),
    )(cached_length, query_heads, key_value_cache, new_kv)
    return out.reshape(row_count, heads * HEAD)


def body(
    hidden,
    input_norm_gain,
    key_value_weight,
    adapter_down,
    adapter_up,
    query,
    key_value_cache,
    segment_adapter,
    segment_sizes,
    cached_length,
):
    row_count = hidden.shape[0]
    part_width = hidden.shape[1]
    kv_width = key_value_weight.shape[2]
    kv_local = kv_width // HEAD
    cache_len = key_value_cache.shape[1]
    adapter_rank_size = adapter_up.shape[2]
    replicas = lax.axis_size("replica")
    segments = segment_sizes.shape[1]
    gathered = lax.all_gather(hidden, "tensor", axis=1, tiled=True)
    widened = gathered.astype(jnp.float32)
    normed = (
        widened
        * lax.rsqrt(jnp.mean(widened * widened, axis=1, keepdims=True) + EPSILON)
        * input_norm_gain
    ).astype(jnp.bfloat16)
    own_cols = lax.dynamic_slice_in_dim(
        normed, lax.axis_index("tensor") * part_width, part_width, 1
    )
    seg_counts = segment_sizes[0]
    adapters = segment_adapter[0]
    seg_ends = jnp.cumsum(seg_counts, dtype=jnp.int32)
    starts = seg_ends - seg_counts
    offsets = jnp.arange(SLOT, dtype=jnp.int32)
    row_ids = jnp.arange(row_count, dtype=jnp.int32)
    segment_index = jnp.sum((seg_ends[None, :] <= row_ids[:, None]).astype(jnp.int32), axis=1)
    token_position = row_ids - starts[segment_index]
    owners = adapters // ADP_DEV
    local_ids = adapters % ADP_DEV
    seg_ids = jnp.arange(segments, dtype=jnp.int32)
    slot_rank = jnp.sum(
        ((owners[None, :] == owners[:, None]) & (seg_ids[None, :] < seg_ids[:, None])).astype(
            jnp.int32
        ),
        axis=1,
    )
    owner_hit = (owners[None, None, :] == jnp.arange(replicas, dtype=jnp.int32)[:, None, None]) & (
        slot_rank[None, None, :] == jnp.arange(CAP, dtype=jnp.int32)[None, :, None]
    )
    wanted = jnp.sum(jnp.where(owner_hit, local_ids[None, None, :], 0), axis=2)
    fetch_slot = owners * CAP + slot_rank
    seg_at = jnp.sum(jnp.where(owner_hit, seg_ids[None, None, :], 0), axis=2)
    filled = jnp.any(owner_hit, axis=2)
    slot_counts = jnp.where(filled, seg_counts[seg_at], 0)
    slot_live = offsets[None, None, :] < slot_counts[:, :, None]
    source_row = jnp.where(slot_live, starts[seg_at][:, :, None] + offsets[None, None, :], 0)
    slot_rows = jnp.where(
        slot_live[:, :, :, None], own_cols[source_row], jnp.zeros((), jnp.bfloat16)
    )
    segment_member_mask = lax.all_to_all(wanted, "replica", split_axis=0, concat_axis=0, tiled=True)
    selected_down = adapter_down[segment_member_mask]
    selected_up = adapter_up[segment_member_mask]
    down_got = lax.all_to_all(selected_down, "replica", split_axis=0, concat_axis=0, tiled=True)
    up_got = lax.all_to_all(selected_up, "replica", split_axis=0, concat_axis=0, tiled=True)
    partial_value = jnp.einsum(
        "oksd,okdr->oksr", slot_rows, down_got, preferred_element_type=jnp.float32
    )
    summed = lax.psum(partial_value, "tensor").astype(jnp.bfloat16)
    summed = summed.reshape(summed.shape[:3] + (2, adapter_rank_size))
    slot_delta = (
        jnp.einsum("okscr,okcrw->okscw", summed, up_got, preferred_element_type=jnp.float32)
        * ADAPTER_SCALE
    )
    flat_delta = slot_delta.reshape((replicas * CAP * SLOT,) + slot_delta.shape[3:])
    adapter_delta = flat_delta[fetch_slot[segment_index] * SLOT + token_position]
    base_projection = jnp.dot(
        normed,
        key_value_weight.reshape(key_value_weight.shape[0], 2 * kv_width),
        preferred_element_type=jnp.float32,
    ).reshape(row_count, 2, kv_width)
    current_key_value = base_projection + adapter_delta
    rotated = rotate(
        current_key_value[:, 0].reshape(row_count, kv_local, HEAD), cached_length
    ).reshape(row_count, kv_width)
    new_kv = jnp.stack([rotated, current_key_value[:, 1]], axis=1).astype(jnp.bfloat16)
    group_size = query.shape[1] // HEAD // kv_local
    attended = attend(query, key_value_cache, new_kv, cached_length, kv_local, group_size)
    return (new_kv, attended)


def solution(mesh):
    in_specs = (
        P("replica", "tensor"),
        P(),
        P(None, None, "tensor"),
        P("replica", "tensor", None),
        P("replica", None, None, "tensor"),
        P("replica", "tensor"),
        P("replica", None, None, "tensor"),
        P("replica", None),
        P("replica", None),
        P("replica"),
    )
    out_specs = (P("replica", None, "tensor"), P("replica", "tensor"))
    return jax.shard_map(body, mesh=mesh, in_specs=in_specs, out_specs=out_specs, check_vma=False)
```

```python
import functools

import jax
import jax.numpy as jnp
from jax import lax
from jax.experimental import pallas as pl
from jax.experimental.pallas import tpu as pltpu
from jax.sharding import PartitionSpec as P

HEAD = 128
ADP_DEV = 16
SLOT = 4
CAP = 2


ADAPTER_SCALE = 0.5
ROPE_BASE = 500000.0
EPSILON = 1e-05


def rotate(key_heads, token_position):
    half_size = key_heads.shape[-1] // 2
    inv_freq = ROPE_BASE ** (
        -(jnp.arange(half_size, dtype=jnp.float32) * 2.0) / key_heads.shape[-1]
    )
    angles = token_position.astype(jnp.float32)[:, None] * inv_freq[None, :]
    cosine_term = jnp.cos(angles)[:, None, :]
    sine_term = jnp.sin(angles)[:, None, :]
    first_half = key_heads[..., :half_size]
    second_half = key_heads[..., half_size:]
    return jnp.concatenate(
        [
            first_half * cosine_term - second_half * sine_term,
            second_half * cosine_term + first_half * sine_term,
        ],
        axis=-1,
    )


def attention_kernel(len_ref, q_ref, kv_ref, nkv_ref, o_ref, *, rows, kv_local, group_size):
    scale = float(HEAD) ** (-0.5)
    step = pl.program_id(0)
    cache_len = kv_ref.shape[1]
    for i in range(rows):
        length = len_ref[step * rows + i]
        keys = kv_ref[i, :, 0, :]
        values = kv_ref[i, :, 1, :]
        live = lax.broadcasted_iota(jnp.int32, (group_size, cache_len), 1) < length
        for h in range(kv_local):
            cols = slice(h * HEAD, (h + 1) * HEAD)
            qrows = slice(h * group_size, (h + 1) * group_size)
            q = q_ref[i, qrows, :]
            scores = lax.dot_general(
                q, keys[:, cols], (((1,), (1,)), ((), ())), preferred_element_type=jnp.float32
            ) * scale
            scores = jnp.where(live, scores, -jnp.inf)
            new_key = nkv_ref[i, 0:1, cols].astype(jnp.float32)
            new_value = nkv_ref[i, 1:2, cols].astype(jnp.float32)
            own = jnp.sum(q.astype(jnp.float32) * new_key, axis=1, keepdims=True) * scale
            top = jnp.maximum(jnp.max(scores, axis=1, keepdims=True), own)
            weights = jnp.exp(scores - top)
            own_weight = jnp.exp(own - top)
            total = jnp.sum(weights, axis=1, keepdims=True) + own_weight
            probs = (weights / total).astype(jnp.bfloat16)
            own_prob = (own_weight / total).astype(jnp.bfloat16).astype(jnp.float32)
            context = jnp.dot(probs, values[:, cols], preferred_element_type=jnp.float32)
            context = context + own_prob * new_value
            o_ref[i, qrows, :] = context.astype(o_ref.dtype)


def attend(query, key_value_cache, new_kv, cached_length, kv_local, group_size):
    row_count = query.shape[0]
    cache_len = key_value_cache.shape[1]
    width = key_value_cache.shape[3]
    heads = kv_local * group_size
    rows = 4
    query_heads = query.reshape(row_count, heads, HEAD)
    kernel = functools.partial(
        attention_kernel, rows=rows, kv_local=kv_local, group_size=group_size
    )
    out = pl.pallas_call(
        kernel,
        out_shape=jax.ShapeDtypeStruct((row_count, heads, HEAD), jnp.bfloat16),
        grid_spec=pltpu.PrefetchScalarGridSpec(
            num_scalar_prefetch=1,
            grid=(row_count // rows,),
            in_specs=[
                pl.BlockSpec((rows, heads, HEAD), lambda b, lens: (b, 0, 0)),
                pl.BlockSpec((rows, cache_len, 2, width), lambda b, lens: (b, 0, 0, 0)),
                pl.BlockSpec((rows, 2, width), lambda b, lens: (b, 0, 0)),
            ],
            out_specs=pl.BlockSpec((rows, heads, HEAD), lambda b, lens: (b, 0, 0)),
        ),
    )(cached_length, query_heads, key_value_cache, new_kv)
    return out.reshape(row_count, heads * HEAD)


def body(
    hidden,
    input_norm_gain,
    key_value_weight,
    adapter_down,
    adapter_up,
    query,
    key_value_cache,
    segment_adapter,
    segment_sizes,
    cached_length,
):
    row_count = hidden.shape[0]
    part_width = hidden.shape[1]
    kv_width = key_value_weight.shape[2]
    kv_local = kv_width // HEAD
    cache_len = key_value_cache.shape[1]
    adapter_rank_size = adapter_up.shape[2]
    replicas = lax.axis_size("replica")
    segments = segment_sizes.shape[1]
    gathered = lax.all_gather(hidden, "tensor", axis=1, tiled=True)
    widened = gathered.astype(jnp.float32)
    normed = (
        widened
        * lax.rsqrt(jnp.mean(widened * widened, axis=1, keepdims=True) + EPSILON)
        * input_norm_gain
    ).astype(jnp.bfloat16)
    own_cols = lax.dynamic_slice_in_dim(
        normed, lax.axis_index("tensor") * part_width, part_width, 1
    )
    seg_counts = segment_sizes[0]
    adapters = segment_adapter[0]
    seg_ends = jnp.cumsum(seg_counts, dtype=jnp.int32)
    starts = seg_ends - seg_counts
    offsets = jnp.arange(SLOT, dtype=jnp.int32)
    row_ids = jnp.arange(row_count, dtype=jnp.int32)
    segment_index = jnp.sum((seg_ends[None, :] <= row_ids[:, None]).astype(jnp.int32), axis=1)
    token_position = row_ids - starts[segment_index]
    owners = adapters // ADP_DEV
    local_ids = adapters % ADP_DEV
    seg_ids = jnp.arange(segments, dtype=jnp.int32)
    slot_rank = jnp.sum(
        ((owners[None, :] == owners[:, None]) & (seg_ids[None, :] < seg_ids[:, None])).astype(
            jnp.int32
        ),
        axis=1,
    )
    owner_hit = (owners[None, None, :] == jnp.arange(replicas, dtype=jnp.int32)[:, None, None]) & (
        slot_rank[None, None, :] == jnp.arange(CAP, dtype=jnp.int32)[None, :, None]
    )
    wanted = jnp.sum(jnp.where(owner_hit, local_ids[None, None, :], 0), axis=2)
    fetch_slot = owners * CAP + slot_rank
    seg_at = jnp.sum(jnp.where(owner_hit, seg_ids[None, None, :], 0), axis=2)
    filled = jnp.any(owner_hit, axis=2)
    slot_counts = jnp.where(filled, seg_counts[seg_at], 0)
    slot_live = offsets[None, None, :] < slot_counts[:, :, None]
    source_row = jnp.where(slot_live, starts[seg_at][:, :, None] + offsets[None, None, :], 0)
    slot_rows = jnp.where(
        slot_live[:, :, :, None], own_cols[source_row], jnp.zeros((), jnp.bfloat16)
    )
    tags = jnp.broadcast_to(
        wanted.astype(jnp.bfloat16)[:, :, None, None], wanted.shape + (SLOT, HEAD)
    )
    payload = jnp.concatenate([slot_rows, tags], axis=3)
    got = lax.all_to_all(payload, "replica", split_axis=0, concat_axis=0, tiled=True)
    got_rows = got[..., :part_width]
    got_ids = got[:, :, 0, part_width].astype(jnp.int32)
    selected_down = adapter_down[got_ids]
    selected_up = adapter_up[got_ids]
    partial_value = jnp.einsum(
        "oksd,okdr->oksr", got_rows, selected_down, preferred_element_type=jnp.float32
    )
    summed = lax.psum(partial_value, "tensor").astype(jnp.bfloat16)
    summed = summed.reshape(summed.shape[:3] + (2, adapter_rank_size))
    owner_delta = (
        jnp.einsum("okscr,okcrw->okscw", summed, selected_up, preferred_element_type=jnp.float32)
        * ADAPTER_SCALE
    )
    slot_delta = lax.all_to_all(owner_delta, "replica", split_axis=0, concat_axis=0, tiled=True)
    flat_delta = slot_delta.reshape((replicas * CAP * SLOT,) + slot_delta.shape[3:])
    adapter_delta = flat_delta[fetch_slot[segment_index] * SLOT + token_position]
    base_projection = jnp.dot(
        normed,
        key_value_weight.reshape(key_value_weight.shape[0], 2 * kv_width),
        preferred_element_type=jnp.float32,
    ).reshape(row_count, 2, kv_width)
    current_key_value = base_projection + adapter_delta
    rotated = rotate(
        current_key_value[:, 0].reshape(row_count, kv_local, HEAD), cached_length
    ).reshape(row_count, kv_width)
    new_kv = jnp.stack([rotated, current_key_value[:, 1]], axis=1).astype(jnp.bfloat16)
    group_size = query.shape[1] // HEAD // kv_local
    attended = attend(query, key_value_cache, new_kv, cached_length, kv_local, group_size)
    return (new_kv, attended)


def solution(mesh):
    in_specs = (
        P("replica", "tensor"),
        P(),
        P(None, None, "tensor"),
        P("replica", "tensor", None),
        P("replica", None, None, "tensor"),
        P("replica", "tensor"),
        P("replica", None, None, "tensor"),
        P("replica", None),
        P("replica", None),
        P("replica"),
    )
    out_specs = (P("replica", None, "tensor"), P("replica", "tensor"))
    return jax.shard_map(body, mesh=mesh, in_specs=in_specs, out_specs=out_specs, check_vma=False)
```

```python
import functools

import jax
import jax.numpy as jnp
from jax import lax
from jax.experimental import pallas as pl
from jax.experimental.pallas import tpu as pltpu
from jax.sharding import PartitionSpec as P

HEAD = 128
ADP_DEV = 16
SLOT = 4
CAP = 2


ADAPTER_SCALE = 0.5
ROPE_BASE = 500000.0
EPSILON = 1e-05


def rotate(key_heads, token_position):
    half_size = key_heads.shape[-1] // 2
    inv_freq = ROPE_BASE ** (
        -(jnp.arange(half_size, dtype=jnp.float32) * 2.0) / key_heads.shape[-1]
    )
    angles = token_position.astype(jnp.float32)[:, None] * inv_freq[None, :]
    cosine_term = jnp.cos(angles)[:, None, :]
    sine_term = jnp.sin(angles)[:, None, :]
    first_half = key_heads[..., :half_size]
    second_half = key_heads[..., half_size:]
    return jnp.concatenate(
        [
            first_half * cosine_term - second_half * sine_term,
            second_half * cosine_term + first_half * sine_term,
        ],
        axis=-1,
    )


def attention_kernel(len_ref, q_ref, kv_ref, nkv_ref, o_ref, *, rows, kv_local, group_size):
    scale = float(HEAD) ** (-0.5)
    step = pl.program_id(0)
    cache_len = kv_ref.shape[1]
    width = kv_ref.shape[3]
    pos = lax.broadcasted_iota(jnp.int32, (group_size, 2 * cache_len), 1)
    for i in range(rows):
        length = len_ref[step * rows + i]
        stacked = kv_ref[i].reshape(2 * cache_len, width)
        live = (pos % 2 == 0) & (pos < 2 * length)
        for h in range(kv_local):
            cols = slice(h * HEAD, (h + 1) * HEAD)
            qrows = slice(h * group_size, (h + 1) * group_size)
            q = q_ref[i, qrows, :]
            block = stacked[:, cols]
            scores = lax.dot_general(
                q, block, (((1,), (1,)), ((), ())), preferred_element_type=jnp.float32
            ) * scale
            scores = jnp.where(live, scores, -jnp.inf)
            new_key = nkv_ref[i, 0:1, cols].astype(jnp.float32)
            new_value = nkv_ref[i, 1:2, cols].astype(jnp.float32)
            own = jnp.sum(q.astype(jnp.float32) * new_key, axis=1, keepdims=True) * scale
            top = jnp.maximum(jnp.max(scores, axis=1, keepdims=True), own)
            weights = jnp.exp(scores - top)
            own_weight = jnp.exp(own - top)
            total = jnp.sum(weights, axis=1, keepdims=True) + own_weight
            probs = pltpu.roll(weights / total, 1, 1).astype(jnp.bfloat16)
            own_prob = (own_weight / total).astype(jnp.bfloat16).astype(jnp.float32)
            context = jnp.dot(probs, block, preferred_element_type=jnp.float32)
            context = context + own_prob * new_value
            o_ref[i, qrows, :] = context.astype(o_ref.dtype)


def attend(query, key_value_cache, new_kv, cached_length, kv_local, group_size):
    row_count = query.shape[0]
    cache_len = key_value_cache.shape[1]
    width = key_value_cache.shape[3]
    heads = kv_local * group_size
    rows = 4
    query_heads = query.reshape(row_count, heads, HEAD)
    kernel = functools.partial(
        attention_kernel, rows=rows, kv_local=kv_local, group_size=group_size
    )
    out = pl.pallas_call(
        kernel,
        out_shape=jax.ShapeDtypeStruct((row_count, heads, HEAD), jnp.bfloat16),
        grid_spec=pltpu.PrefetchScalarGridSpec(
            num_scalar_prefetch=1,
            grid=(row_count // rows,),
            in_specs=[
                pl.BlockSpec((rows, heads, HEAD), lambda b, lens: (b, 0, 0)),
                pl.BlockSpec((rows, cache_len, 2, width), lambda b, lens: (b, 0, 0, 0)),
                pl.BlockSpec((rows, 2, width), lambda b, lens: (b, 0, 0)),
            ],
            out_specs=pl.BlockSpec((rows, heads, HEAD), lambda b, lens: (b, 0, 0)),
        ),
    )(cached_length, query_heads, key_value_cache, new_kv)
    return out.reshape(row_count, heads * HEAD)


def body(
    hidden,
    input_norm_gain,
    key_value_weight,
    adapter_down,
    adapter_up,
    query,
    key_value_cache,
    segment_adapter,
    segment_sizes,
    cached_length,
):
    row_count = hidden.shape[0]
    part_width = hidden.shape[1]
    kv_width = key_value_weight.shape[2]
    kv_local = kv_width // HEAD
    cache_len = key_value_cache.shape[1]
    adapter_rank_size = adapter_up.shape[2]
    replicas = lax.axis_size("replica")
    segments = segment_sizes.shape[1]
    gathered = lax.all_gather(hidden, "tensor", axis=1, tiled=True)
    widened = gathered.astype(jnp.float32)
    normed = (
        widened
        * lax.rsqrt(jnp.mean(widened * widened, axis=1, keepdims=True) + EPSILON)
        * input_norm_gain
    ).astype(jnp.bfloat16)
    own_cols = lax.dynamic_slice_in_dim(
        normed, lax.axis_index("tensor") * part_width, part_width, 1
    )
    seg_counts = segment_sizes[0]
    adapters = segment_adapter[0]
    seg_ends = jnp.cumsum(seg_counts, dtype=jnp.int32)
    starts = seg_ends - seg_counts
    offsets = jnp.arange(SLOT, dtype=jnp.int32)
    row_ids = jnp.arange(row_count, dtype=jnp.int32)
    segment_index = jnp.sum((seg_ends[None, :] <= row_ids[:, None]).astype(jnp.int32), axis=1)
    token_position = row_ids - starts[segment_index]
    owners = adapters // ADP_DEV
    local_ids = adapters % ADP_DEV
    seg_ids = jnp.arange(segments, dtype=jnp.int32)
    slot_rank = jnp.sum(
        ((owners[None, :] == owners[:, None]) & (seg_ids[None, :] < seg_ids[:, None])).astype(
            jnp.int32
        ),
        axis=1,
    )
    owner_hit = (owners[None, None, :] == jnp.arange(replicas, dtype=jnp.int32)[:, None, None]) & (
        slot_rank[None, None, :] == jnp.arange(CAP, dtype=jnp.int32)[None, :, None]
    )
    wanted = jnp.sum(jnp.where(owner_hit, local_ids[None, None, :], 0), axis=2)
    fetch_slot = owners * CAP + slot_rank
    seg_at = jnp.sum(jnp.where(owner_hit, seg_ids[None, None, :], 0), axis=2)
    filled = jnp.any(owner_hit, axis=2)
    slot_counts = jnp.where(filled, seg_counts[seg_at], 0)
    slot_live = offsets[None, None, :] < slot_counts[:, :, None]
    source_row = jnp.where(slot_live, starts[seg_at][:, :, None] + offsets[None, None, :], 0)
    slot_rows = jnp.where(
        slot_live[:, :, :, None], own_cols[source_row], jnp.zeros((), jnp.bfloat16)
    )
    tags = jnp.broadcast_to(
        wanted.astype(jnp.bfloat16)[:, :, None, None], wanted.shape + (SLOT, HEAD)
    )
    payload = jnp.concatenate([slot_rows, tags], axis=3)
    got = lax.all_to_all(payload, "replica", split_axis=0, concat_axis=0, tiled=True)
    got_rows = got[..., :part_width]
    got_ids = got[:, :, 0, part_width].astype(jnp.int32)
    selected_down = adapter_down[got_ids]
    selected_up = adapter_up[got_ids]
    partial_value = jnp.einsum(
        "oksd,okdr->oksr", got_rows, selected_down, preferred_element_type=jnp.float32
    )
    summed = lax.psum(partial_value, "tensor").astype(jnp.bfloat16)
    summed = summed.reshape(summed.shape[:3] + (2, adapter_rank_size))
    owner_delta = (
        jnp.einsum("okscr,okcrw->okscw", summed, selected_up, preferred_element_type=jnp.float32)
        * ADAPTER_SCALE
    )
    slot_delta = lax.all_to_all(owner_delta, "replica", split_axis=0, concat_axis=0, tiled=True)
    flat_delta = slot_delta.reshape((replicas * CAP * SLOT,) + slot_delta.shape[3:])
    adapter_delta = flat_delta[fetch_slot[segment_index] * SLOT + token_position]
    base_projection = jnp.dot(
        normed,
        key_value_weight.reshape(key_value_weight.shape[0], 2 * kv_width),
        preferred_element_type=jnp.float32,
    ).reshape(row_count, 2, kv_width)
    current_key_value = base_projection + adapter_delta
    rotated = rotate(
        current_key_value[:, 0].reshape(row_count, kv_local, HEAD), cached_length
    ).reshape(row_count, kv_width)
    new_kv = jnp.stack([rotated, current_key_value[:, 1]], axis=1).astype(jnp.bfloat16)
    group_size = query.shape[1] // HEAD // kv_local
    attended = attend(query, key_value_cache, new_kv, cached_length, kv_local, group_size)
    return (new_kv, attended)


def solution(mesh):
    in_specs = (
        P("replica", "tensor"),
        P(),
        P(None, None, "tensor"),
        P("replica", "tensor", None),
        P("replica", None, None, "tensor"),
        P("replica", "tensor"),
        P("replica", None, None, "tensor"),
        P("replica", None),
        P("replica", None),
        P("replica"),
    )
    out_specs = (P("replica", None, "tensor"), P("replica", "tensor"))
    return jax.shard_map(body, mesh=mesh, in_specs=in_specs, out_specs=out_specs, check_vma=False)
```

```python
import functools

import jax
import jax.numpy as jnp
from jax import lax
from jax.experimental import pallas as pl
from jax.experimental.pallas import tpu as pltpu
from jax.sharding import PartitionSpec as P

HEAD = 128
ADP_DEV = 16
SLOT = 4
CAP = 2


ADAPTER_SCALE = 0.5
ROPE_BASE = 500000.0
EPSILON = 1e-05


def rotate(key_heads, token_position):
    half_size = key_heads.shape[-1] // 2
    inv_freq = ROPE_BASE ** (
        -(jnp.arange(half_size, dtype=jnp.float32) * 2.0) / key_heads.shape[-1]
    )
    angles = token_position.astype(jnp.float32)[:, None] * inv_freq[None, :]
    cosine_term = jnp.cos(angles)[:, None, :]
    sine_term = jnp.sin(angles)[:, None, :]
    first_half = key_heads[..., :half_size]
    second_half = key_heads[..., half_size:]
    return jnp.concatenate(
        [
            first_half * cosine_term - second_half * sine_term,
            second_half * cosine_term + first_half * sine_term,
        ],
        axis=-1,
    )


def attention_kernel(len_ref, q_ref, kv_ref, nkv_ref, o_ref, *, rows, kv_local, group_size):
    scale = float(HEAD) ** (-0.5)
    step = pl.program_id(0)
    cache_len = kv_ref.shape[1]
    width = kv_ref.shape[3]
    pos = lax.broadcasted_iota(jnp.int32, (group_size, 2 * cache_len), 1)
    for i in range(rows):
        length = len_ref[step * rows + i]
        stacked = kv_ref[i].reshape(2 * cache_len, width)
        live = (pos % 2 == 0) & (pos < 2 * length)
        for h in range(kv_local):
            cols = slice(h * HEAD, (h + 1) * HEAD)
            qrows = slice(h * group_size, (h + 1) * group_size)
            q = q_ref[i, qrows, :]
            block = stacked[:, cols]
            scores = lax.dot_general(
                q, block, (((1,), (1,)), ((), ())), preferred_element_type=jnp.float32
            ) * scale
            scores = jnp.where(live, scores, -jnp.inf)
            new_key = nkv_ref[i, 0:1, cols].astype(jnp.float32)
            new_value = nkv_ref[i, 1:2, cols].astype(jnp.float32)
            own = jnp.sum(q.astype(jnp.float32) * new_key, axis=1, keepdims=True) * scale
            top = jnp.maximum(jnp.max(scores, axis=1, keepdims=True), own)
            weights = jnp.exp(scores - top)
            own_weight = jnp.exp(own - top)
            total = jnp.sum(weights, axis=1, keepdims=True) + own_weight
            probs = pltpu.roll(weights / total, 1, 1).astype(jnp.bfloat16)
            own_prob = (own_weight / total).astype(jnp.bfloat16).astype(jnp.float32)
            context = jnp.dot(probs, block, preferred_element_type=jnp.float32)
            context = context + own_prob * new_value
            o_ref[i, qrows, :] = context.astype(o_ref.dtype)


def attend(query, key_value_cache, new_kv, cached_length, kv_local, group_size):
    row_count = query.shape[0]
    cache_len = key_value_cache.shape[1]
    width = key_value_cache.shape[3]
    heads = kv_local * group_size
    rows = 4
    query_heads = query.reshape(row_count, heads, HEAD)
    kernel = functools.partial(
        attention_kernel, rows=rows, kv_local=kv_local, group_size=group_size
    )
    out = pl.pallas_call(
        kernel,
        out_shape=jax.ShapeDtypeStruct((row_count, heads, HEAD), jnp.bfloat16),
        grid_spec=pltpu.PrefetchScalarGridSpec(
            num_scalar_prefetch=1,
            grid=(row_count // rows,),
            in_specs=[
                pl.BlockSpec((rows, heads, HEAD), lambda b, lens: (b, 0, 0)),
                pl.BlockSpec((rows, cache_len, 2, width), lambda b, lens: (b, 0, 0, 0)),
                pl.BlockSpec((rows, 2, width), lambda b, lens: (b, 0, 0)),
            ],
            out_specs=pl.BlockSpec((rows, heads, HEAD), lambda b, lens: (b, 0, 0)),
        ),
    )(cached_length, query_heads, key_value_cache, new_kv)
    return out.reshape(row_count, heads * HEAD)


def body(
    hidden,
    input_norm_gain,
    key_value_weight,
    adapter_down,
    adapter_up,
    query,
    key_value_cache,
    segment_adapter,
    segment_sizes,
    cached_length,
):
    row_count = hidden.shape[0]
    part_width = hidden.shape[1]
    kv_width = key_value_weight.shape[2]
    kv_local = kv_width // HEAD
    cache_len = key_value_cache.shape[1]
    adapter_rank_size = adapter_up.shape[2]
    replicas = lax.axis_size("replica")
    segments = segment_sizes.shape[1]
    gathered = lax.all_gather(hidden, "tensor", axis=1, tiled=True)
    widened = gathered.astype(jnp.float32)
    normed = (
        widened
        * lax.rsqrt(jnp.mean(widened * widened, axis=1, keepdims=True) + EPSILON)
        * input_norm_gain
    ).astype(jnp.bfloat16)
    own_cols = lax.dynamic_slice_in_dim(
        normed, lax.axis_index("tensor") * part_width, part_width, 1
    )
    seg_counts = segment_sizes[0]
    adapters = segment_adapter[0]
    seg_ends = jnp.cumsum(seg_counts, dtype=jnp.int32)
    starts = seg_ends - seg_counts
    offsets = jnp.arange(SLOT, dtype=jnp.int32)
    row_ids = jnp.arange(row_count, dtype=jnp.int32)
    segment_index = jnp.sum((seg_ends[None, :] <= row_ids[:, None]).astype(jnp.int32), axis=1)
    token_position = row_ids - starts[segment_index]
    owners = adapters // ADP_DEV
    local_ids = adapters % ADP_DEV
    seg_ids = jnp.arange(segments, dtype=jnp.int32)
    slot_rank = jnp.sum(
        ((owners[None, :] == owners[:, None]) & (seg_ids[None, :] < seg_ids[:, None])).astype(
            jnp.int32
        ),
        axis=1,
    )
    owner_hit = (owners[None, None, :] == jnp.arange(replicas, dtype=jnp.int32)[:, None, None]) & (
        slot_rank[None, None, :] == jnp.arange(CAP, dtype=jnp.int32)[None, :, None]
    )
    wanted = jnp.sum(jnp.where(owner_hit, local_ids[None, None, :], 0), axis=2)
    fetch_slot = owners * CAP + slot_rank
    seg_at = jnp.sum(jnp.where(owner_hit, seg_ids[None, None, :], 0), axis=2)
    filled = jnp.any(owner_hit, axis=2)
    slot_counts = jnp.where(filled, seg_counts[seg_at], 0)
    slot_live = offsets[None, None, :] < slot_counts[:, :, None]
    source_row = jnp.where(slot_live, starts[seg_at][:, :, None] + offsets[None, None, :], 0)
    slot_rows = jnp.where(
        slot_live[:, :, :, None], own_cols[source_row], jnp.zeros((), jnp.bfloat16)
    )
    tags = jnp.broadcast_to(
        wanted.astype(jnp.bfloat16)[:, :, None, None], wanted.shape + (SLOT, HEAD)
    )
    payload = jnp.concatenate([slot_rows, tags], axis=3)
    got = lax.all_to_all(payload, "replica", split_axis=0, concat_axis=0, tiled=True)
    got_rows = got[..., :part_width]
    got_ids = got[:, :, 0, part_width].astype(jnp.int32)
    selected_down = adapter_down[got_ids]
    selected_up = adapter_up[got_ids]
    partial_value = jnp.einsum(
        "oksd,okdr->oksr", got_rows, selected_down, preferred_element_type=jnp.float32
    )
    summed = lax.psum(partial_value, "tensor").astype(jnp.bfloat16)
    summed = summed.reshape(summed.shape[:3] + (2, adapter_rank_size))
    owner_delta = (
        jnp.einsum("okscr,okcrw->okscw", summed, selected_up, preferred_element_type=jnp.float32)
        * ADAPTER_SCALE
    )
    slot_delta = lax.all_to_all(owner_delta, "replica", split_axis=0, concat_axis=0, tiled=True)
    flat_delta = slot_delta.reshape((replicas * CAP * SLOT,) + slot_delta.shape[3:])
    adapter_delta = flat_delta[fetch_slot[segment_index] * SLOT + token_position]
    base_projection = jnp.einsum(
        "jd,dcw->jcw", normed, key_value_weight, preferred_element_type=jnp.float32
    )
    current_key_value = base_projection + adapter_delta
    rotated = rotate(
        current_key_value[:, 0].reshape(row_count, kv_local, HEAD), cached_length
    ).reshape(row_count, kv_width)
    new_kv = jnp.stack([rotated, current_key_value[:, 1]], axis=1).astype(jnp.bfloat16)
    group_size = query.shape[1] // HEAD // kv_local
    attended = attend(query, key_value_cache, new_kv, cached_length, kv_local, group_size)
    return (new_kv, attended)


def solution(mesh):
    in_specs = (
        P("replica", "tensor"),
        P(),
        P(None, None, "tensor"),
        P("replica", "tensor", None),
        P("replica", None, None, "tensor"),
        P("replica", "tensor"),
        P("replica", None, None, "tensor"),
        P("replica", None),
        P("replica", None),
        P("replica"),
    )
    out_specs = (P("replica", None, "tensor"), P("replica", "tensor"))
    return jax.shard_map(body, mesh=mesh, in_specs=in_specs, out_specs=out_specs, check_vma=False)
```

```python
import functools

import jax
import jax.numpy as jnp
from jax import lax
from jax.experimental import pallas as pl
from jax.experimental.pallas import tpu as pltpu
from jax.sharding import PartitionSpec as P

HEAD = 128
ADP_DEV = 16
SLOT = 4
CAP = 2


ADAPTER_SCALE = 0.5
ROPE_BASE = 500000.0
EPSILON = 1e-05


def rotate(key_heads, token_position):
    half_size = key_heads.shape[-1] // 2
    inv_freq = ROPE_BASE ** (
        -(jnp.arange(half_size, dtype=jnp.float32) * 2.0) / key_heads.shape[-1]
    )
    angles = token_position.astype(jnp.float32)[:, None] * inv_freq[None, :]
    cosine_term = jnp.cos(angles)[:, None, :]
    sine_term = jnp.sin(angles)[:, None, :]
    first_half = key_heads[..., :half_size]
    second_half = key_heads[..., half_size:]
    return jnp.concatenate(
        [
            first_half * cosine_term - second_half * sine_term,
            second_half * cosine_term + first_half * sine_term,
        ],
        axis=-1,
    )


def cached_attention_kernel(len_ref, q_ref, kv_ref, acc_ref, stat_ref, *, rows, kv_local, group_size):
    scale = float(HEAD) ** (-0.5)
    step = pl.program_id(0)
    cache_len = kv_ref.shape[1]
    width = kv_ref.shape[3]
    pos = lax.broadcasted_iota(jnp.int32, (group_size, 2 * cache_len), 1)
    lane = lax.broadcasted_iota(jnp.int32, (group_size, HEAD), 1)
    for i in range(rows):
        length = len_ref[step * rows + i]
        stacked = kv_ref[i].reshape(2 * cache_len, width)
        live = (pos % 2 == 0) & (pos < 2 * length)
        for h in range(kv_local):
            cols = slice(h * HEAD, (h + 1) * HEAD)
            qrows = slice(h * group_size, (h + 1) * group_size)
            q = q_ref[i, qrows, :]
            block = stacked[:, cols]
            scores = lax.dot_general(
                q, block, (((1,), (1,)), ((), ())), preferred_element_type=jnp.float32
            ) * scale
            scores = jnp.where(live, scores, -jnp.inf)
            top = jnp.max(scores, axis=1, keepdims=True)
            weights = jnp.exp(scores - top)
            mass = jnp.sum(weights, axis=1, keepdims=True)
            shifted = pltpu.roll(weights, 1, 1).astype(jnp.bfloat16)
            acc_ref[i, qrows, :] = jnp.dot(shifted, block, preferred_element_type=jnp.float32)
            stat_ref[i, qrows, :] = jnp.where(lane == 0, top, jnp.where(lane == 1, mass, 0.0))


def cached_attention(query, key_value_cache, cached_length, kv_local, group_size):
    row_count = query.shape[0]
    cache_len = key_value_cache.shape[1]
    width = key_value_cache.shape[3]
    heads = kv_local * group_size
    rows = 4
    query_heads = query.reshape(row_count, heads, HEAD)
    kernel = functools.partial(
        cached_attention_kernel, rows=rows, kv_local=kv_local, group_size=group_size
    )
    spec = pl.BlockSpec((rows, heads, HEAD), lambda b, lens: (b, 0, 0))
    return pl.pallas_call(
        kernel,
        out_shape=(
            jax.ShapeDtypeStruct((row_count, heads, HEAD), jnp.float32),
            jax.ShapeDtypeStruct((row_count, heads, HEAD), jnp.float32),
        ),
        grid_spec=pltpu.PrefetchScalarGridSpec(
            num_scalar_prefetch=1,
            grid=(row_count // rows,),
            in_specs=[
                spec,
                pl.BlockSpec((rows, cache_len, 2, width), lambda b, lens: (b, 0, 0, 0)),
            ],
            out_specs=(spec, spec),
        ),
    )(cached_length, query_heads, key_value_cache)


def attend(query, key_value_cache, new_kv, cached_length, kv_local, group_size):
    row_count = query.shape[0]
    heads = kv_local * group_size
    scale = float(HEAD) ** (-0.5)
    acc, stats = cached_attention(query, key_value_cache, cached_length, kv_local, group_size)
    cached_top = stats[:, :, 0].reshape(row_count, kv_local, group_size)
    cached_mass = stats[:, :, 1].reshape(row_count, kv_local, group_size)
    acc = acc.reshape(row_count, kv_local, group_size, HEAD)
    query_heads = query.reshape(row_count, kv_local, group_size, HEAD)
    new_key = new_kv[:, 0].reshape(row_count, kv_local, HEAD)
    new_value = new_kv[:, 1].astype(jnp.float32).reshape(row_count, kv_local, HEAD)
    own_score = (
        jnp.einsum("bhgd,bhd->bhg", query_heads, new_key, preferred_element_type=jnp.float32)
        * scale
    )
    top = jnp.maximum(cached_top, own_score)
    cached_factor = jnp.exp(cached_top - top)
    own_weight = jnp.exp(own_score - top)
    total = cached_mass * cached_factor + own_weight
    own_prob = (own_weight / total).astype(jnp.bfloat16).astype(jnp.float32)
    context = acc * (cached_factor / total)[..., None]
    context = context + own_prob[..., None] * new_value[:, :, None, :]
    return context.reshape(row_count, heads * HEAD).astype(jnp.bfloat16)


def body(
    hidden,
    input_norm_gain,
    key_value_weight,
    adapter_down,
    adapter_up,
    query,
    key_value_cache,
    segment_adapter,
    segment_sizes,
    cached_length,
):
    row_count = hidden.shape[0]
    part_width = hidden.shape[1]
    kv_width = key_value_weight.shape[2]
    kv_local = kv_width // HEAD
    cache_len = key_value_cache.shape[1]
    adapter_rank_size = adapter_up.shape[2]
    replicas = lax.axis_size("replica")
    segments = segment_sizes.shape[1]
    gathered = lax.all_gather(hidden, "tensor", axis=1, tiled=True)
    widened = gathered.astype(jnp.float32)
    normed = (
        widened
        * lax.rsqrt(jnp.mean(widened * widened, axis=1, keepdims=True) + EPSILON)
        * input_norm_gain
    ).astype(jnp.bfloat16)
    own_cols = lax.dynamic_slice_in_dim(
        normed, lax.axis_index("tensor") * part_width, part_width, 1
    )
    seg_counts = segment_sizes[0]
    adapters = segment_adapter[0]
    seg_ends = jnp.cumsum(seg_counts, dtype=jnp.int32)
    starts = seg_ends - seg_counts
    offsets = jnp.arange(SLOT, dtype=jnp.int32)
    row_ids = jnp.arange(row_count, dtype=jnp.int32)
    segment_index = jnp.sum((seg_ends[None, :] <= row_ids[:, None]).astype(jnp.int32), axis=1)
    token_position = row_ids - starts[segment_index]
    owners = adapters // ADP_DEV
    local_ids = adapters % ADP_DEV
    seg_ids = jnp.arange(segments, dtype=jnp.int32)
    slot_rank = jnp.sum(
        ((owners[None, :] == owners[:, None]) & (seg_ids[None, :] < seg_ids[:, None])).astype(
            jnp.int32
        ),
        axis=1,
    )
    owner_hit = (owners[None, None, :] == jnp.arange(replicas, dtype=jnp.int32)[:, None, None]) & (
        slot_rank[None, None, :] == jnp.arange(CAP, dtype=jnp.int32)[None, :, None]
    )
    wanted = jnp.sum(jnp.where(owner_hit, local_ids[None, None, :], 0), axis=2)
    fetch_slot = owners * CAP + slot_rank
    seg_at = jnp.sum(jnp.where(owner_hit, seg_ids[None, None, :], 0), axis=2)
    filled = jnp.any(owner_hit, axis=2)
    slot_counts = jnp.where(filled, seg_counts[seg_at], 0)
    slot_live = offsets[None, None, :] < slot_counts[:, :, None]
    source_row = jnp.where(slot_live, starts[seg_at][:, :, None] + offsets[None, None, :], 0)
    slot_rows = jnp.where(
        slot_live[:, :, :, None], own_cols[source_row], jnp.zeros((), jnp.bfloat16)
    )
    tags = jnp.broadcast_to(
        wanted.astype(jnp.bfloat16)[:, :, None, None], wanted.shape + (SLOT, HEAD)
    )
    payload = jnp.concatenate([slot_rows, tags], axis=3)
    got = lax.all_to_all(payload, "replica", split_axis=0, concat_axis=0, tiled=True)
    got_rows = got[..., :part_width]
    got_ids = got[:, :, 0, part_width].astype(jnp.int32)
    selected_down = adapter_down[got_ids]
    selected_up = adapter_up[got_ids]
    partial_value = jnp.einsum(
        "oksd,okdr->oksr", got_rows, selected_down, preferred_element_type=jnp.float32
    )
    summed = lax.psum(partial_value, "tensor").astype(jnp.bfloat16)
    summed = summed.reshape(summed.shape[:3] + (2, adapter_rank_size))
    owner_delta = (
        jnp.einsum("okscr,okcrw->okscw", summed, selected_up, preferred_element_type=jnp.float32)
        * ADAPTER_SCALE
    )
    slot_delta = lax.all_to_all(owner_delta, "replica", split_axis=0, concat_axis=0, tiled=True)
    flat_delta = slot_delta.reshape((replicas * CAP * SLOT,) + slot_delta.shape[3:])
    adapter_delta = flat_delta[fetch_slot[segment_index] * SLOT + token_position]
    base_projection = jnp.einsum(
        "jd,dcw->jcw", normed, key_value_weight, preferred_element_type=jnp.float32
    )
    current_key_value = base_projection + adapter_delta
    rotated = rotate(
        current_key_value[:, 0].reshape(row_count, kv_local, HEAD), cached_length
    ).reshape(row_count, kv_width)
    new_kv = jnp.stack([rotated, current_key_value[:, 1]], axis=1).astype(jnp.bfloat16)
    group_size = query.shape[1] // HEAD // kv_local
    attended = attend(query, key_value_cache, new_kv, cached_length, kv_local, group_size)
    return (new_kv, attended)


def solution(mesh):
    in_specs = (
        P("replica", "tensor"),
        P(),
        P(None, None, "tensor"),
        P("replica", "tensor", None),
        P("replica", None, None, "tensor"),
        P("replica", "tensor"),
        P("replica", None, None, "tensor"),
        P("replica", None),
        P("replica", None),
        P("replica"),
    )
    out_specs = (P("replica", None, "tensor"), P("replica", "tensor"))
    return jax.shard_map(body, mesh=mesh, in_specs=in_specs, out_specs=out_specs, check_vma=False)
```

```python
import functools

import jax
import jax.numpy as jnp
from jax import lax
from jax.experimental import pallas as pl
from jax.experimental.pallas import tpu as pltpu
from jax.sharding import PartitionSpec as P

HEAD = 128
ADP_DEV = 16
SLOT = 4
CAP = 2


ADAPTER_SCALE = 0.5
ROPE_BASE = 500000.0
EPSILON = 1e-05


def rotate(key_heads, token_position):
    half_size = key_heads.shape[-1] // 2
    inv_freq = ROPE_BASE ** (
        -(jnp.arange(half_size, dtype=jnp.float32) * 2.0) / key_heads.shape[-1]
    )
    angles = token_position.astype(jnp.float32)[:, None] * inv_freq[None, :]
    cosine_term = jnp.cos(angles)[:, None, :]
    sine_term = jnp.sin(angles)[:, None, :]
    first_half = key_heads[..., :half_size]
    second_half = key_heads[..., half_size:]
    return jnp.concatenate(
        [
            first_half * cosine_term - second_half * sine_term,
            second_half * cosine_term + first_half * sine_term,
        ],
        axis=-1,
    )


def attention_kernel(len_ref, q_ref, kv_ref, nkv_ref, o_ref, score_ref, acc_ref, *, rows, kv_local,
                     group_size, chunk):
    scale = float(HEAD) ** (-0.5)
    step = pl.program_id(0)
    cache_len = kv_ref.shape[1]
    width = kv_ref.shape[3]
    chunks = cache_len // chunk
    pos = lax.broadcasted_iota(jnp.int32, (group_size, 2 * cache_len), 1)
    for i in range(rows):
        length = len_ref[step * rows + i]
        live = (pos % 2 == 0) & (pos < 2 * length)
        for h in range(kv_local):
            cols = slice(h * HEAD, (h + 1) * HEAD)
            qrows = slice(h * group_size, (h + 1) * group_size)
            q = q_ref[i, qrows, :]
            for c in range(chunks):
                span = slice(2 * c * chunk, 2 * (c + 1) * chunk)

                @pl.when(c * chunk < length)
                def _():
                    block = kv_ref[i, c * chunk:(c + 1) * chunk].reshape(2 * chunk, width)
                    score_ref[:, span] = lax.dot_general(
                        q, block[:, cols], (((1,), (1,)), ((), ())),
                        preferred_element_type=jnp.float32,
                    )

                @pl.when(c * chunk >= length)
                def _():
                    score_ref[:, span] = jnp.zeros((group_size, 2 * chunk), jnp.float32)

            scores = jnp.where(live, score_ref[...] * scale, -jnp.inf)
            new_key = nkv_ref[i, 0:1, cols].astype(jnp.float32)
            new_value = nkv_ref[i, 1:2, cols].astype(jnp.float32)
            own = jnp.sum(q.astype(jnp.float32) * new_key, axis=1, keepdims=True) * scale
            top = jnp.maximum(jnp.max(scores, axis=1, keepdims=True), own)
            weights = jnp.exp(scores - top)
            own_weight = jnp.exp(own - top)
            total = jnp.sum(weights, axis=1, keepdims=True) + own_weight
            probs = pltpu.roll(weights / total, 1, 1).astype(jnp.bfloat16)
            own_prob = (own_weight / total).astype(jnp.bfloat16).astype(jnp.float32)
            acc_ref[...] = own_prob * new_value
            for c in range(chunks):
                span = slice(2 * c * chunk, 2 * (c + 1) * chunk)

                @pl.when(c * chunk < length)
                def _():
                    block = kv_ref[i, c * chunk:(c + 1) * chunk].reshape(2 * chunk, width)
                    acc_ref[...] += jnp.dot(
                        probs[:, span], block[:, cols], preferred_element_type=jnp.float32
                    )

            o_ref[i, qrows, :] = acc_ref[...].astype(o_ref.dtype)


def attend(query, key_value_cache, new_kv, cached_length, kv_local, group_size):
    row_count = query.shape[0]
    cache_len = key_value_cache.shape[1]
    width = key_value_cache.shape[3]
    heads = kv_local * group_size
    rows = 4
    query_heads = query.reshape(row_count, heads, HEAD)
    kernel = functools.partial(
        attention_kernel, rows=rows, kv_local=kv_local, group_size=group_size,
        chunk=min(cache_len, 128),
    )
    out = pl.pallas_call(
        kernel,
        out_shape=jax.ShapeDtypeStruct((row_count, heads, HEAD), jnp.bfloat16),
        grid_spec=pltpu.PrefetchScalarGridSpec(
            num_scalar_prefetch=1,
            grid=(row_count // rows,),
            in_specs=[
                pl.BlockSpec((rows, heads, HEAD), lambda b, lens: (b, 0, 0)),
                pl.BlockSpec((rows, cache_len, 2, width), lambda b, lens: (b, 0, 0, 0)),
                pl.BlockSpec((rows, 2, width), lambda b, lens: (b, 0, 0)),
            ],
            out_specs=pl.BlockSpec((rows, heads, HEAD), lambda b, lens: (b, 0, 0)),
            scratch_shapes=[
                pltpu.VMEM((group_size, 2 * cache_len), jnp.float32),
                pltpu.VMEM((group_size, HEAD), jnp.float32),
            ],
        ),
    )(cached_length, query_heads, key_value_cache, new_kv)
    return out.reshape(row_count, heads * HEAD)


def body(
    hidden,
    input_norm_gain,
    key_value_weight,
    adapter_down,
    adapter_up,
    query,
    key_value_cache,
    segment_adapter,
    segment_sizes,
    cached_length,
):
    row_count = hidden.shape[0]
    part_width = hidden.shape[1]
    kv_width = key_value_weight.shape[2]
    kv_local = kv_width // HEAD
    cache_len = key_value_cache.shape[1]
    adapter_rank_size = adapter_up.shape[2]
    replicas = lax.axis_size("replica")
    segments = segment_sizes.shape[1]
    gathered = lax.all_gather(hidden, "tensor", axis=1, tiled=True)
    widened = gathered.astype(jnp.float32)
    normed = (
        widened
        * lax.rsqrt(jnp.mean(widened * widened, axis=1, keepdims=True) + EPSILON)
        * input_norm_gain
    ).astype(jnp.bfloat16)
    own_cols = lax.dynamic_slice_in_dim(
        normed, lax.axis_index("tensor") * part_width, part_width, 1
    )
    seg_counts = segment_sizes[0]
    adapters = segment_adapter[0]
    seg_ends = jnp.cumsum(seg_counts, dtype=jnp.int32)
    starts = seg_ends - seg_counts
    offsets = jnp.arange(SLOT, dtype=jnp.int32)
    row_ids = jnp.arange(row_count, dtype=jnp.int32)
    segment_index = jnp.sum((seg_ends[None, :] <= row_ids[:, None]).astype(jnp.int32), axis=1)
    token_position = row_ids - starts[segment_index]
    owners = adapters // ADP_DEV
    local_ids = adapters % ADP_DEV
    seg_ids = jnp.arange(segments, dtype=jnp.int32)
    slot_rank = jnp.sum(
        ((owners[None, :] == owners[:, None]) & (seg_ids[None, :] < seg_ids[:, None])).astype(
            jnp.int32
        ),
        axis=1,
    )
    owner_hit = (owners[None, None, :] == jnp.arange(replicas, dtype=jnp.int32)[:, None, None]) & (
        slot_rank[None, None, :] == jnp.arange(CAP, dtype=jnp.int32)[None, :, None]
    )
    wanted = jnp.sum(jnp.where(owner_hit, local_ids[None, None, :], 0), axis=2)
    fetch_slot = owners * CAP + slot_rank
    seg_at = jnp.sum(jnp.where(owner_hit, seg_ids[None, None, :], 0), axis=2)
    filled = jnp.any(owner_hit, axis=2)
    slot_counts = jnp.where(filled, seg_counts[seg_at], 0)
    slot_live = offsets[None, None, :] < slot_counts[:, :, None]
    source_row = jnp.where(slot_live, starts[seg_at][:, :, None] + offsets[None, None, :], 0)
    slot_rows = jnp.where(
        slot_live[:, :, :, None], own_cols[source_row], jnp.zeros((), jnp.bfloat16)
    )
    tags = jnp.broadcast_to(
        wanted.astype(jnp.bfloat16)[:, :, None, None], wanted.shape + (SLOT, HEAD)
    )
    payload = jnp.concatenate([slot_rows, tags], axis=3)
    got = lax.all_to_all(payload, "replica", split_axis=0, concat_axis=0, tiled=True)
    got_rows = got[..., :part_width]
    got_ids = got[:, :, 0, part_width].astype(jnp.int32)
    selected_down = adapter_down[got_ids]
    selected_up = adapter_up[got_ids]
    partial_value = jnp.einsum(
        "oksd,okdr->oksr", got_rows, selected_down, preferred_element_type=jnp.float32
    )
    summed = lax.psum(partial_value, "tensor").astype(jnp.bfloat16)
    summed = summed.reshape(summed.shape[:3] + (2, adapter_rank_size))
    owner_delta = (
        jnp.einsum("okscr,okcrw->okscw", summed, selected_up, preferred_element_type=jnp.float32)
        * ADAPTER_SCALE
    )
    slot_delta = lax.all_to_all(owner_delta, "replica", split_axis=0, concat_axis=0, tiled=True)
    flat_delta = slot_delta.reshape((replicas * CAP * SLOT,) + slot_delta.shape[3:])
    adapter_delta = flat_delta[fetch_slot[segment_index] * SLOT + token_position]
    base_projection = jnp.einsum(
        "jd,dcw->jcw", normed, key_value_weight, preferred_element_type=jnp.float32
    )
    current_key_value = base_projection + adapter_delta
    rotated = rotate(
        current_key_value[:, 0].reshape(row_count, kv_local, HEAD), cached_length
    ).reshape(row_count, kv_width)
    new_kv = jnp.stack([rotated, current_key_value[:, 1]], axis=1).astype(jnp.bfloat16)
    group_size = query.shape[1] // HEAD // kv_local
    attended = attend(query, key_value_cache, new_kv, cached_length, kv_local, group_size)
    return (new_kv, attended)


def solution(mesh):
    in_specs = (
        P("replica", "tensor"),
        P(),
        P(None, None, "tensor"),
        P("replica", "tensor", None),
        P("replica", None, None, "tensor"),
        P("replica", "tensor"),
        P("replica", None, None, "tensor"),
        P("replica", None),
        P("replica", None),
        P("replica"),
    )
    out_specs = (P("replica", None, "tensor"), P("replica", "tensor"))
    return jax.shard_map(body, mesh=mesh, in_specs=in_specs, out_specs=out_specs, check_vma=False)
```

```python
import functools

import jax
import jax.numpy as jnp
from jax import lax
from jax.experimental import pallas as pl
from jax.experimental.pallas import tpu as pltpu
from jax.sharding import PartitionSpec as P

HEAD = 128
ADP_DEV = 16
SLOT = 4
CAP = 2


ADAPTER_SCALE = 0.5
ROPE_BASE = 500000.0
EPSILON = 1e-05


def rotate(key_heads, token_position):
    half_size = key_heads.shape[-1] // 2
    inv_freq = ROPE_BASE ** (
        -(jnp.arange(half_size, dtype=jnp.float32) * 2.0) / key_heads.shape[-1]
    )
    angles = token_position.astype(jnp.float32)[:, None] * inv_freq[None, :]
    cosine_term = jnp.cos(angles)[:, None, :]
    sine_term = jnp.sin(angles)[:, None, :]
    first_half = key_heads[..., :half_size]
    second_half = key_heads[..., half_size:]
    return jnp.concatenate(
        [
            first_half * cosine_term - second_half * sine_term,
            second_half * cosine_term + first_half * sine_term,
        ],
        axis=-1,
    )


def attention_kernel(len_ref, q_ref, kv_ref, nkv_ref, o_ref, *, rows, kv_local, group_size):
    scale = float(HEAD) ** (-0.5)
    step = pl.program_id(0)
    cache_len = kv_ref.shape[1]
    width = kv_ref.shape[3]
    pos = lax.broadcasted_iota(jnp.int32, (group_size, 2 * cache_len), 1)
    for i in range(rows):
        length = len_ref[step * rows + i]
        stacked = kv_ref[i].reshape(2 * cache_len, width)
        live = (pos % 2 == 0) & (pos < 2 * length)
        for h in range(kv_local):
            cols = slice(h * HEAD, (h + 1) * HEAD)
            qrows = slice(h * group_size, (h + 1) * group_size)
            q = q_ref[i, qrows, :]
            block = stacked[:, cols]
            scores = lax.dot_general(
                q, block, (((1,), (1,)), ((), ())), preferred_element_type=jnp.float32
            ) * scale
            scores = jnp.where(live, scores, -jnp.inf)
            new_key = nkv_ref[i, 0:1, cols].astype(jnp.float32)
            new_value = nkv_ref[i, 1:2, cols].astype(jnp.float32)
            own = jnp.sum(q.astype(jnp.float32) * new_key, axis=1, keepdims=True) * scale
            top = jnp.maximum(jnp.max(scores, axis=1, keepdims=True), own)
            weights = jnp.exp(scores - top)
            own_weight = jnp.exp(own - top)
            total = jnp.sum(weights, axis=1, keepdims=True) + own_weight
            probs = pltpu.roll(weights / total, 1, 1).astype(jnp.bfloat16)
            own_prob = (own_weight / total).astype(jnp.bfloat16).astype(jnp.float32)
            context = jnp.dot(probs, block, preferred_element_type=jnp.float32)
            context = context + own_prob * new_value
            o_ref[i, qrows, :] = context.astype(o_ref.dtype)


def attend(query, key_value_cache, new_kv, cached_length, kv_local, group_size):
    row_count = query.shape[0]
    cache_len = key_value_cache.shape[1]
    width = key_value_cache.shape[3]
    heads = kv_local * group_size
    rows = 4
    query_heads = query.reshape(row_count, heads, HEAD)
    kernel = functools.partial(
        attention_kernel, rows=rows, kv_local=kv_local, group_size=group_size
    )
    out = pl.pallas_call(
        kernel,
        out_shape=jax.ShapeDtypeStruct((row_count, heads, HEAD), jnp.bfloat16),
        grid_spec=pltpu.PrefetchScalarGridSpec(
            num_scalar_prefetch=1,
            grid=(row_count // rows,),
            in_specs=[
                pl.BlockSpec((rows, heads, HEAD), lambda b, lens: (b, 0, 0)),
                pl.BlockSpec((rows, cache_len, 2, width), lambda b, lens: (b, 0, 0, 0)),
                pl.BlockSpec((rows, 2, width), lambda b, lens: (b, 0, 0)),
            ],
            out_specs=pl.BlockSpec((rows, heads, HEAD), lambda b, lens: (b, 0, 0)),
        ),
    )(cached_length, query_heads, key_value_cache, new_kv)
    return out.reshape(row_count, heads * HEAD)


def butterfly_sum(value, axis):
    size = lax.axis_size(axis)
    if size & (size - 1):
        return lax.psum(value, axis)
    stride = 1
    while stride < size:
        pairs = [(i, i ^ stride) for i in range(size)]
        value = value + lax.ppermute(value, axis, pairs)
        stride *= 2
    return value


def body(
    hidden,
    input_norm_gain,
    key_value_weight,
    adapter_down,
    adapter_up,
    query,
    key_value_cache,
    segment_adapter,
    segment_sizes,
    cached_length,
):
    row_count = hidden.shape[0]
    part_width = hidden.shape[1]
    kv_width = key_value_weight.shape[2]
    kv_local = kv_width // HEAD
    cache_len = key_value_cache.shape[1]
    adapter_rank_size = adapter_up.shape[2]
    replicas = lax.axis_size("replica")
    segments = segment_sizes.shape[1]
    gathered = lax.all_gather(hidden, "tensor", axis=1, tiled=True)
    widened = gathered.astype(jnp.float32)
    normed = (
        widened
        * lax.rsqrt(jnp.mean(widened * widened, axis=1, keepdims=True) + EPSILON)
        * input_norm_gain
    ).astype(jnp.bfloat16)
    own_cols = lax.dynamic_slice_in_dim(
        normed, lax.axis_index("tensor") * part_width, part_width, 1
    )
    seg_counts = segment_sizes[0]
    adapters = segment_adapter[0]
    seg_ends = jnp.cumsum(seg_counts, dtype=jnp.int32)
    starts = seg_ends - seg_counts
    offsets = jnp.arange(SLOT, dtype=jnp.int32)
    row_ids = jnp.arange(row_count, dtype=jnp.int32)
    segment_index = jnp.sum((seg_ends[None, :] <= row_ids[:, None]).astype(jnp.int32), axis=1)
    token_position = row_ids - starts[segment_index]
    owners = adapters // ADP_DEV
    local_ids = adapters % ADP_DEV
    seg_ids = jnp.arange(segments, dtype=jnp.int32)
    slot_rank = jnp.sum(
        ((owners[None, :] == owners[:, None]) & (seg_ids[None, :] < seg_ids[:, None])).astype(
            jnp.int32
        ),
        axis=1,
    )
    owner_hit = (owners[None, None, :] == jnp.arange(replicas, dtype=jnp.int32)[:, None, None]) & (
        slot_rank[None, None, :] == jnp.arange(CAP, dtype=jnp.int32)[None, :, None]
    )
    wanted = jnp.sum(jnp.where(owner_hit, local_ids[None, None, :], 0), axis=2)
    fetch_slot = owners * CAP + slot_rank
    seg_at = jnp.sum(jnp.where(owner_hit, seg_ids[None, None, :], 0), axis=2)
    filled = jnp.any(owner_hit, axis=2)
    slot_counts = jnp.where(filled, seg_counts[seg_at], 0)
    slot_live = offsets[None, None, :] < slot_counts[:, :, None]
    source_row = jnp.where(slot_live, starts[seg_at][:, :, None] + offsets[None, None, :], 0)
    slot_rows = jnp.where(
        slot_live[:, :, :, None], own_cols[source_row], jnp.zeros((), jnp.bfloat16)
    )
    tags = jnp.broadcast_to(
        wanted.astype(jnp.bfloat16)[:, :, None, None], wanted.shape + (SLOT, HEAD)
    )
    payload = jnp.concatenate([slot_rows, tags], axis=3)
    got = lax.all_to_all(payload, "replica", split_axis=0, concat_axis=0, tiled=True)
    got_rows = got[..., :part_width]
    got_ids = got[:, :, 0, part_width].astype(jnp.int32)
    selected_down = adapter_down[got_ids]
    selected_up = adapter_up[got_ids]
    partial_value = jnp.einsum(
        "oksd,okdr->oksr", got_rows, selected_down, preferred_element_type=jnp.float32
    )
    summed = butterfly_sum(partial_value, "tensor").astype(jnp.bfloat16)
    summed = summed.reshape(summed.shape[:3] + (2, adapter_rank_size))
    owner_delta = (
        jnp.einsum("okscr,okcrw->okscw", summed, selected_up, preferred_element_type=jnp.float32)
        * ADAPTER_SCALE
    )
    slot_delta = lax.all_to_all(owner_delta, "replica", split_axis=0, concat_axis=0, tiled=True)
    flat_delta = slot_delta.reshape((replicas * CAP * SLOT,) + slot_delta.shape[3:])
    adapter_delta = flat_delta[fetch_slot[segment_index] * SLOT + token_position]
    base_projection = jnp.einsum(
        "jd,dcw->jcw", normed, key_value_weight, preferred_element_type=jnp.float32
    )
    current_key_value = base_projection + adapter_delta
    rotated = rotate(
        current_key_value[:, 0].reshape(row_count, kv_local, HEAD), cached_length
    ).reshape(row_count, kv_width)
    new_kv = jnp.stack([rotated, current_key_value[:, 1]], axis=1).astype(jnp.bfloat16)
    group_size = query.shape[1] // HEAD // kv_local
    attended = attend(query, key_value_cache, new_kv, cached_length, kv_local, group_size)
    return (new_kv, attended)


def solution(mesh):
    in_specs = (
        P("replica", "tensor"),
        P(),
        P(None, None, "tensor"),
        P("replica", "tensor", None),
        P("replica", None, None, "tensor"),
        P("replica", "tensor"),
        P("replica", None, None, "tensor"),
        P("replica", None),
        P("replica", None),
        P("replica"),
    )
    out_specs = (P("replica", None, "tensor"), P("replica", "tensor"))
    return jax.shard_map(body, mesh=mesh, in_specs=in_specs, out_specs=out_specs, check_vma=False)
```

```python
import functools

import jax
import jax.numpy as jnp
from jax import lax
from jax.experimental import pallas as pl
from jax.experimental.pallas import tpu as pltpu
from jax.sharding import PartitionSpec as P

HEAD = 128
ADP_DEV = 16
SLOT = 4
CAP = 2


ADAPTER_SCALE = 0.5
ROPE_BASE = 500000.0
EPSILON = 1e-05


def rotate(key_heads, token_position):
    half_size = key_heads.shape[-1] // 2
    inv_freq = ROPE_BASE ** (
        -(jnp.arange(half_size, dtype=jnp.float32) * 2.0) / key_heads.shape[-1]
    )
    angles = token_position.astype(jnp.float32)[:, None] * inv_freq[None, :]
    cosine_term = jnp.cos(angles)[:, None, :]
    sine_term = jnp.sin(angles)[:, None, :]
    first_half = key_heads[..., :half_size]
    second_half = key_heads[..., half_size:]
    return jnp.concatenate(
        [
            first_half * cosine_term - second_half * sine_term,
            second_half * cosine_term + first_half * sine_term,
        ],
        axis=-1,
    )


def attention_kernel(len_ref, q_ref, kv_ref, nkv_ref, o_ref, *, rows, kv_local, group_size):
    scale = float(HEAD) ** (-0.5)
    step = pl.program_id(0)
    cache_len = kv_ref.shape[1]
    width = kv_ref.shape[3]
    pos = lax.broadcasted_iota(jnp.int32, (group_size, 2 * cache_len), 1)
    for i in range(rows):
        length = len_ref[step * rows + i]
        stacked = kv_ref[i].reshape(2 * cache_len, width)
        live = (pos % 2 == 0) & (pos < 2 * length)
        for h in range(kv_local):
            cols = slice(h * HEAD, (h + 1) * HEAD)
            qrows = slice(h * group_size, (h + 1) * group_size)
            q = q_ref[i, qrows, :]
            block = stacked[:, cols]
            scores = lax.dot_general(
                q, block, (((1,), (1,)), ((), ())), preferred_element_type=jnp.float32
            ) * scale
            scores = jnp.where(live, scores, -jnp.inf)
            new_key = nkv_ref[i, 0:1, cols].astype(jnp.float32)
            new_value = nkv_ref[i, 1:2, cols].astype(jnp.float32)
            own = jnp.sum(q.astype(jnp.float32) * new_key, axis=1, keepdims=True) * scale
            top = jnp.maximum(jnp.max(scores, axis=1, keepdims=True), own)
            weights = jnp.exp(scores - top)
            own_weight = jnp.exp(own - top)
            total = jnp.sum(weights, axis=1, keepdims=True) + own_weight
            probs = pltpu.roll(weights / total, 1, 1).astype(jnp.bfloat16)
            own_prob = (own_weight / total).astype(jnp.bfloat16).astype(jnp.float32)
            context = jnp.dot(probs, block, preferred_element_type=jnp.float32)
            context = context + own_prob * new_value
            o_ref[i, qrows, :] = context.astype(o_ref.dtype)


def attend(query, key_value_cache, new_kv, cached_length, kv_local, group_size):
    row_count = query.shape[0]
    cache_len = key_value_cache.shape[1]
    width = key_value_cache.shape[3]
    heads = kv_local * group_size
    rows = 4
    query_heads = query.reshape(row_count, heads, HEAD)
    kernel = functools.partial(
        attention_kernel, rows=rows, kv_local=kv_local, group_size=group_size
    )
    out = pl.pallas_call(
        kernel,
        out_shape=jax.ShapeDtypeStruct((row_count, heads, HEAD), jnp.bfloat16),
        grid_spec=pltpu.PrefetchScalarGridSpec(
            num_scalar_prefetch=1,
            grid=(row_count // rows,),
            in_specs=[
                pl.BlockSpec((rows, heads, HEAD), lambda b, lens: (b, 0, 0)),
                pl.BlockSpec((rows, cache_len, 2, width), lambda b, lens: (b, 0, 0, 0)),
                pl.BlockSpec((rows, 2, width), lambda b, lens: (b, 0, 0)),
            ],
            out_specs=pl.BlockSpec((rows, heads, HEAD), lambda b, lens: (b, 0, 0)),
        ),
    )(cached_length, query_heads, key_value_cache, new_kv)
    return out.reshape(row_count, heads * HEAD)


def butterfly_sum(value, axis):
    size = lax.axis_size(axis)
    if size & (size - 1):
        return lax.psum(value, axis)
    stride = 1
    while stride < size:
        pairs = [(i, i ^ stride) for i in range(size)]
        value = value + lax.ppermute(value, axis, pairs)
        stride *= 2
    return value


def butterfly_gather(value, axis):
    size = lax.axis_size(axis)
    if size & (size - 1):
        return lax.all_gather(value, axis, axis=1, tiled=True)
    index = lax.axis_index(axis)
    stride = 1
    while stride < size:
        pairs = [(i, i ^ stride) for i in range(size)]
        other = lax.ppermute(value, axis, pairs)
        value = jnp.where(
            (index & stride) == 0,
            jnp.concatenate([value, other], axis=1),
            jnp.concatenate([other, value], axis=1),
        )
        stride *= 2
    return value


def body(
    hidden,
    input_norm_gain,
    key_value_weight,
    adapter_down,
    adapter_up,
    query,
    key_value_cache,
    segment_adapter,
    segment_sizes,
    cached_length,
):
    row_count = hidden.shape[0]
    part_width = hidden.shape[1]
    kv_width = key_value_weight.shape[2]
    kv_local = kv_width // HEAD
    cache_len = key_value_cache.shape[1]
    adapter_rank_size = adapter_up.shape[2]
    replicas = lax.axis_size("replica")
    segments = segment_sizes.shape[1]
    gathered = butterfly_gather(hidden, "tensor")
    widened = gathered.astype(jnp.float32)
    normed = (
        widened
        * lax.rsqrt(jnp.mean(widened * widened, axis=1, keepdims=True) + EPSILON)
        * input_norm_gain
    ).astype(jnp.bfloat16)
    own_cols = lax.dynamic_slice_in_dim(
        normed, lax.axis_index("tensor") * part_width, part_width, 1
    )
    seg_counts = segment_sizes[0]
    adapters = segment_adapter[0]
    seg_ends = jnp.cumsum(seg_counts, dtype=jnp.int32)
    starts = seg_ends - seg_counts
    offsets = jnp.arange(SLOT, dtype=jnp.int32)
    row_ids = jnp.arange(row_count, dtype=jnp.int32)
    segment_index = jnp.sum((seg_ends[None, :] <= row_ids[:, None]).astype(jnp.int32), axis=1)
    token_position = row_ids - starts[segment_index]
    owners = adapters // ADP_DEV
    local_ids = adapters % ADP_DEV
    seg_ids = jnp.arange(segments, dtype=jnp.int32)
    slot_rank = jnp.sum(
        ((owners[None, :] == owners[:, None]) & (seg_ids[None, :] < seg_ids[:, None])).astype(
            jnp.int32
        ),
        axis=1,
    )
    owner_hit = (owners[None, None, :] == jnp.arange(replicas, dtype=jnp.int32)[:, None, None]) & (
        slot_rank[None, None, :] == jnp.arange(CAP, dtype=jnp.int32)[None, :, None]
    )
    wanted = jnp.sum(jnp.where(owner_hit, local_ids[None, None, :], 0), axis=2)
    fetch_slot = owners * CAP + slot_rank
    seg_at = jnp.sum(jnp.where(owner_hit, seg_ids[None, None, :], 0), axis=2)
    filled = jnp.any(owner_hit, axis=2)
    slot_counts = jnp.where(filled, seg_counts[seg_at], 0)
    slot_live = offsets[None, None, :] < slot_counts[:, :, None]
    source_row = jnp.where(slot_live, starts[seg_at][:, :, None] + offsets[None, None, :], 0)
    slot_rows = jnp.where(
        slot_live[:, :, :, None], own_cols[source_row], jnp.zeros((), jnp.bfloat16)
    )
    tags = jnp.broadcast_to(
        wanted.astype(jnp.bfloat16)[:, :, None, None], wanted.shape + (SLOT, HEAD)
    )
    payload = jnp.concatenate([slot_rows, tags], axis=3)
    got = lax.all_to_all(payload, "replica", split_axis=0, concat_axis=0, tiled=True)
    got_rows = got[..., :part_width]
    got_ids = got[:, :, 0, part_width].astype(jnp.int32)
    selected_down = adapter_down[got_ids]
    selected_up = adapter_up[got_ids]
    partial_value = jnp.einsum(
        "oksd,okdr->oksr", got_rows, selected_down, preferred_element_type=jnp.float32
    )
    summed = butterfly_sum(partial_value, "tensor").astype(jnp.bfloat16)
    summed = summed.reshape(summed.shape[:3] + (2, adapter_rank_size))
    owner_delta = (
        jnp.einsum("okscr,okcrw->okscw", summed, selected_up, preferred_element_type=jnp.float32)
        * ADAPTER_SCALE
    )
    slot_delta = lax.all_to_all(owner_delta, "replica", split_axis=0, concat_axis=0, tiled=True)
    flat_delta = slot_delta.reshape((replicas * CAP * SLOT,) + slot_delta.shape[3:])
    adapter_delta = flat_delta[fetch_slot[segment_index] * SLOT + token_position]
    base_projection = jnp.einsum(
        "jd,dcw->jcw", normed, key_value_weight, preferred_element_type=jnp.float32
    )
    current_key_value = base_projection + adapter_delta
    rotated = rotate(
        current_key_value[:, 0].reshape(row_count, kv_local, HEAD), cached_length
    ).reshape(row_count, kv_width)
    new_kv = jnp.stack([rotated, current_key_value[:, 1]], axis=1).astype(jnp.bfloat16)
    group_size = query.shape[1] // HEAD // kv_local
    attended = attend(query, key_value_cache, new_kv, cached_length, kv_local, group_size)
    return (new_kv, attended)


def solution(mesh):
    in_specs = (
        P("replica", "tensor"),
        P(),
        P(None, None, "tensor"),
        P("replica", "tensor", None),
        P("replica", None, None, "tensor"),
        P("replica", "tensor"),
        P("replica", None, None, "tensor"),
        P("replica", None),
        P("replica", None),
        P("replica"),
    )
    out_specs = (P("replica", None, "tensor"), P("replica", "tensor"))
    return jax.shard_map(body, mesh=mesh, in_specs=in_specs, out_specs=out_specs, check_vma=False)
```

```python
import functools

import jax
import jax.numpy as jnp
from jax import lax
from jax.experimental import pallas as pl
from jax.experimental.pallas import tpu as pltpu
from jax.sharding import PartitionSpec as P

HEAD = 128
ADP_DEV = 16
SLOT = 4
CAP = 2


ADAPTER_SCALE = 0.5
ROPE_BASE = 500000.0
EPSILON = 1e-05


def rotate(key_heads, token_position):
    half_size = key_heads.shape[-1] // 2
    inv_freq = ROPE_BASE ** (
        -(jnp.arange(half_size, dtype=jnp.float32) * 2.0) / key_heads.shape[-1]
    )
    angles = token_position.astype(jnp.float32)[:, None] * inv_freq[None, :]
    cosine_term = jnp.cos(angles)[:, None, :]
    sine_term = jnp.sin(angles)[:, None, :]
    first_half = key_heads[..., :half_size]
    second_half = key_heads[..., half_size:]
    return jnp.concatenate(
        [
            first_half * cosine_term - second_half * sine_term,
            second_half * cosine_term + first_half * sine_term,
        ],
        axis=-1,
    )


def attention_kernel(len_ref, q_ref, kv_ref, nkv_ref, o_ref, *, rows, kv_local, group_size):
    scale = float(HEAD) ** (-0.5)
    step = pl.program_id(0)
    cache_len = kv_ref.shape[1]
    width = kv_ref.shape[3]
    pos = lax.broadcasted_iota(jnp.int32, (group_size, 2 * cache_len), 1)
    for i in range(rows):
        length = len_ref[step * rows + i]
        stacked = kv_ref[i].reshape(2 * cache_len, width)
        live = (pos % 2 == 0) & (pos < 2 * length)
        for h in range(kv_local):
            cols = slice(h * HEAD, (h + 1) * HEAD)
            qrows = slice(h * group_size, (h + 1) * group_size)
            q = q_ref[i, qrows, :]
            block = stacked[:, cols]
            scores = lax.dot_general(
                q, block, (((1,), (1,)), ((), ())), preferred_element_type=jnp.float32
            ) * scale
            scores = jnp.where(live, scores, -jnp.inf)
            new_key = nkv_ref[i, 0:1, cols].astype(jnp.float32)
            new_value = nkv_ref[i, 1:2, cols].astype(jnp.float32)
            own = jnp.sum(q.astype(jnp.float32) * new_key, axis=1, keepdims=True) * scale
            top = jnp.maximum(jnp.max(scores, axis=1, keepdims=True), own)
            weights = jnp.exp(scores - top)
            own_weight = jnp.exp(own - top)
            total = jnp.sum(weights, axis=1, keepdims=True) + own_weight
            probs = pltpu.roll(weights / total, 1, 1).astype(jnp.bfloat16)
            own_prob = (own_weight / total).astype(jnp.bfloat16).astype(jnp.float32)
            context = jnp.dot(probs, block, preferred_element_type=jnp.float32)
            context = context + own_prob * new_value
            o_ref[i, qrows, :] = context.astype(o_ref.dtype)


def attend(query, key_value_cache, new_kv, cached_length, kv_local, group_size):
    row_count = query.shape[0]
    cache_len = key_value_cache.shape[1]
    width = key_value_cache.shape[3]
    heads = kv_local * group_size
    rows = 4
    query_heads = query.reshape(row_count, heads, HEAD)
    kernel = functools.partial(
        attention_kernel, rows=rows, kv_local=kv_local, group_size=group_size
    )
    out = pl.pallas_call(
        kernel,
        out_shape=jax.ShapeDtypeStruct((row_count, heads, HEAD), jnp.bfloat16),
        grid_spec=pltpu.PrefetchScalarGridSpec(
            num_scalar_prefetch=1,
            grid=(row_count // rows,),
            in_specs=[
                pl.BlockSpec((rows, heads, HEAD), lambda b, lens: (b, 0, 0)),
                pl.BlockSpec((rows, cache_len, 2, width), lambda b, lens: (b, 0, 0, 0)),
                pl.BlockSpec((rows, 2, width), lambda b, lens: (b, 0, 0)),
            ],
            out_specs=pl.BlockSpec((rows, heads, HEAD), lambda b, lens: (b, 0, 0)),
        ),
    )(cached_length, query_heads, key_value_cache, new_kv)
    return out.reshape(row_count, heads * HEAD)


def butterfly_sum(value, axis):
    size = lax.axis_size(axis)
    if size & (size - 1):
        return lax.psum(value, axis)
    stride = 1
    while stride < size:
        pairs = [(i, i ^ stride) for i in range(size)]
        value = value + lax.ppermute(value, axis, pairs)
        stride *= 2
    return value


def down_kernel(ids_ref, rows_ref, down_ref, out_ref):
    out_ref[0] = jnp.dot(rows_ref[0], down_ref[0], preferred_element_type=jnp.float32)


def down_project(rows, ids, adapter_down):
    lead = ids.shape
    slots = ids.size
    slot_len, width = rows.shape[-2:]
    rank2 = adapter_down.shape[2]
    out = pl.pallas_call(
        down_kernel,
        out_shape=jax.ShapeDtypeStruct((slots, slot_len, rank2), jnp.float32),
        grid_spec=pltpu.PrefetchScalarGridSpec(
            num_scalar_prefetch=1,
            grid=(slots,),
            in_specs=[
                pl.BlockSpec((1, slot_len, width), lambda s, ids: (s, 0, 0)),
                pl.BlockSpec((1, width, rank2), lambda s, ids: (ids[s], 0, 0)),
            ],
            out_specs=pl.BlockSpec((1, slot_len, rank2), lambda s, ids: (s, 0, 0)),
        ),
    )(ids.reshape(slots), rows.reshape(slots, slot_len, width), adapter_down)
    return out.reshape(lead + (slot_len, rank2))


def body(
    hidden,
    input_norm_gain,
    key_value_weight,
    adapter_down,
    adapter_up,
    query,
    key_value_cache,
    segment_adapter,
    segment_sizes,
    cached_length,
):
    row_count = hidden.shape[0]
    part_width = hidden.shape[1]
    kv_width = key_value_weight.shape[2]
    kv_local = kv_width // HEAD
    cache_len = key_value_cache.shape[1]
    adapter_rank_size = adapter_up.shape[2]
    replicas = lax.axis_size("replica")
    segments = segment_sizes.shape[1]
    gathered = lax.all_gather(hidden, "tensor", axis=1, tiled=True)
    widened = gathered.astype(jnp.float32)
    normed = (
        widened
        * lax.rsqrt(jnp.mean(widened * widened, axis=1, keepdims=True) + EPSILON)
        * input_norm_gain
    ).astype(jnp.bfloat16)
    own_cols = lax.dynamic_slice_in_dim(
        normed, lax.axis_index("tensor") * part_width, part_width, 1
    )
    seg_counts = segment_sizes[0]
    adapters = segment_adapter[0]
    seg_ends = jnp.cumsum(seg_counts, dtype=jnp.int32)
    starts = seg_ends - seg_counts
    offsets = jnp.arange(SLOT, dtype=jnp.int32)
    row_ids = jnp.arange(row_count, dtype=jnp.int32)
    segment_index = jnp.sum((seg_ends[None, :] <= row_ids[:, None]).astype(jnp.int32), axis=1)
    token_position = row_ids - starts[segment_index]
    owners = adapters // ADP_DEV
    local_ids = adapters % ADP_DEV
    seg_ids = jnp.arange(segments, dtype=jnp.int32)
    slot_rank = jnp.sum(
        ((owners[None, :] == owners[:, None]) & (seg_ids[None, :] < seg_ids[:, None])).astype(
            jnp.int32
        ),
        axis=1,
    )
    owner_hit = (owners[None, None, :] == jnp.arange(replicas, dtype=jnp.int32)[:, None, None]) & (
        slot_rank[None, None, :] == jnp.arange(CAP, dtype=jnp.int32)[None, :, None]
    )
    wanted = jnp.sum(jnp.where(owner_hit, local_ids[None, None, :], 0), axis=2)
    fetch_slot = owners * CAP + slot_rank
    seg_at = jnp.sum(jnp.where(owner_hit, seg_ids[None, None, :], 0), axis=2)
    filled = jnp.any(owner_hit, axis=2)
    slot_counts = jnp.where(filled, seg_counts[seg_at], 0)
    slot_live = offsets[None, None, :] < slot_counts[:, :, None]
    source_row = jnp.where(slot_live, starts[seg_at][:, :, None] + offsets[None, None, :], 0)
    slot_rows = jnp.where(
        slot_live[:, :, :, None], own_cols[source_row], jnp.zeros((), jnp.bfloat16)
    )
    tags = jnp.broadcast_to(
        wanted.astype(jnp.bfloat16)[:, :, None, None], wanted.shape + (SLOT, HEAD)
    )
    payload = jnp.concatenate([slot_rows, tags], axis=3)
    got = lax.all_to_all(payload, "replica", split_axis=0, concat_axis=0, tiled=True)
    got_rows = got[..., :part_width]
    got_ids = got[:, :, 0, part_width].astype(jnp.int32)
    got_ids = jnp.clip(got_ids, 0, adapter_down.shape[0] - 1)
    selected_up = adapter_up[got_ids]
    partial_value = down_project(got_rows, got_ids, adapter_down)
    summed = butterfly_sum(partial_value, "tensor").astype(jnp.bfloat16)
    summed = summed.reshape(summed.shape[:3] + (2, adapter_rank_size))
    owner_delta = (
        jnp.einsum("okscr,okcrw->okscw", summed, selected_up, preferred_element_type=jnp.float32)
        * ADAPTER_SCALE
    )
    slot_delta = lax.all_to_all(owner_delta, "replica", split_axis=0, concat_axis=0, tiled=True)
    flat_delta = slot_delta.reshape((replicas * CAP * SLOT,) + slot_delta.shape[3:])
    adapter_delta = flat_delta[fetch_slot[segment_index] * SLOT + token_position]
    base_projection = jnp.einsum(
        "jd,dcw->jcw", normed, key_value_weight, preferred_element_type=jnp.float32
    )
    current_key_value = base_projection + adapter_delta
    rotated = rotate(
        current_key_value[:, 0].reshape(row_count, kv_local, HEAD), cached_length
    ).reshape(row_count, kv_width)
    new_kv = jnp.stack([rotated, current_key_value[:, 1]], axis=1).astype(jnp.bfloat16)
    group_size = query.shape[1] // HEAD // kv_local
    attended = attend(query, key_value_cache, new_kv, cached_length, kv_local, group_size)
    return (new_kv, attended)


def solution(mesh):
    in_specs = (
        P("replica", "tensor"),
        P(),
        P(None, None, "tensor"),
        P("replica", "tensor", None),
        P("replica", None, None, "tensor"),
        P("replica", "tensor"),
        P("replica", None, None, "tensor"),
        P("replica", None),
        P("replica", None),
        P("replica"),
    )
    out_specs = (P("replica", None, "tensor"), P("replica", "tensor"))
    return jax.shard_map(body, mesh=mesh, in_specs=in_specs, out_specs=out_specs, check_vma=False)
```

```python
import functools

import jax
import jax.numpy as jnp
from jax import lax
from jax.experimental import pallas as pl
from jax.experimental.pallas import tpu as pltpu
from jax.sharding import PartitionSpec as P

HEAD = 128
ADP_DEV = 16
SLOT = 4
CAP = 2


ADAPTER_SCALE = 0.5
ROPE_BASE = 500000.0
EPSILON = 1e-05


def rotate(key_heads, token_position):
    half_size = key_heads.shape[-1] // 2
    inv_freq = ROPE_BASE ** (
        -(jnp.arange(half_size, dtype=jnp.float32) * 2.0) / key_heads.shape[-1]
    )
    angles = token_position.astype(jnp.float32)[:, None] * inv_freq[None, :]
    cosine_term = jnp.cos(angles)[:, None, :]
    sine_term = jnp.sin(angles)[:, None, :]
    first_half = key_heads[..., :half_size]
    second_half = key_heads[..., half_size:]
    return jnp.concatenate(
        [
            first_half * cosine_term - second_half * sine_term,
            second_half * cosine_term + first_half * sine_term,
        ],
        axis=-1,
    )


def score_kernel(len_ref, q_ref, kv_ref, s_ref, *, rows, kv_local, group_size):
    scale = float(HEAD) ** (-0.5)
    step = pl.program_id(0)
    cache_len = kv_ref.shape[1]
    width = kv_ref.shape[3]
    pos = lax.broadcasted_iota(jnp.int32, (group_size, 2 * cache_len), 1)
    for i in range(rows):
        length = len_ref[step * rows + i]
        stacked = kv_ref[i].reshape(2 * cache_len, width)
        live = (pos % 2 == 0) & (pos < 2 * length)
        for h in range(kv_local):
            cols = slice(h * HEAD, (h + 1) * HEAD)
            qrows = slice(h * group_size, (h + 1) * group_size)
            scores = lax.dot_general(
                q_ref[i, qrows, :], stacked[:, cols], (((1,), (1,)), ((), ())),
                preferred_element_type=jnp.float32,
            ) * scale
            s_ref[i, qrows, :] = jnp.where(live, scores, -jnp.inf)


def mix_kernel(q_ref, s_ref, kv_ref, nkv_ref, o_ref, *, rows, kv_local, group_size):
    scale = float(HEAD) ** (-0.5)
    cache_len = kv_ref.shape[1]
    width = kv_ref.shape[3]
    for i in range(rows):
        stacked = kv_ref[i].reshape(2 * cache_len, width)
        for h in range(kv_local):
            cols = slice(h * HEAD, (h + 1) * HEAD)
            qrows = slice(h * group_size, (h + 1) * group_size)
            q = q_ref[i, qrows, :]
            scores = s_ref[i, qrows, :]
            new_key = nkv_ref[i, 0:1, cols].astype(jnp.float32)
            new_value = nkv_ref[i, 1:2, cols].astype(jnp.float32)
            own = jnp.sum(q.astype(jnp.float32) * new_key, axis=1, keepdims=True) * scale
            top = jnp.maximum(jnp.max(scores, axis=1, keepdims=True), own)
            weights = jnp.exp(scores - top)
            own_weight = jnp.exp(own - top)
            total = jnp.sum(weights, axis=1, keepdims=True) + own_weight
            probs = pltpu.roll(weights / total, 1, 1).astype(jnp.bfloat16)
            own_prob = (own_weight / total).astype(jnp.bfloat16).astype(jnp.float32)
            context = jnp.dot(probs, stacked[:, cols], preferred_element_type=jnp.float32)
            context = context + own_prob * new_value
            o_ref[i, qrows, :] = context.astype(o_ref.dtype)


def attend(query, key_value_cache, new_kv, cached_length, kv_local, group_size):
    row_count = query.shape[0]
    cache_len = key_value_cache.shape[1]
    width = key_value_cache.shape[3]
    heads = kv_local * group_size
    rows = 4
    query_heads = query.reshape(row_count, heads, HEAD)
    opts = dict(rows=rows, kv_local=kv_local, group_size=group_size)
    cache_spec = pl.BlockSpec((rows, cache_len, 2, width), lambda b, *_: (b, 0, 0, 0))
    head_spec = pl.BlockSpec((rows, heads, HEAD), lambda b, *_: (b, 0, 0))
    score_spec = pl.BlockSpec((rows, heads, 2 * cache_len), lambda b, *_: (b, 0, 0))
    scores = pl.pallas_call(
        functools.partial(score_kernel, **opts),
        out_shape=jax.ShapeDtypeStruct((row_count, heads, 2 * cache_len), jnp.float32),
        grid_spec=pltpu.PrefetchScalarGridSpec(
            num_scalar_prefetch=1,
            grid=(row_count // rows,),
            in_specs=[head_spec, cache_spec],
            out_specs=score_spec,
        ),
    )(cached_length, query_heads, key_value_cache)
    out = pl.pallas_call(
        functools.partial(mix_kernel, **opts),
        out_shape=jax.ShapeDtypeStruct((row_count, heads, HEAD), jnp.bfloat16),
        grid=(row_count // rows,),
        in_specs=[
            head_spec,
            score_spec,
            cache_spec,
            pl.BlockSpec((rows, 2, width), lambda b: (b, 0, 0)),
        ],
        out_specs=head_spec,
    )(query_heads, scores, key_value_cache, new_kv)
    return out.reshape(row_count, heads * HEAD)


def butterfly_sum(value, axis):
    size = lax.axis_size(axis)
    if size & (size - 1):
        return lax.psum(value, axis)
    stride = 1
    while stride < size:
        pairs = [(i, i ^ stride) for i in range(size)]
        value = value + lax.ppermute(value, axis, pairs)
        stride *= 2
    return value


def body(
    hidden,
    input_norm_gain,
    key_value_weight,
    adapter_down,
    adapter_up,
    query,
    key_value_cache,
    segment_adapter,
    segment_sizes,
    cached_length,
):
    row_count = hidden.shape[0]
    part_width = hidden.shape[1]
    kv_width = key_value_weight.shape[2]
    kv_local = kv_width // HEAD
    cache_len = key_value_cache.shape[1]
    adapter_rank_size = adapter_up.shape[2]
    replicas = lax.axis_size("replica")
    segments = segment_sizes.shape[1]
    gathered = lax.all_gather(hidden, "tensor", axis=1, tiled=True)
    widened = gathered.astype(jnp.float32)
    normed = (
        widened
        * lax.rsqrt(jnp.mean(widened * widened, axis=1, keepdims=True) + EPSILON)
        * input_norm_gain
    ).astype(jnp.bfloat16)
    own_cols = lax.dynamic_slice_in_dim(
        normed, lax.axis_index("tensor") * part_width, part_width, 1
    )
    seg_counts = segment_sizes[0]
    adapters = segment_adapter[0]
    seg_ends = jnp.cumsum(seg_counts, dtype=jnp.int32)
    starts = seg_ends - seg_counts
    offsets = jnp.arange(SLOT, dtype=jnp.int32)
    row_ids = jnp.arange(row_count, dtype=jnp.int32)
    segment_index = jnp.sum((seg_ends[None, :] <= row_ids[:, None]).astype(jnp.int32), axis=1)
    token_position = row_ids - starts[segment_index]
    owners = adapters // ADP_DEV
    local_ids = adapters % ADP_DEV
    seg_ids = jnp.arange(segments, dtype=jnp.int32)
    slot_rank = jnp.sum(
        ((owners[None, :] == owners[:, None]) & (seg_ids[None, :] < seg_ids[:, None])).astype(
            jnp.int32
        ),
        axis=1,
    )
    owner_hit = (owners[None, None, :] == jnp.arange(replicas, dtype=jnp.int32)[:, None, None]) & (
        slot_rank[None, None, :] == jnp.arange(CAP, dtype=jnp.int32)[None, :, None]
    )
    wanted = jnp.sum(jnp.where(owner_hit, local_ids[None, None, :], 0), axis=2)
    fetch_slot = owners * CAP + slot_rank
    seg_at = jnp.sum(jnp.where(owner_hit, seg_ids[None, None, :], 0), axis=2)
    filled = jnp.any(owner_hit, axis=2)
    slot_counts = jnp.where(filled, seg_counts[seg_at], 0)
    slot_live = offsets[None, None, :] < slot_counts[:, :, None]
    source_row = jnp.where(slot_live, starts[seg_at][:, :, None] + offsets[None, None, :], 0)
    slot_rows = jnp.where(
        slot_live[:, :, :, None], own_cols[source_row], jnp.zeros((), jnp.bfloat16)
    )
    tags = jnp.broadcast_to(
        wanted.astype(jnp.bfloat16)[:, :, None, None], wanted.shape + (SLOT, HEAD)
    )
    payload = jnp.concatenate([slot_rows, tags], axis=3)
    got = lax.all_to_all(payload, "replica", split_axis=0, concat_axis=0, tiled=True)
    got_rows = got[..., :part_width]
    got_ids = got[:, :, 0, part_width].astype(jnp.int32)
    selected_down = adapter_down[got_ids]
    selected_up = adapter_up[got_ids]
    partial_value = jnp.einsum(
        "oksd,okdr->oksr", got_rows, selected_down, preferred_element_type=jnp.float32
    )
    summed = butterfly_sum(partial_value, "tensor").astype(jnp.bfloat16)
    summed = summed.reshape(summed.shape[:3] + (2, adapter_rank_size))
    owner_delta = (
        jnp.einsum("okscr,okcrw->okscw", summed, selected_up, preferred_element_type=jnp.float32)
        * ADAPTER_SCALE
    )
    slot_delta = lax.all_to_all(owner_delta, "replica", split_axis=0, concat_axis=0, tiled=True)
    flat_delta = slot_delta.reshape((replicas * CAP * SLOT,) + slot_delta.shape[3:])
    adapter_delta = flat_delta[fetch_slot[segment_index] * SLOT + token_position]
    base_projection = jnp.einsum(
        "jd,dcw->jcw", normed, key_value_weight, preferred_element_type=jnp.float32
    )
    current_key_value = base_projection + adapter_delta
    rotated = rotate(
        current_key_value[:, 0].reshape(row_count, kv_local, HEAD), cached_length
    ).reshape(row_count, kv_width)
    new_kv = jnp.stack([rotated, current_key_value[:, 1]], axis=1).astype(jnp.bfloat16)
    group_size = query.shape[1] // HEAD // kv_local
    attended = attend(query, key_value_cache, new_kv, cached_length, kv_local, group_size)
    return (new_kv, attended)


def solution(mesh):
    in_specs = (
        P("replica", "tensor"),
        P(),
        P(None, None, "tensor"),
        P("replica", "tensor", None),
        P("replica", None, None, "tensor"),
        P("replica", "tensor"),
        P("replica", None, None, "tensor"),
        P("replica", None),
        P("replica", None),
        P("replica"),
    )
    out_specs = (P("replica", None, "tensor"), P("replica", "tensor"))
    return jax.shard_map(body, mesh=mesh, in_specs=in_specs, out_specs=out_specs, check_vma=False)
```

```python
import functools

import jax
import jax.numpy as jnp
from jax import lax
from jax.experimental import pallas as pl
from jax.experimental.pallas import tpu as pltpu
from jax.sharding import PartitionSpec as P

HEAD = 128
ADP_DEV = 16
SLOT = 4
CAP = 2


ADAPTER_SCALE = 0.5
ROPE_BASE = 500000.0
EPSILON = 1e-05


def rotate(key_heads, token_position):
    half_size = key_heads.shape[-1] // 2
    inv_freq = ROPE_BASE ** (
        -(jnp.arange(half_size, dtype=jnp.float32) * 2.0) / key_heads.shape[-1]
    )
    angles = token_position.astype(jnp.float32)[:, None] * inv_freq[None, :]
    cosine_term = jnp.cos(angles)[:, None, :]
    sine_term = jnp.sin(angles)[:, None, :]
    first_half = key_heads[..., :half_size]
    second_half = key_heads[..., half_size:]
    return jnp.concatenate(
        [
            first_half * cosine_term - second_half * sine_term,
            second_half * cosine_term + first_half * sine_term,
        ],
        axis=-1,
    )


def score_kernel(len_ref, q_ref, kv_ref, s_ref, *, rows, kv_local, group_size):
    scale = float(HEAD) ** (-0.5)
    step = pl.program_id(0)
    cache_len = kv_ref.shape[1]
    width = kv_ref.shape[3]
    pos = lax.broadcasted_iota(jnp.int32, (group_size, 2 * cache_len), 1)
    for i in range(rows):
        length = len_ref[step * rows + i]
        stacked = kv_ref[i].reshape(2 * cache_len, width)
        live = (pos % 2 == 0) & (pos < 2 * length)
        for h in range(kv_local):
            cols = slice(h * HEAD, (h + 1) * HEAD)
            qrows = slice(h * group_size, (h + 1) * group_size)
            scores = lax.dot_general(
                q_ref[i, qrows, :], stacked[:, cols], (((1,), (1,)), ((), ())),
                preferred_element_type=jnp.float32,
            ) * scale
            s_ref[i, qrows, :] = jnp.where(live, scores, -jnp.inf)


def mix_kernel(q_ref, s_ref, kv_ref, nkv_ref, o_ref, *, rows, kv_local, group_size):
    scale = float(HEAD) ** (-0.5)
    cache_len = kv_ref.shape[1]
    width = kv_ref.shape[3]
    for i in range(rows):
        stacked = kv_ref[i].reshape(2 * cache_len, width)
        for h in range(kv_local):
            cols = slice(h * HEAD, (h + 1) * HEAD)
            qrows = slice(h * group_size, (h + 1) * group_size)
            q = q_ref[i, qrows, :]
            scores = s_ref[i, qrows, :]
            new_key = nkv_ref[i, 0:1, cols].astype(jnp.float32)
            new_value = nkv_ref[i, 1:2, cols].astype(jnp.float32)
            own = jnp.sum(q.astype(jnp.float32) * new_key, axis=1, keepdims=True) * scale
            top = jnp.maximum(jnp.max(scores, axis=1, keepdims=True), own)
            weights = jnp.exp(scores - top)
            own_weight = jnp.exp(own - top)
            total = jnp.sum(weights, axis=1, keepdims=True) + own_weight
            probs = pltpu.roll(weights / total, 1, 1).astype(jnp.bfloat16)
            own_prob = (own_weight / total).astype(jnp.bfloat16).astype(jnp.float32)
            context = jnp.dot(probs, stacked[:, cols], preferred_element_type=jnp.float32)
            context = context + own_prob * new_value
            o_ref[i, qrows, :] = context.astype(o_ref.dtype)


def attend(query, key_value_cache, new_kv, cached_length, kv_local, group_size):
    row_count = query.shape[0]
    cache_len = key_value_cache.shape[1]
    width = key_value_cache.shape[3]
    heads = kv_local * group_size
    rows = 4
    query_heads = query.reshape(row_count, heads, HEAD)
    opts = dict(rows=rows, kv_local=kv_local, group_size=group_size)
    cache_spec = pl.BlockSpec((rows, cache_len, 2, width), lambda b, *_: (b, 0, 0, 0))
    head_spec = pl.BlockSpec((rows, heads, HEAD), lambda b, *_: (b, 0, 0))
    score_spec = pl.BlockSpec((rows, heads, 2 * cache_len), lambda b, *_: (b, 0, 0))
    scores = pl.pallas_call(
        functools.partial(score_kernel, **opts),
        out_shape=jax.ShapeDtypeStruct((row_count, heads, 2 * cache_len), jnp.float32),
        grid_spec=pltpu.PrefetchScalarGridSpec(
            num_scalar_prefetch=1,
            grid=(row_count // rows,),
            in_specs=[head_spec, cache_spec],
            out_specs=score_spec,
        ),
    )(cached_length, query_heads, key_value_cache)
    out = pl.pallas_call(
        functools.partial(mix_kernel, **opts),
        out_shape=jax.ShapeDtypeStruct((row_count, heads, HEAD), jnp.bfloat16),
        grid=(row_count // rows,),
        in_specs=[
            head_spec,
            score_spec,
            cache_spec,
            pl.BlockSpec((rows, 2, width), lambda b: (b, 0, 0)),
        ],
        out_specs=head_spec,
    )(query_heads, scores, key_value_cache, new_kv)
    return out.reshape(row_count, heads * HEAD)


def butterfly_sum(value, axis):
    size = lax.axis_size(axis)
    if size & (size - 1):
        return lax.psum(value, axis)
    stride = 1
    while stride < size:
        pairs = [(i, i ^ stride) for i in range(size)]
        value = value + lax.ppermute(value, axis, pairs)
        stride *= 2
    return value


def body(
    hidden,
    input_norm_gain,
    key_value_weight,
    adapter_down,
    adapter_up,
    query,
    key_value_cache,
    segment_adapter,
    segment_sizes,
    cached_length,
):
    row_count = hidden.shape[0]
    part_width = hidden.shape[1]
    kv_width = key_value_weight.shape[2]
    kv_local = kv_width // HEAD
    cache_len = key_value_cache.shape[1]
    adapter_rank_size = adapter_up.shape[2]
    replicas = lax.axis_size("replica")
    segments = segment_sizes.shape[1]
    gathered = lax.all_gather(hidden, "tensor", axis=1, tiled=True)
    widened = gathered.astype(jnp.float32)
    normed = (
        widened
        * lax.rsqrt(jnp.mean(widened * widened, axis=1, keepdims=True) + EPSILON)
        * input_norm_gain
    ).astype(jnp.bfloat16)
    own_cols = lax.dynamic_slice_in_dim(
        normed, lax.axis_index("tensor") * part_width, part_width, 1
    )
    seg_counts = segment_sizes[0]
    adapters = segment_adapter[0]
    seg_ends = jnp.cumsum(seg_counts, dtype=jnp.int32)
    starts = seg_ends - seg_counts
    offsets = jnp.arange(SLOT, dtype=jnp.int32)
    row_ids = jnp.arange(row_count, dtype=jnp.int32)
    segment_index = jnp.sum((seg_ends[None, :] <= row_ids[:, None]).astype(jnp.int32), axis=1)
    token_position = row_ids - starts[segment_index]
    owners = adapters // ADP_DEV
    local_ids = adapters % ADP_DEV
    seg_ids = jnp.arange(segments, dtype=jnp.int32)
    slot_rank = jnp.sum(
        ((owners[None, :] == owners[:, None]) & (seg_ids[None, :] < seg_ids[:, None])).astype(
            jnp.int32
        ),
        axis=1,
    )
    owner_hit = (owners[None, None, :] == jnp.arange(replicas, dtype=jnp.int32)[:, None, None]) & (
        slot_rank[None, None, :] == jnp.arange(CAP, dtype=jnp.int32)[None, :, None]
    )
    wanted = jnp.sum(jnp.where(owner_hit, local_ids[None, None, :], 0), axis=2)
    fetch_slot = owners * CAP + slot_rank
    seg_at = jnp.sum(jnp.where(owner_hit, seg_ids[None, None, :], 0), axis=2)
    filled = jnp.any(owner_hit, axis=2)
    slot_counts = jnp.where(filled, seg_counts[seg_at], 0)
    slot_live = offsets[None, None, :] < slot_counts[:, :, None]
    source_row = jnp.where(slot_live, starts[seg_at][:, :, None] + offsets[None, None, :], 0)
    slot_rows = jnp.where(
        slot_live[:, :, :, None], own_cols[source_row], jnp.zeros((), jnp.bfloat16)
    )
    tags = jnp.broadcast_to(
        wanted.astype(jnp.bfloat16)[:, :, None, None], wanted.shape + (SLOT, HEAD)
    )
    payload = jnp.concatenate([slot_rows, tags], axis=3)
    got = lax.all_to_all(payload, "replica", split_axis=0, concat_axis=0, tiled=True)
    got_rows = got[..., :part_width]
    got_ids = got[:, :, 0, part_width].astype(jnp.int32)
    selected_up = adapter_up[got_ids]
    every_adapter = jnp.einsum(
        "oksd,adr->oksar", got_rows, adapter_down, preferred_element_type=jnp.float32
    )
    picked = got_ids[:, :, None] == jnp.arange(adapter_down.shape[0], dtype=jnp.int32)
    partial_value = jnp.sum(
        jnp.where(picked[:, :, None, :, None], every_adapter, 0.0), axis=3
    )
    summed = butterfly_sum(partial_value, "tensor").astype(jnp.bfloat16)
    summed = summed.reshape(summed.shape[:3] + (2, adapter_rank_size))
    owner_delta = (
        jnp.einsum("okscr,okcrw->okscw", summed, selected_up, preferred_element_type=jnp.float32)
        * ADAPTER_SCALE
    )
    slot_delta = lax.all_to_all(owner_delta, "replica", split_axis=0, concat_axis=0, tiled=True)
    flat_delta = slot_delta.reshape((replicas * CAP * SLOT,) + slot_delta.shape[3:])
    adapter_delta = flat_delta[fetch_slot[segment_index] * SLOT + token_position]
    base_projection = jnp.einsum(
        "jd,dcw->jcw", normed, key_value_weight, preferred_element_type=jnp.float32
    )
    current_key_value = base_projection + adapter_delta
    rotated = rotate(
        current_key_value[:, 0].reshape(row_count, kv_local, HEAD), cached_length
    ).reshape(row_count, kv_width)
    new_kv = jnp.stack([rotated, current_key_value[:, 1]], axis=1).astype(jnp.bfloat16)
    group_size = query.shape[1] // HEAD // kv_local
    attended = attend(query, key_value_cache, new_kv, cached_length, kv_local, group_size)
    return (new_kv, attended)


def solution(mesh):
    in_specs = (
        P("replica", "tensor"),
        P(),
        P(None, None, "tensor"),
        P("replica", "tensor", None),
        P("replica", None, None, "tensor"),
        P("replica", "tensor"),
        P("replica", None, None, "tensor"),
        P("replica", None),
        P("replica", None),
        P("replica"),
    )
    out_specs = (P("replica", None, "tensor"), P("replica", "tensor"))
    return jax.shard_map(body, mesh=mesh, in_specs=in_specs, out_specs=out_specs, check_vma=False)
```

```python
import functools

import jax
import jax.numpy as jnp
from jax import lax
from jax.experimental import pallas as pl
from jax.experimental.pallas import tpu as pltpu
from jax.sharding import PartitionSpec as P

HEAD = 128
ADP_DEV = 16
SLOT = 4
CAP = 2


ADAPTER_SCALE = 0.5
ROPE_BASE = 500000.0
EPSILON = 1e-05


def rotate(key_heads, token_position):
    half_size = key_heads.shape[-1] // 2
    inv_freq = ROPE_BASE ** (
        -(jnp.arange(half_size, dtype=jnp.float32) * 2.0) / key_heads.shape[-1]
    )
    angles = token_position.astype(jnp.float32)[:, None] * inv_freq[None, :]
    cosine_term = jnp.cos(angles)[:, None, :]
    sine_term = jnp.sin(angles)[:, None, :]
    first_half = key_heads[..., :half_size]
    second_half = key_heads[..., half_size:]
    return jnp.concatenate(
        [
            first_half * cosine_term - second_half * sine_term,
            second_half * cosine_term + first_half * sine_term,
        ],
        axis=-1,
    )


def score_kernel(len_ref, q_ref, kv_ref, s_ref, *, rows, kv_local, group_size):
    scale = float(HEAD) ** (-0.5)
    step = pl.program_id(0)
    cache_len = kv_ref.shape[1]
    width = kv_ref.shape[3]
    pos = lax.broadcasted_iota(jnp.int32, (group_size, 2 * cache_len), 1)
    for i in range(rows):
        length = len_ref[step * rows + i]
        stacked = kv_ref[i].reshape(2 * cache_len, width)
        live = (pos % 2 == 0) & (pos < 2 * length)
        for h in range(kv_local):
            cols = slice(h * HEAD, (h + 1) * HEAD)
            qrows = slice(h * group_size, (h + 1) * group_size)
            scores = lax.dot_general(
                q_ref[i, qrows, :], stacked[:, cols], (((1,), (1,)), ((), ())),
                preferred_element_type=jnp.float32,
            ) * scale
            s_ref[i, qrows, :] = jnp.where(live, scores, -jnp.inf)


def mix_kernel(q_ref, s_ref, kv_ref, nkv_ref, o_ref, *, rows, kv_local, group_size):
    scale = float(HEAD) ** (-0.5)
    cache_len = kv_ref.shape[1]
    width = kv_ref.shape[3]
    for i in range(rows):
        stacked = kv_ref[i].reshape(2 * cache_len, width)
        for h in range(kv_local):
            cols = slice(h * HEAD, (h + 1) * HEAD)
            qrows = slice(h * group_size, (h + 1) * group_size)
            q = q_ref[i, qrows, :]
            scores = s_ref[i, qrows, :]
            new_key = nkv_ref[i, 0:1, cols].astype(jnp.float32)
            new_value = nkv_ref[i, 1:2, cols].astype(jnp.float32)
            own = jnp.sum(q.astype(jnp.float32) * new_key, axis=1, keepdims=True) * scale
            top = jnp.maximum(jnp.max(scores, axis=1, keepdims=True), own)
            weights = jnp.exp(scores - top)
            own_weight = jnp.exp(own - top)
            total = jnp.sum(weights, axis=1, keepdims=True) + own_weight
            probs = pltpu.roll(weights / total, 1, 1).astype(jnp.bfloat16)
            own_prob = (own_weight / total).astype(jnp.bfloat16).astype(jnp.float32)
            context = jnp.dot(probs, stacked[:, cols], preferred_element_type=jnp.float32)
            context = context + own_prob * new_value
            context = context.astype(o_ref.dtype)
            for g in range(group_size):
                lanes = slice((h * group_size + g) * HEAD, (h * group_size + g + 1) * HEAD)
                o_ref[i:i + 1, lanes] = context[g:g + 1]


def attend(query, key_value_cache, new_kv, cached_length, kv_local, group_size):
    row_count = query.shape[0]
    cache_len = key_value_cache.shape[1]
    width = key_value_cache.shape[3]
    heads = kv_local * group_size
    rows = 4
    query_heads = query.reshape(row_count, heads, HEAD)
    opts = dict(rows=rows, kv_local=kv_local, group_size=group_size)
    cache_spec = pl.BlockSpec((rows, cache_len, 2, width), lambda b, *_: (b, 0, 0, 0))
    head_spec = pl.BlockSpec((rows, heads, HEAD), lambda b, *_: (b, 0, 0))
    score_spec = pl.BlockSpec((rows, heads, 2 * cache_len), lambda b, *_: (b, 0, 0))
    scores = pl.pallas_call(
        functools.partial(score_kernel, **opts),
        out_shape=jax.ShapeDtypeStruct((row_count, heads, 2 * cache_len), jnp.float32),
        grid_spec=pltpu.PrefetchScalarGridSpec(
            num_scalar_prefetch=1,
            grid=(row_count // rows,),
            in_specs=[head_spec, cache_spec],
            out_specs=score_spec,
        ),
    )(cached_length, query_heads, key_value_cache)
    mix_rows = 8 if row_count % 8 == 0 else row_count
    out = pl.pallas_call(
        functools.partial(mix_kernel, rows=mix_rows, kv_local=kv_local, group_size=group_size),
        out_shape=jax.ShapeDtypeStruct((row_count, heads * HEAD), jnp.bfloat16),
        grid=(row_count // mix_rows,),
        in_specs=[
            pl.BlockSpec((mix_rows, heads, HEAD), lambda b: (b, 0, 0)),
            pl.BlockSpec((mix_rows, heads, 2 * cache_len), lambda b: (b, 0, 0)),
            pl.BlockSpec((mix_rows, cache_len, 2, width), lambda b: (b, 0, 0, 0)),
            pl.BlockSpec((mix_rows, 2, width), lambda b: (b, 0, 0)),
        ],
        out_specs=pl.BlockSpec((mix_rows, heads * HEAD), lambda b: (b, 0)),
    )(query_heads, scores, key_value_cache, new_kv)
    return out


def butterfly_sum(value, axis):
    size = lax.axis_size(axis)
    if size & (size - 1):
        return lax.psum(value, axis)
    stride = 1
    while stride < size:
        pairs = [(i, i ^ stride) for i in range(size)]
        value = value + lax.ppermute(value, axis, pairs)
        stride *= 2
    return value


def body(
    hidden,
    input_norm_gain,
    key_value_weight,
    adapter_down,
    adapter_up,
    query,
    key_value_cache,
    segment_adapter,
    segment_sizes,
    cached_length,
):
    row_count = hidden.shape[0]
    part_width = hidden.shape[1]
    kv_width = key_value_weight.shape[2]
    kv_local = kv_width // HEAD
    cache_len = key_value_cache.shape[1]
    adapter_rank_size = adapter_up.shape[2]
    replicas = lax.axis_size("replica")
    segments = segment_sizes.shape[1]
    gathered = lax.all_gather(hidden, "tensor", axis=1, tiled=True)
    widened = gathered.astype(jnp.float32)
    normed = (
        widened
        * lax.rsqrt(jnp.mean(widened * widened, axis=1, keepdims=True) + EPSILON)
        * input_norm_gain
    ).astype(jnp.bfloat16)
    own_cols = lax.dynamic_slice_in_dim(
        normed, lax.axis_index("tensor") * part_width, part_width, 1
    )
    seg_counts = segment_sizes[0]
    adapters = segment_adapter[0]
    seg_ends = jnp.cumsum(seg_counts, dtype=jnp.int32)
    starts = seg_ends - seg_counts
    offsets = jnp.arange(SLOT, dtype=jnp.int32)
    row_ids = jnp.arange(row_count, dtype=jnp.int32)
    segment_index = jnp.sum((seg_ends[None, :] <= row_ids[:, None]).astype(jnp.int32), axis=1)
    token_position = row_ids - starts[segment_index]
    owners = adapters // ADP_DEV
    local_ids = adapters % ADP_DEV
    seg_ids = jnp.arange(segments, dtype=jnp.int32)
    slot_rank = jnp.sum(
        ((owners[None, :] == owners[:, None]) & (seg_ids[None, :] < seg_ids[:, None])).astype(
            jnp.int32
        ),
        axis=1,
    )
    owner_hit = (owners[None, None, :] == jnp.arange(replicas, dtype=jnp.int32)[:, None, None]) & (
        slot_rank[None, None, :] == jnp.arange(CAP, dtype=jnp.int32)[None, :, None]
    )
    wanted = jnp.sum(jnp.where(owner_hit, local_ids[None, None, :], 0), axis=2)
    fetch_slot = owners * CAP + slot_rank
    seg_at = jnp.sum(jnp.where(owner_hit, seg_ids[None, None, :], 0), axis=2)
    filled = jnp.any(owner_hit, axis=2)
    slot_counts = jnp.where(filled, seg_counts[seg_at], 0)
    slot_live = offsets[None, None, :] < slot_counts[:, :, None]
    source_row = jnp.where(slot_live, starts[seg_at][:, :, None] + offsets[None, None, :], 0)
    slot_rows = jnp.where(
        slot_live[:, :, :, None], own_cols[source_row], jnp.zeros((), jnp.bfloat16)
    )
    tags = jnp.broadcast_to(
        wanted.astype(jnp.bfloat16)[:, :, None, None], wanted.shape + (SLOT, HEAD)
    )
    payload = jnp.concatenate([slot_rows, tags], axis=3)
    got = lax.all_to_all(payload, "replica", split_axis=0, concat_axis=0, tiled=True)
    got_rows = got[..., :part_width]
    got_ids = got[:, :, 0, part_width].astype(jnp.int32)
    selected_up = adapter_up[got_ids]
    every_adapter = jnp.einsum(
        "oksd,adr->oksar", got_rows, adapter_down, preferred_element_type=jnp.float32
    )
    picked = got_ids[:, :, None] == jnp.arange(adapter_down.shape[0], dtype=jnp.int32)
    partial_value = jnp.sum(
        jnp.where(picked[:, :, None, :, None], every_adapter, 0.0), axis=3
    )
    summed = butterfly_sum(partial_value, "tensor").astype(jnp.bfloat16)
    summed = summed.reshape(summed.shape[:3] + (2, adapter_rank_size))
    owner_delta = (
        jnp.einsum("okscr,okcrw->okscw", summed, selected_up, preferred_element_type=jnp.float32)
        * ADAPTER_SCALE
    )
    slot_delta = lax.all_to_all(owner_delta, "replica", split_axis=0, concat_axis=0, tiled=True)
    flat_delta = slot_delta.reshape((replicas * CAP * SLOT,) + slot_delta.shape[3:])
    adapter_delta = flat_delta[fetch_slot[segment_index] * SLOT + token_position]
    base_projection = jnp.einsum(
        "jd,dcw->jcw", normed, key_value_weight, preferred_element_type=jnp.float32
    )
    current_key_value = base_projection + adapter_delta
    rotated = rotate(
        current_key_value[:, 0].reshape(row_count, kv_local, HEAD), cached_length
    ).reshape(row_count, kv_width)
    new_kv = jnp.stack([rotated, current_key_value[:, 1]], axis=1).astype(jnp.bfloat16)
    group_size = query.shape[1] // HEAD // kv_local
    attended = attend(query, key_value_cache, new_kv, cached_length, kv_local, group_size)
    return (new_kv, attended)


def solution(mesh):
    in_specs = (
        P("replica", "tensor"),
        P(),
        P(None, None, "tensor"),
        P("replica", "tensor", None),
        P("replica", None, None, "tensor"),
        P("replica", "tensor"),
        P("replica", None, None, "tensor"),
        P("replica", None),
        P("replica", None),
        P("replica"),
    )
    out_specs = (P("replica", None, "tensor"), P("replica", "tensor"))
    return jax.shard_map(body, mesh=mesh, in_specs=in_specs, out_specs=out_specs, check_vma=False)
```

```python
import functools

import jax
import jax.numpy as jnp
from jax import lax
from jax.experimental import pallas as pl
from jax.experimental.pallas import tpu as pltpu
from jax.sharding import PartitionSpec as P

HEAD = 128
ADP_DEV = 16
SLOT = 4
CAP = 2


ADAPTER_SCALE = 0.5
ROPE_BASE = 500000.0
EPSILON = 1e-05


def rotate(key_heads, token_position):
    half_size = key_heads.shape[-1] // 2
    inv_freq = ROPE_BASE ** (
        -(jnp.arange(half_size, dtype=jnp.float32) * 2.0) / key_heads.shape[-1]
    )
    angles = token_position.astype(jnp.float32)[:, None] * inv_freq[None, :]
    cosine_term = jnp.cos(angles)[:, None, :]
    sine_term = jnp.sin(angles)[:, None, :]
    first_half = key_heads[..., :half_size]
    second_half = key_heads[..., half_size:]
    return jnp.concatenate(
        [
            first_half * cosine_term - second_half * sine_term,
            second_half * cosine_term + first_half * sine_term,
        ],
        axis=-1,
    )


def score_kernel(len_ref, q_ref, kv_ref, s_ref, *, rows, kv_local, group_size):
    scale = float(HEAD) ** (-0.5)
    step = pl.program_id(0)
    cache_len = kv_ref.shape[1]
    width = kv_ref.shape[3]
    pos = lax.broadcasted_iota(jnp.int32, (group_size, 2 * cache_len), 1)
    for i in range(rows):
        length = len_ref[step * rows + i]
        stacked = kv_ref[i].reshape(2 * cache_len, width)
        live = (pos % 2 == 0) & (pos < 2 * length)
        for h in range(kv_local):
            cols = slice(h * HEAD, (h + 1) * HEAD)
            qrows = slice(h * group_size, (h + 1) * group_size)
            scores = lax.dot_general(
                q_ref[i, qrows, :], stacked[:, cols], (((1,), (1,)), ((), ())),
                preferred_element_type=jnp.float32,
            ) * scale
            s_ref[i, qrows, :] = jnp.where(live, scores, -jnp.inf)


def mix_kernel(q_ref, s_ref, kv_ref, nkv_ref, o_ref, *, rows, kv_local, group_size):
    scale = float(HEAD) ** (-0.5)
    cache_len = kv_ref.shape[1]
    width = kv_ref.shape[3]
    for i in range(rows):
        stacked = kv_ref[i].reshape(2 * cache_len, width)
        for h in range(kv_local):
            cols = slice(h * HEAD, (h + 1) * HEAD)
            qrows = slice(h * group_size, (h + 1) * group_size)
            q = q_ref[i, qrows, :]
            scores = s_ref[i, qrows, :]
            new_key = nkv_ref[i, 0:1, cols].astype(jnp.float32)
            new_value = nkv_ref[i, 1:2, cols].astype(jnp.float32)
            own = jnp.sum(q.astype(jnp.float32) * new_key, axis=1, keepdims=True) * scale
            top = jnp.maximum(jnp.max(scores, axis=1, keepdims=True), own)
            weights = jnp.exp(scores - top)
            own_weight = jnp.exp(own - top)
            total = jnp.sum(weights, axis=1, keepdims=True) + own_weight
            probs = pltpu.roll(weights / total, 1, 1).astype(jnp.bfloat16)
            own_prob = (own_weight / total).astype(jnp.bfloat16).astype(jnp.float32)
            context = jnp.dot(probs, stacked[:, cols], preferred_element_type=jnp.float32)
            context = context + own_prob * new_value
            context = context.astype(o_ref.dtype)
            for g in range(group_size):
                lanes = slice((h * group_size + g) * HEAD, (h * group_size + g + 1) * HEAD)
                o_ref[i:i + 1, lanes] = context[g:g + 1]


def attention_scores(query, key_value_cache, cached_length, kv_local, group_size):
    row_count = query.shape[0]
    cache_len = key_value_cache.shape[1]
    width = key_value_cache.shape[3]
    heads = kv_local * group_size
    rows = 4
    query_heads = query.reshape(row_count, heads, HEAD)
    opts = dict(rows=rows, kv_local=kv_local, group_size=group_size)
    cache_spec = pl.BlockSpec((rows, cache_len, 2, width), lambda b, *_: (b, 0, 0, 0))
    head_spec = pl.BlockSpec((rows, heads, HEAD), lambda b, *_: (b, 0, 0))
    score_spec = pl.BlockSpec((rows, heads, 2 * cache_len), lambda b, *_: (b, 0, 0))
    scores = pl.pallas_call(
        functools.partial(score_kernel, **opts),
        out_shape=jax.ShapeDtypeStruct((row_count, heads, 2 * cache_len), jnp.float32),
        grid_spec=pltpu.PrefetchScalarGridSpec(
            num_scalar_prefetch=1,
            grid=(row_count // rows,),
            in_specs=[head_spec, cache_spec],
            out_specs=score_spec,
        ),
    )(cached_length, query_heads, key_value_cache)
    return query_heads, scores


def attend(query_heads, scores, key_value_cache, new_kv, kv_local, group_size):
    row_count = query_heads.shape[0]
    cache_len = key_value_cache.shape[1]
    width = key_value_cache.shape[3]
    heads = kv_local * group_size
    mix_rows = 8 if row_count % 8 == 0 else row_count
    out = pl.pallas_call(
        functools.partial(mix_kernel, rows=mix_rows, kv_local=kv_local, group_size=group_size),
        out_shape=jax.ShapeDtypeStruct((row_count, heads * HEAD), jnp.bfloat16),
        grid=(row_count // mix_rows,),
        in_specs=[
            pl.BlockSpec((mix_rows, heads, HEAD), lambda b: (b, 0, 0)),
            pl.BlockSpec((mix_rows, heads, 2 * cache_len), lambda b: (b, 0, 0)),
            pl.BlockSpec((mix_rows, cache_len, 2, width), lambda b: (b, 0, 0, 0)),
            pl.BlockSpec((mix_rows, 2, width), lambda b: (b, 0, 0)),
        ],
        out_specs=pl.BlockSpec((mix_rows, heads * HEAD), lambda b: (b, 0)),
    )(query_heads, scores, key_value_cache, new_kv)
    return out


def butterfly_sum(value, axis):
    size = lax.axis_size(axis)
    if size & (size - 1):
        return lax.psum(value, axis)
    stride = 1
    while stride < size:
        pairs = [(i, i ^ stride) for i in range(size)]
        value = value + lax.ppermute(value, axis, pairs)
        stride *= 2
    return value


def body(
    hidden,
    input_norm_gain,
    key_value_weight,
    adapter_down,
    adapter_up,
    query,
    key_value_cache,
    segment_adapter,
    segment_sizes,
    cached_length,
):
    row_count = hidden.shape[0]
    part_width = hidden.shape[1]
    kv_width = key_value_weight.shape[2]
    kv_local = kv_width // HEAD
    cache_len = key_value_cache.shape[1]
    adapter_rank_size = adapter_up.shape[2]
    replicas = lax.axis_size("replica")
    segments = segment_sizes.shape[1]
    gathered = lax.all_gather(hidden, "tensor", axis=1, tiled=True)
    widened = gathered.astype(jnp.float32)
    normed = (
        widened
        * lax.rsqrt(jnp.mean(widened * widened, axis=1, keepdims=True) + EPSILON)
        * input_norm_gain
    ).astype(jnp.bfloat16)
    own_cols = lax.dynamic_slice_in_dim(
        normed, lax.axis_index("tensor") * part_width, part_width, 1
    )
    seg_counts = segment_sizes[0]
    adapters = segment_adapter[0]
    seg_ends = jnp.cumsum(seg_counts, dtype=jnp.int32)
    starts = seg_ends - seg_counts
    offsets = jnp.arange(SLOT, dtype=jnp.int32)
    row_ids = jnp.arange(row_count, dtype=jnp.int32)
    segment_index = jnp.sum((seg_ends[None, :] <= row_ids[:, None]).astype(jnp.int32), axis=1)
    token_position = row_ids - starts[segment_index]
    owners = adapters // ADP_DEV
    local_ids = adapters % ADP_DEV
    seg_ids = jnp.arange(segments, dtype=jnp.int32)
    slot_rank = jnp.sum(
        ((owners[None, :] == owners[:, None]) & (seg_ids[None, :] < seg_ids[:, None])).astype(
            jnp.int32
        ),
        axis=1,
    )
    owner_hit = (owners[None, None, :] == jnp.arange(replicas, dtype=jnp.int32)[:, None, None]) & (
        slot_rank[None, None, :] == jnp.arange(CAP, dtype=jnp.int32)[None, :, None]
    )
    wanted = jnp.sum(jnp.where(owner_hit, local_ids[None, None, :], 0), axis=2)
    fetch_slot = owners * CAP + slot_rank
    seg_at = jnp.sum(jnp.where(owner_hit, seg_ids[None, None, :], 0), axis=2)
    filled = jnp.any(owner_hit, axis=2)
    slot_counts = jnp.where(filled, seg_counts[seg_at], 0)
    slot_live = offsets[None, None, :] < slot_counts[:, :, None]
    source_row = jnp.where(slot_live, starts[seg_at][:, :, None] + offsets[None, None, :], 0)
    slot_rows = jnp.where(
        slot_live[:, :, :, None], own_cols[source_row], jnp.zeros((), jnp.bfloat16)
    )
    tags = jnp.broadcast_to(
        wanted.astype(jnp.bfloat16)[:, :, None, None], wanted.shape + (SLOT, HEAD)
    )
    payload = jnp.concatenate([slot_rows, tags], axis=3)
    got = lax.all_to_all(payload, "replica", split_axis=0, concat_axis=0, tiled=True)
    group_size = query.shape[1] // HEAD // kv_local
    query_heads, scores = attention_scores(
        query, key_value_cache, cached_length, kv_local, group_size
    )
    got, query_heads, scores = lax.optimization_barrier((got, query_heads, scores))
    got_rows = got[..., :part_width]
    got_ids = got[:, :, 0, part_width].astype(jnp.int32)
    selected_up = adapter_up[got_ids]
    every_adapter = jnp.einsum(
        "oksd,adr->oksar", got_rows, adapter_down, preferred_element_type=jnp.float32
    )
    picked = got_ids[:, :, None] == jnp.arange(adapter_down.shape[0], dtype=jnp.int32)
    partial_value = jnp.sum(
        jnp.where(picked[:, :, None, :, None], every_adapter, 0.0), axis=3
    )
    summed = butterfly_sum(partial_value, "tensor").astype(jnp.bfloat16)
    summed = summed.reshape(summed.shape[:3] + (2, adapter_rank_size))
    owner_delta = (
        jnp.einsum("okscr,okcrw->okscw", summed, selected_up, preferred_element_type=jnp.float32)
        * ADAPTER_SCALE
    )
    owner_delta, late_normed = lax.optimization_barrier((owner_delta, normed))
    slot_delta = lax.all_to_all(owner_delta, "replica", split_axis=0, concat_axis=0, tiled=True)
    flat_delta = slot_delta.reshape((replicas * CAP * SLOT,) + slot_delta.shape[3:])
    adapter_delta = flat_delta[fetch_slot[segment_index] * SLOT + token_position]
    base_projection = jnp.einsum(
        "jd,dcw->jcw", late_normed, key_value_weight, preferred_element_type=jnp.float32
    )
    current_key_value = base_projection + adapter_delta
    rotated = rotate(
        current_key_value[:, 0].reshape(row_count, kv_local, HEAD), cached_length
    ).reshape(row_count, kv_width)
    new_kv = jnp.stack([rotated, current_key_value[:, 1]], axis=1).astype(jnp.bfloat16)
    group_size = query.shape[1] // HEAD // kv_local
    attended = attend(query_heads, scores, key_value_cache, new_kv, kv_local, group_size)
    return (new_kv, attended)


def solution(mesh):
    in_specs = (
        P("replica", "tensor"),
        P(),
        P(None, None, "tensor"),
        P("replica", "tensor", None),
        P("replica", None, None, "tensor"),
        P("replica", "tensor"),
        P("replica", None, None, "tensor"),
        P("replica", None),
        P("replica", None),
        P("replica"),
    )
    out_specs = (P("replica", None, "tensor"), P("replica", "tensor"))
    return jax.shard_map(body, mesh=mesh, in_specs=in_specs, out_specs=out_specs, check_vma=False)
```

```python
import functools

import jax
import jax.numpy as jnp
from jax import lax
from jax.experimental import pallas as pl
from jax.experimental.pallas import tpu as pltpu
from jax.sharding import PartitionSpec as P

HEAD = 128
ADP_DEV = 16
SLOT = 4
CAP = 2


ADAPTER_SCALE = 0.5
ROPE_BASE = 500000.0
EPSILON = 1e-05


def rotate(key_heads, token_position):
    half_size = key_heads.shape[-1] // 2
    inv_freq = ROPE_BASE ** (
        -(jnp.arange(half_size, dtype=jnp.float32) * 2.0) / key_heads.shape[-1]
    )
    angles = token_position.astype(jnp.float32)[:, None] * inv_freq[None, :]
    cosine_term = jnp.cos(angles)[:, None, :]
    sine_term = jnp.sin(angles)[:, None, :]
    first_half = key_heads[..., :half_size]
    second_half = key_heads[..., half_size:]
    return jnp.concatenate(
        [
            first_half * cosine_term - second_half * sine_term,
            second_half * cosine_term + first_half * sine_term,
        ],
        axis=-1,
    )


def score_kernel(len_ref, q_ref, kv_ref, s_ref, *, rows, kv_local, group_size):
    scale = float(HEAD) ** (-0.5)
    step = pl.program_id(0)
    cache_len = kv_ref.shape[1]
    width = kv_ref.shape[3]
    pos = lax.broadcasted_iota(jnp.int32, (group_size, 2 * cache_len), 1)
    for i in range(rows):
        length = len_ref[step * rows + i]
        stacked = kv_ref[i].reshape(2 * cache_len, width)
        live = (pos % 2 == 0) & (pos < 2 * length)
        for h in range(kv_local):
            cols = slice(h * HEAD, (h + 1) * HEAD)
            qrows = slice(h * group_size, (h + 1) * group_size)
            scores = lax.dot_general(
                q_ref[i, qrows, :], stacked[:, cols], (((1,), (1,)), ((), ())),
                preferred_element_type=jnp.float32,
            ) * scale
            s_ref[i, qrows, :] = jnp.where(live, scores, -jnp.inf)


def mix_kernel(q_ref, s_ref, kv_ref, nkv_ref, o_ref, *, rows, kv_local, group_size):
    scale = float(HEAD) ** (-0.5)
    cache_len = kv_ref.shape[1]
    width = kv_ref.shape[3]
    for i in range(rows):
        stacked = kv_ref[i].reshape(2 * cache_len, width)
        for h in range(kv_local):
            cols = slice(h * HEAD, (h + 1) * HEAD)
            qrows = slice(h * group_size, (h + 1) * group_size)
            q = q_ref[i, qrows, :]
            scores = s_ref[i, qrows, :]
            new_key = nkv_ref[i, 0:1, cols].astype(jnp.float32)
            new_value = nkv_ref[i, 1:2, cols].astype(jnp.float32)
            own = jnp.sum(q.astype(jnp.float32) * new_key, axis=1, keepdims=True) * scale
            top = jnp.maximum(jnp.max(scores, axis=1, keepdims=True), own)
            weights = jnp.exp(scores - top)
            own_weight = jnp.exp(own - top)
            total = jnp.sum(weights, axis=1, keepdims=True) + own_weight
            probs = pltpu.roll(weights / total, 1, 1).astype(jnp.bfloat16)
            own_prob = (own_weight / total).astype(jnp.bfloat16).astype(jnp.float32)
            context = jnp.dot(probs, stacked[:, cols], preferred_element_type=jnp.float32)
            context = context + own_prob * new_value
            context = context.astype(o_ref.dtype)
            for g in range(group_size):
                lanes = slice((h * group_size + g) * HEAD, (h * group_size + g + 1) * HEAD)
                o_ref[i:i + 1, lanes] = context[g:g + 1]


def attend(query, key_value_cache, new_kv, cached_length, kv_local, group_size):
    row_count = query.shape[0]
    cache_len = key_value_cache.shape[1]
    width = key_value_cache.shape[3]
    heads = kv_local * group_size
    rows = 8 if row_count % 8 == 0 else row_count
    query_heads = query.reshape(row_count, heads, HEAD)
    opts = dict(rows=rows, kv_local=kv_local, group_size=group_size)
    cache_spec = pl.BlockSpec((rows, cache_len, 2, width), lambda b, *_: (b, 0, 0, 0))
    head_spec = pl.BlockSpec((rows, heads, HEAD), lambda b, *_: (b, 0, 0))
    score_spec = pl.BlockSpec((rows, heads, 2 * cache_len), lambda b, *_: (b, 0, 0))
    scores = pl.pallas_call(
        functools.partial(score_kernel, **opts),
        out_shape=jax.ShapeDtypeStruct((row_count, heads, 2 * cache_len), jnp.float32),
        grid_spec=pltpu.PrefetchScalarGridSpec(
            num_scalar_prefetch=1,
            grid=(row_count // rows,),
            in_specs=[head_spec, cache_spec],
            out_specs=score_spec,
        ),
    )(cached_length, query_heads, key_value_cache)
    mix_rows = 8 if row_count % 8 == 0 else row_count
    out = pl.pallas_call(
        functools.partial(mix_kernel, rows=mix_rows, kv_local=kv_local, group_size=group_size),
        out_shape=jax.ShapeDtypeStruct((row_count, heads * HEAD), jnp.bfloat16),
        grid=(row_count // mix_rows,),
        in_specs=[
            pl.BlockSpec((mix_rows, heads, HEAD), lambda b: (b, 0, 0)),
            pl.BlockSpec((mix_rows, heads, 2 * cache_len), lambda b: (b, 0, 0)),
            pl.BlockSpec((mix_rows, cache_len, 2, width), lambda b: (b, 0, 0, 0)),
            pl.BlockSpec((mix_rows, 2, width), lambda b: (b, 0, 0)),
        ],
        out_specs=pl.BlockSpec((mix_rows, heads * HEAD), lambda b: (b, 0)),
    )(query_heads, scores, key_value_cache, new_kv)
    return out


def butterfly_sum(value, axis):
    size = lax.axis_size(axis)
    if size & (size - 1):
        return lax.psum(value, axis)
    stride = 1
    while stride < size:
        pairs = [(i, i ^ stride) for i in range(size)]
        value = value + lax.ppermute(value, axis, pairs)
        stride *= 2
    return value


def body(
    hidden,
    input_norm_gain,
    key_value_weight,
    adapter_down,
    adapter_up,
    query,
    key_value_cache,
    segment_adapter,
    segment_sizes,
    cached_length,
):
    row_count = hidden.shape[0]
    part_width = hidden.shape[1]
    kv_width = key_value_weight.shape[2]
    kv_local = kv_width // HEAD
    cache_len = key_value_cache.shape[1]
    adapter_rank_size = adapter_up.shape[2]
    replicas = lax.axis_size("replica")
    segments = segment_sizes.shape[1]
    gathered = lax.all_gather(hidden, "tensor", axis=1, tiled=True)
    widened = gathered.astype(jnp.float32)
    normed = (
        widened
        * lax.rsqrt(jnp.mean(widened * widened, axis=1, keepdims=True) + EPSILON)
        * input_norm_gain
    ).astype(jnp.bfloat16)
    own_cols = lax.dynamic_slice_in_dim(
        normed, lax.axis_index("tensor") * part_width, part_width, 1
    )
    seg_counts = segment_sizes[0]
    adapters = segment_adapter[0]
    seg_ends = jnp.cumsum(seg_counts, dtype=jnp.int32)
    starts = seg_ends - seg_counts
    offsets = jnp.arange(SLOT, dtype=jnp.int32)
    row_ids = jnp.arange(row_count, dtype=jnp.int32)
    segment_index = jnp.sum((seg_ends[None, :] <= row_ids[:, None]).astype(jnp.int32), axis=1)
    token_position = row_ids - starts[segment_index]
    owners = adapters // ADP_DEV
    local_ids = adapters % ADP_DEV
    seg_ids = jnp.arange(segments, dtype=jnp.int32)
    slot_rank = jnp.sum(
        ((owners[None, :] == owners[:, None]) & (seg_ids[None, :] < seg_ids[:, None])).astype(
            jnp.int32
        ),
        axis=1,
    )
    owner_hit = (owners[None, None, :] == jnp.arange(replicas, dtype=jnp.int32)[:, None, None]) & (
        slot_rank[None, None, :] == jnp.arange(CAP, dtype=jnp.int32)[None, :, None]
    )
    wanted = jnp.sum(jnp.where(owner_hit, local_ids[None, None, :], 0), axis=2)
    fetch_slot = owners * CAP + slot_rank
    seg_at = jnp.sum(jnp.where(owner_hit, seg_ids[None, None, :], 0), axis=2)
    filled = jnp.any(owner_hit, axis=2)
    slot_counts = jnp.where(filled, seg_counts[seg_at], 0)
    slot_live = offsets[None, None, :] < slot_counts[:, :, None]
    source_row = jnp.where(slot_live, starts[seg_at][:, :, None] + offsets[None, None, :], 0)
    slot_rows = jnp.where(
        slot_live[:, :, :, None], own_cols[source_row], jnp.zeros((), jnp.bfloat16)
    )
    tags = jnp.broadcast_to(
        wanted.astype(jnp.bfloat16)[:, :, None, None], wanted.shape + (SLOT, HEAD)
    )
    payload = jnp.concatenate([slot_rows, tags], axis=3)
    got = lax.all_to_all(payload, "replica", split_axis=0, concat_axis=0, tiled=True)
    got_rows = got[..., :part_width]
    got_ids = got[:, :, 0, part_width].astype(jnp.int32)
    selected_up = adapter_up[got_ids]
    every_adapter = jnp.einsum(
        "oksd,adr->oksar", got_rows, adapter_down, preferred_element_type=jnp.float32
    )
    picked = got_ids[:, :, None] == jnp.arange(adapter_down.shape[0], dtype=jnp.int32)
    partial_value = jnp.sum(
        jnp.where(picked[:, :, None, :, None], every_adapter, 0.0), axis=3
    )
    summed = butterfly_sum(partial_value, "tensor").astype(jnp.bfloat16)
    summed = summed.reshape(summed.shape[:3] + (2, adapter_rank_size))
    owner_delta = (
        jnp.einsum("okscr,okcrw->okscw", summed, selected_up, preferred_element_type=jnp.float32)
        * ADAPTER_SCALE
    )
    slot_delta = lax.all_to_all(owner_delta, "replica", split_axis=0, concat_axis=0, tiled=True)
    flat_delta = slot_delta.reshape((replicas * CAP * SLOT,) + slot_delta.shape[3:])
    adapter_delta = flat_delta[fetch_slot[segment_index] * SLOT + token_position]
    base_projection = jnp.einsum(
        "jd,dcw->jcw", normed, key_value_weight, preferred_element_type=jnp.float32
    )
    current_key_value = base_projection + adapter_delta
    rotated = rotate(
        current_key_value[:, 0].reshape(row_count, kv_local, HEAD), cached_length
    ).reshape(row_count, kv_width)
    new_kv = jnp.stack([rotated, current_key_value[:, 1]], axis=1).astype(jnp.bfloat16)
    group_size = query.shape[1] // HEAD // kv_local
    attended = attend(query, key_value_cache, new_kv, cached_length, kv_local, group_size)
    return (new_kv, attended)


def solution(mesh):
    in_specs = (
        P("replica", "tensor"),
        P(),
        P(None, None, "tensor"),
        P("replica", "tensor", None),
        P("replica", None, None, "tensor"),
        P("replica", "tensor"),
        P("replica", None, None, "tensor"),
        P("replica", None),
        P("replica", None),
        P("replica"),
    )
    out_specs = (P("replica", None, "tensor"), P("replica", "tensor"))
    return jax.shard_map(body, mesh=mesh, in_specs=in_specs, out_specs=out_specs, check_vma=False)
```

```python
import functools

import jax
import jax.numpy as jnp
from jax import lax
from jax.experimental import pallas as pl
from jax.experimental.pallas import tpu as pltpu
from jax.sharding import PartitionSpec as P

HEAD = 128
ADP_DEV = 16
SLOT = 4
CAP = 2


ADAPTER_SCALE = 0.5
ROPE_BASE = 500000.0
EPSILON = 1e-05


def rotate(key_heads, token_position):
    half_size = key_heads.shape[-1] // 2
    inv_freq = ROPE_BASE ** (
        -(jnp.arange(half_size, dtype=jnp.float32) * 2.0) / key_heads.shape[-1]
    )
    angles = token_position.astype(jnp.float32)[:, None] * inv_freq[None, :]
    cosine_term = jnp.cos(angles)[:, None, :]
    sine_term = jnp.sin(angles)[:, None, :]
    first_half = key_heads[..., :half_size]
    second_half = key_heads[..., half_size:]
    return jnp.concatenate(
        [
            first_half * cosine_term - second_half * sine_term,
            second_half * cosine_term + first_half * sine_term,
        ],
        axis=-1,
    )


def score_kernel(len_ref, q_ref, kv_ref, s_ref, *, rows, kv_local, group_size):
    scale = float(HEAD) ** (-0.5)
    step = pl.program_id(0)
    cache_len = kv_ref.shape[1]
    width = kv_ref.shape[3]
    pos = lax.broadcasted_iota(jnp.int32, (group_size, 2 * cache_len), 1)
    for i in range(rows):
        length = len_ref[step * rows + i]
        stacked = kv_ref[i].reshape(2 * cache_len, width)
        live = (pos % 2 == 0) & (pos < 2 * length)
        for h in range(kv_local):
            cols = slice(h * HEAD, (h + 1) * HEAD)
            qrows = slice(h * group_size, (h + 1) * group_size)
            scores = lax.dot_general(
                q_ref[i, qrows, :], stacked[:, cols], (((1,), (1,)), ((), ())),
                preferred_element_type=jnp.float32,
            ) * scale
            s_ref[i, qrows, :] = jnp.where(live, scores, -jnp.inf)


def mix_kernel(q_ref, s_ref, kv_ref, nkv_ref, o_ref, *, rows, kv_local, group_size):
    scale = float(HEAD) ** (-0.5)
    cache_len = kv_ref.shape[1]
    width = kv_ref.shape[3]
    for i in range(rows):
        stacked = kv_ref[i].reshape(2 * cache_len, width)
        for h in range(kv_local):
            cols = slice(h * HEAD, (h + 1) * HEAD)
            qrows = slice(h * group_size, (h + 1) * group_size)
            q = q_ref[i, qrows, :]
            scores = s_ref[i, qrows, :]
            new_key = nkv_ref[i, 0:1, cols].astype(jnp.float32)
            new_value = nkv_ref[i, 1:2, cols].astype(jnp.float32)
            own = jnp.sum(q.astype(jnp.float32) * new_key, axis=1, keepdims=True) * scale
            top = jnp.maximum(jnp.max(scores, axis=1, keepdims=True), own)
            weights = jnp.exp(scores - top)
            own_weight = jnp.exp(own - top)
            total = jnp.sum(weights, axis=1, keepdims=True) + own_weight
            probs = pltpu.roll(weights / total, 1, 1).astype(jnp.bfloat16)
            own_prob = (own_weight / total).astype(jnp.bfloat16).astype(jnp.float32)
            context = jnp.dot(probs, stacked[:, cols], preferred_element_type=jnp.float32)
            context = context + own_prob * new_value
            context = context.astype(o_ref.dtype)
            for g in range(group_size):
                lanes = slice((h * group_size + g) * HEAD, (h * group_size + g + 1) * HEAD)
                o_ref[i:i + 1, lanes] = context[g:g + 1]


def attend(query, key_value_cache, new_kv, cached_length, kv_local, group_size):
    row_count = query.shape[0]
    cache_len = key_value_cache.shape[1]
    width = key_value_cache.shape[3]
    heads = kv_local * group_size
    rows = 16 if row_count % 16 == 0 else row_count
    query_heads = query.reshape(row_count, heads, HEAD)
    opts = dict(rows=rows, kv_local=kv_local, group_size=group_size)
    cache_spec = pl.BlockSpec((rows, cache_len, 2, width), lambda b, *_: (b, 0, 0, 0))
    head_spec = pl.BlockSpec((rows, heads, HEAD), lambda b, *_: (b, 0, 0))
    score_spec = pl.BlockSpec((rows, heads, 2 * cache_len), lambda b, *_: (b, 0, 0))
    scores = pl.pallas_call(
        functools.partial(score_kernel, **opts),
        out_shape=jax.ShapeDtypeStruct((row_count, heads, 2 * cache_len), jnp.float32),
        grid_spec=pltpu.PrefetchScalarGridSpec(
            num_scalar_prefetch=1,
            grid=(row_count // rows,),
            in_specs=[head_spec, cache_spec],
            out_specs=score_spec,
        ),
    )(cached_length, query_heads, key_value_cache)
    mix_rows = 16 if row_count % 16 == 0 else row_count
    out = pl.pallas_call(
        functools.partial(mix_kernel, rows=mix_rows, kv_local=kv_local, group_size=group_size),
        out_shape=jax.ShapeDtypeStruct((row_count, heads * HEAD), jnp.bfloat16),
        grid=(row_count // mix_rows,),
        in_specs=[
            pl.BlockSpec((mix_rows, heads, HEAD), lambda b: (b, 0, 0)),
            pl.BlockSpec((mix_rows, heads, 2 * cache_len), lambda b: (b, 0, 0)),
            pl.BlockSpec((mix_rows, cache_len, 2, width), lambda b: (b, 0, 0, 0)),
            pl.BlockSpec((mix_rows, 2, width), lambda b: (b, 0, 0)),
        ],
        out_specs=pl.BlockSpec((mix_rows, heads * HEAD), lambda b: (b, 0)),
    )(query_heads, scores, key_value_cache, new_kv)
    return out


def butterfly_sum(value, axis):
    size = lax.axis_size(axis)
    if size & (size - 1):
        return lax.psum(value, axis)
    stride = 1
    while stride < size:
        pairs = [(i, i ^ stride) for i in range(size)]
        value = value + lax.ppermute(value, axis, pairs)
        stride *= 2
    return value


def body(
    hidden,
    input_norm_gain,
    key_value_weight,
    adapter_down,
    adapter_up,
    query,
    key_value_cache,
    segment_adapter,
    segment_sizes,
    cached_length,
):
    row_count = hidden.shape[0]
    part_width = hidden.shape[1]
    kv_width = key_value_weight.shape[2]
    kv_local = kv_width // HEAD
    cache_len = key_value_cache.shape[1]
    adapter_rank_size = adapter_up.shape[2]
    replicas = lax.axis_size("replica")
    segments = segment_sizes.shape[1]
    gathered = lax.all_gather(hidden, "tensor", axis=1, tiled=True)
    widened = gathered.astype(jnp.float32)
    normed = (
        widened
        * lax.rsqrt(jnp.mean(widened * widened, axis=1, keepdims=True) + EPSILON)
        * input_norm_gain
    ).astype(jnp.bfloat16)
    own_cols = lax.dynamic_slice_in_dim(
        normed, lax.axis_index("tensor") * part_width, part_width, 1
    )
    seg_counts = segment_sizes[0]
    adapters = segment_adapter[0]
    seg_ends = jnp.cumsum(seg_counts, dtype=jnp.int32)
    starts = seg_ends - seg_counts
    offsets = jnp.arange(SLOT, dtype=jnp.int32)
    row_ids = jnp.arange(row_count, dtype=jnp.int32)
    segment_index = jnp.sum((seg_ends[None, :] <= row_ids[:, None]).astype(jnp.int32), axis=1)
    token_position = row_ids - starts[segment_index]
    owners = adapters // ADP_DEV
    local_ids = adapters % ADP_DEV
    seg_ids = jnp.arange(segments, dtype=jnp.int32)
    slot_rank = jnp.sum(
        ((owners[None, :] == owners[:, None]) & (seg_ids[None, :] < seg_ids[:, None])).astype(
            jnp.int32
        ),
        axis=1,
    )
    owner_hit = (owners[None, None, :] == jnp.arange(replicas, dtype=jnp.int32)[:, None, None]) & (
        slot_rank[None, None, :] == jnp.arange(CAP, dtype=jnp.int32)[None, :, None]
    )
    wanted = jnp.sum(jnp.where(owner_hit, local_ids[None, None, :], 0), axis=2)
    fetch_slot = owners * CAP + slot_rank
    seg_at = jnp.sum(jnp.where(owner_hit, seg_ids[None, None, :], 0), axis=2)
    filled = jnp.any(owner_hit, axis=2)
    slot_counts = jnp.where(filled, seg_counts[seg_at], 0)
    slot_live = offsets[None, None, :] < slot_counts[:, :, None]
    source_row = jnp.where(slot_live, starts[seg_at][:, :, None] + offsets[None, None, :], 0)
    slot_rows = jnp.where(
        slot_live[:, :, :, None], own_cols[source_row], jnp.zeros((), jnp.bfloat16)
    )
    tags = jnp.broadcast_to(
        wanted.astype(jnp.bfloat16)[:, :, None, None], wanted.shape + (SLOT, HEAD)
    )
    payload = jnp.concatenate([slot_rows, tags], axis=3)
    got = lax.all_to_all(payload, "replica", split_axis=0, concat_axis=0, tiled=True)
    got_rows = got[..., :part_width]
    got_ids = got[:, :, 0, part_width].astype(jnp.int32)
    selected_up = adapter_up[got_ids]
    every_adapter = jnp.einsum(
        "oksd,adr->oksar", got_rows, adapter_down, preferred_element_type=jnp.float32
    )
    picked = got_ids[:, :, None] == jnp.arange(adapter_down.shape[0], dtype=jnp.int32)
    partial_value = jnp.sum(
        jnp.where(picked[:, :, None, :, None], every_adapter, 0.0), axis=3
    )
    summed = butterfly_sum(partial_value, "tensor").astype(jnp.bfloat16)
    summed = summed.reshape(summed.shape[:3] + (2, adapter_rank_size))
    owner_delta = (
        jnp.einsum("okscr,okcrw->okscw", summed, selected_up, preferred_element_type=jnp.float32)
        * ADAPTER_SCALE
    )
    slot_delta = lax.all_to_all(owner_delta, "replica", split_axis=0, concat_axis=0, tiled=True)
    flat_delta = slot_delta.reshape((replicas * CAP * SLOT,) + slot_delta.shape[3:])
    adapter_delta = flat_delta[fetch_slot[segment_index] * SLOT + token_position]
    base_projection = jnp.einsum(
        "jd,dcw->jcw", normed, key_value_weight, preferred_element_type=jnp.float32
    )
    current_key_value = base_projection + adapter_delta
    rotated = rotate(
        current_key_value[:, 0].reshape(row_count, kv_local, HEAD), cached_length
    ).reshape(row_count, kv_width)
    new_kv = jnp.stack([rotated, current_key_value[:, 1]], axis=1).astype(jnp.bfloat16)
    group_size = query.shape[1] // HEAD // kv_local
    attended = attend(query, key_value_cache, new_kv, cached_length, kv_local, group_size)
    return (new_kv, attended)


def solution(mesh):
    in_specs = (
        P("replica", "tensor"),
        P(),
        P(None, None, "tensor"),
        P("replica", "tensor", None),
        P("replica", None, None, "tensor"),
        P("replica", "tensor"),
        P("replica", None, None, "tensor"),
        P("replica", None),
        P("replica", None),
        P("replica"),
    )
    out_specs = (P("replica", None, "tensor"), P("replica", "tensor"))
    return jax.shard_map(body, mesh=mesh, in_specs=in_specs, out_specs=out_specs, check_vma=False)
```

```python
import functools

import jax
import jax.numpy as jnp
from jax import lax
from jax.experimental import pallas as pl
from jax.experimental.pallas import tpu as pltpu
from jax.sharding import PartitionSpec as P

HEAD = 128
ADP_DEV = 16
SLOT = 4
CAP = 2


ADAPTER_SCALE = 0.5
ROPE_BASE = 500000.0
EPSILON = 1e-05


def rotate(key_heads, token_position):
    half_size = key_heads.shape[-1] // 2
    inv_freq = ROPE_BASE ** (
        -(jnp.arange(half_size, dtype=jnp.float32) * 2.0) / key_heads.shape[-1]
    )
    angles = token_position.astype(jnp.float32)[:, None] * inv_freq[None, :]
    cosine_term = jnp.cos(angles)[:, None, :]
    sine_term = jnp.sin(angles)[:, None, :]
    first_half = key_heads[..., :half_size]
    second_half = key_heads[..., half_size:]
    return jnp.concatenate(
        [
            first_half * cosine_term - second_half * sine_term,
            second_half * cosine_term + first_half * sine_term,
        ],
        axis=-1,
    )


def score_kernel(len_ref, q_ref, kv_ref, s_ref, *, rows, kv_local, group_size):
    scale = float(HEAD) ** (-0.5)
    step = pl.program_id(0)
    cache_len = kv_ref.shape[1]
    width = kv_ref.shape[3]
    pos = lax.broadcasted_iota(jnp.int32, (group_size, 2 * cache_len), 1)
    for i in range(rows):
        length = len_ref[step * rows + i]
        stacked = kv_ref[i].reshape(2 * cache_len, width)
        live = (pos % 2 == 0) & (pos < 2 * length)
        for h in range(kv_local):
            cols = slice(h * HEAD, (h + 1) * HEAD)
            qrows = slice(h * group_size, (h + 1) * group_size)
            scores = lax.dot_general(
                q_ref[i, qrows, :], stacked[:, cols], (((1,), (1,)), ((), ())),
                preferred_element_type=jnp.float32,
            ) * scale
            s_ref[i, qrows, :] = jnp.where(live, scores, -jnp.inf)


def mix_kernel(q_ref, s_ref, kv_ref, nkv_ref, o_ref, *, rows, kv_local, group_size):
    scale = float(HEAD) ** (-0.5)
    cache_len = kv_ref.shape[1]
    width = kv_ref.shape[3]
    for i in range(rows):
        stacked = kv_ref[i].reshape(2 * cache_len, width)
        for h in range(kv_local):
            cols = slice(h * HEAD, (h + 1) * HEAD)
            qrows = slice(h * group_size, (h + 1) * group_size)
            q = q_ref[i, qrows, :]
            scores = s_ref[i, qrows, :]
            new_key = nkv_ref[i, 0:1, cols].astype(jnp.float32)
            new_value = nkv_ref[i, 1:2, cols].astype(jnp.float32)
            own = jnp.sum(q.astype(jnp.float32) * new_key, axis=1, keepdims=True) * scale
            top = jnp.maximum(jnp.max(scores, axis=1, keepdims=True), own)
            weights = jnp.exp(scores - top)
            own_weight = jnp.exp(own - top)
            total = jnp.sum(weights, axis=1, keepdims=True) + own_weight
            probs = pltpu.roll(weights / total, 1, 1).astype(jnp.bfloat16)
            own_prob = (own_weight / total).astype(jnp.bfloat16).astype(jnp.float32)
            context = jnp.dot(probs, stacked[:, cols], preferred_element_type=jnp.float32)
            context = context + own_prob * new_value
            context = context.astype(o_ref.dtype)
            for g in range(group_size):
                lanes = slice((h * group_size + g) * HEAD, (h * group_size + g + 1) * HEAD)
                o_ref[i:i + 1, lanes] = context[g:g + 1]


def attend(query, key_value_cache, new_kv, cached_length, kv_local, group_size):
    row_count = query.shape[0]
    cache_len = key_value_cache.shape[1]
    width = key_value_cache.shape[3]
    heads = kv_local * group_size
    rows = 8 if row_count % 8 == 0 else row_count
    query_heads = query.reshape(row_count, heads, HEAD)
    opts = dict(rows=rows, kv_local=kv_local, group_size=group_size)
    cache_spec = pl.BlockSpec((rows, cache_len, 2, width), lambda b, *_: (b, 0, 0, 0))
    head_spec = pl.BlockSpec((rows, heads, HEAD), lambda b, *_: (b, 0, 0))
    score_spec = pl.BlockSpec((rows, heads, 2 * cache_len), lambda b, *_: (b, 0, 0))
    scores = pl.pallas_call(
        functools.partial(score_kernel, **opts),
        out_shape=jax.ShapeDtypeStruct((row_count, heads, 2 * cache_len), jnp.float32),
        grid_spec=pltpu.PrefetchScalarGridSpec(
            num_scalar_prefetch=1,
            grid=(row_count // rows,),
            in_specs=[head_spec, cache_spec],
            out_specs=score_spec,
        ),
    )(cached_length, query_heads, key_value_cache)
    mix_rows = 8 if row_count % 8 == 0 else row_count
    out = pl.pallas_call(
        functools.partial(mix_kernel, rows=mix_rows, kv_local=kv_local, group_size=group_size),
        out_shape=jax.ShapeDtypeStruct((row_count, heads * HEAD), jnp.bfloat16),
        grid=(row_count // mix_rows,),
        in_specs=[
            pl.BlockSpec((mix_rows, heads, HEAD), lambda b: (b, 0, 0)),
            pl.BlockSpec((mix_rows, heads, 2 * cache_len), lambda b: (b, 0, 0)),
            pl.BlockSpec((mix_rows, cache_len, 2, width), lambda b: (b, 0, 0, 0)),
            pl.BlockSpec((mix_rows, 2, width), lambda b: (b, 0, 0)),
        ],
        out_specs=pl.BlockSpec((mix_rows, heads * HEAD), lambda b: (b, 0)),
    )(query_heads, scores, key_value_cache, new_kv)
    return out


def butterfly_sum(value, axis):
    size = lax.axis_size(axis)
    if size & (size - 1):
        return lax.psum(value, axis)
    stride = 1
    while stride < size:
        pairs = [(i, i ^ stride) for i in range(size)]
        value = value + lax.ppermute(value, axis, pairs)
        stride *= 2
    return value


def butterfly_gather(value, axis):
    size = lax.axis_size(axis)
    if size & (size - 1):
        return lax.all_gather(value, axis, axis=1, tiled=True)
    index = lax.axis_index(axis)
    stride = 1
    while stride < size:
        pairs = [(i, i ^ stride) for i in range(size)]
        other = lax.ppermute(value, axis, pairs)
        value = jnp.where(
            (index & stride) == 0,
            jnp.concatenate([value, other], axis=1),
            jnp.concatenate([other, value], axis=1),
        )
        stride *= 2
    return value


def body(
    hidden,
    input_norm_gain,
    key_value_weight,
    adapter_down,
    adapter_up,
    query,
    key_value_cache,
    segment_adapter,
    segment_sizes,
    cached_length,
):
    row_count = hidden.shape[0]
    part_width = hidden.shape[1]
    kv_width = key_value_weight.shape[2]
    kv_local = kv_width // HEAD
    cache_len = key_value_cache.shape[1]
    adapter_rank_size = adapter_up.shape[2]
    replicas = lax.axis_size("replica")
    segments = segment_sizes.shape[1]
    local = hidden.astype(jnp.float32)
    squares = butterfly_sum(jnp.sum(local * local, axis=1, keepdims=True), "tensor")
    row_scale = lax.rsqrt(squares / (part_width * lax.axis_size("tensor")) + EPSILON)
    own_gain = lax.dynamic_slice_in_dim(
        input_norm_gain, lax.axis_index("tensor") * part_width, part_width, 0
    )
    own_cols = (local * row_scale * own_gain).astype(jnp.bfloat16)
    gathered = butterfly_gather(hidden, "tensor")
    normed = (gathered.astype(jnp.float32) * row_scale * input_norm_gain).astype(jnp.bfloat16)
    seg_counts = segment_sizes[0]
    adapters = segment_adapter[0]
    seg_ends = jnp.cumsum(seg_counts, dtype=jnp.int32)
    starts = seg_ends - seg_counts
    offsets = jnp.arange(SLOT, dtype=jnp.int32)
    row_ids = jnp.arange(row_count, dtype=jnp.int32)
    segment_index = jnp.sum((seg_ends[None, :] <= row_ids[:, None]).astype(jnp.int32), axis=1)
    token_position = row_ids - starts[segment_index]
    owners = adapters // ADP_DEV
    local_ids = adapters % ADP_DEV
    seg_ids = jnp.arange(segments, dtype=jnp.int32)
    slot_rank = jnp.sum(
        ((owners[None, :] == owners[:, None]) & (seg_ids[None, :] < seg_ids[:, None])).astype(
            jnp.int32
        ),
        axis=1,
    )
    owner_hit = (owners[None, None, :] == jnp.arange(replicas, dtype=jnp.int32)[:, None, None]) & (
        slot_rank[None, None, :] == jnp.arange(CAP, dtype=jnp.int32)[None, :, None]
    )
    wanted = jnp.sum(jnp.where(owner_hit, local_ids[None, None, :], 0), axis=2)
    fetch_slot = owners * CAP + slot_rank
    seg_at = jnp.sum(jnp.where(owner_hit, seg_ids[None, None, :], 0), axis=2)
    filled = jnp.any(owner_hit, axis=2)
    slot_counts = jnp.where(filled, seg_counts[seg_at], 0)
    slot_live = offsets[None, None, :] < slot_counts[:, :, None]
    source_row = jnp.where(slot_live, starts[seg_at][:, :, None] + offsets[None, None, :], 0)
    slot_rows = jnp.where(
        slot_live[:, :, :, None], own_cols[source_row], jnp.zeros((), jnp.bfloat16)
    )
    tags = jnp.broadcast_to(
        wanted.astype(jnp.bfloat16)[:, :, None, None], wanted.shape + (SLOT, HEAD)
    )
    payload = jnp.concatenate([slot_rows, tags], axis=3)
    got = lax.all_to_all(payload, "replica", split_axis=0, concat_axis=0, tiled=True)
    got_rows = got[..., :part_width]
    got_ids = got[:, :, 0, part_width].astype(jnp.int32)
    selected_up = adapter_up[got_ids]
    every_adapter = jnp.einsum(
        "oksd,adr->oksar", got_rows, adapter_down, preferred_element_type=jnp.float32
    )
    picked = got_ids[:, :, None] == jnp.arange(adapter_down.shape[0], dtype=jnp.int32)
    partial_value = jnp.sum(
        jnp.where(picked[:, :, None, :, None], every_adapter, 0.0), axis=3
    )
    summed = butterfly_sum(partial_value, "tensor").astype(jnp.bfloat16)
    summed = summed.reshape(summed.shape[:3] + (2, adapter_rank_size))
    owner_delta = (
        jnp.einsum("okscr,okcrw->okscw", summed, selected_up, preferred_element_type=jnp.float32)
        * ADAPTER_SCALE
    )
    slot_delta = lax.all_to_all(owner_delta, "replica", split_axis=0, concat_axis=0, tiled=True)
    flat_delta = slot_delta.reshape((replicas * CAP * SLOT,) + slot_delta.shape[3:])
    adapter_delta = flat_delta[fetch_slot[segment_index] * SLOT + token_position]
    base_projection = jnp.einsum(
        "jd,dcw->jcw", normed, key_value_weight, preferred_element_type=jnp.float32
    )
    current_key_value = base_projection + adapter_delta
    rotated = rotate(
        current_key_value[:, 0].reshape(row_count, kv_local, HEAD), cached_length
    ).reshape(row_count, kv_width)
    new_kv = jnp.stack([rotated, current_key_value[:, 1]], axis=1).astype(jnp.bfloat16)
    group_size = query.shape[1] // HEAD // kv_local
    attended = attend(query, key_value_cache, new_kv, cached_length, kv_local, group_size)
    return (new_kv, attended)


def solution(mesh):
    in_specs = (
        P("replica", "tensor"),
        P(),
        P(None, None, "tensor"),
        P("replica", "tensor", None),
        P("replica", None, None, "tensor"),
        P("replica", "tensor"),
        P("replica", None, None, "tensor"),
        P("replica", None),
        P("replica", None),
        P("replica"),
    )
    out_specs = (P("replica", None, "tensor"), P("replica", "tensor"))
    return jax.shard_map(body, mesh=mesh, in_specs=in_specs, out_specs=out_specs, check_vma=False)
```

```python
import functools

import jax
import jax.numpy as jnp
from jax import lax
from jax.experimental import pallas as pl
from jax.experimental.pallas import tpu as pltpu
from jax.sharding import PartitionSpec as P

HEAD = 128
ADP_DEV = 16
SLOT = 4
CAP = 2


ADAPTER_SCALE = 0.5
ROPE_BASE = 500000.0
EPSILON = 1e-05


def rotate(key_heads, token_position):
    half_size = key_heads.shape[-1] // 2
    inv_freq = ROPE_BASE ** (
        -(jnp.arange(half_size, dtype=jnp.float32) * 2.0) / key_heads.shape[-1]
    )
    angles = token_position.astype(jnp.float32)[:, None] * inv_freq[None, :]
    cosine_term = jnp.cos(angles)[:, None, :]
    sine_term = jnp.sin(angles)[:, None, :]
    first_half = key_heads[..., :half_size]
    second_half = key_heads[..., half_size:]
    return jnp.concatenate(
        [
            first_half * cosine_term - second_half * sine_term,
            second_half * cosine_term + first_half * sine_term,
        ],
        axis=-1,
    )


def score_kernel(len_ref, q_ref, kv_ref, s_ref, *, rows, kv_local, group_size):
    scale = float(HEAD) ** (-0.5)
    step = pl.program_id(0)
    cache_len = kv_ref.shape[1]
    width = kv_ref.shape[3]
    pos = lax.broadcasted_iota(jnp.int32, (group_size, 2 * cache_len), 1)
    for i in range(rows):
        length = len_ref[step * rows + i]
        stacked = kv_ref[i].reshape(2 * cache_len, width)
        live = (pos % 2 == 0) & (pos < 2 * length)
        for h in range(kv_local):
            cols = slice(h * HEAD, (h + 1) * HEAD)
            qrows = slice(h * group_size, (h + 1) * group_size)
            scores = lax.dot_general(
                q_ref[i, qrows, :], stacked[:, cols], (((1,), (1,)), ((), ())),
                preferred_element_type=jnp.float32,
            ) * scale
            s_ref[i, qrows, :] = jnp.where(live, scores, -jnp.inf)


def mix_kernel(q_ref, s_ref, kv_ref, nkv_ref, o_ref, *, rows, kv_local, group_size):
    scale = float(HEAD) ** (-0.5)
    cache_len = kv_ref.shape[1]
    width = kv_ref.shape[3]
    for i in range(rows):
        stacked = kv_ref[i].reshape(2 * cache_len, width)
        for h in range(kv_local):
            cols = slice(h * HEAD, (h + 1) * HEAD)
            qrows = slice(h * group_size, (h + 1) * group_size)
            q = q_ref[i, qrows, :]
            scores = s_ref[i, qrows, :]
            new_key = nkv_ref[i, 0:1, cols].astype(jnp.float32)
            new_value = nkv_ref[i, 1:2, cols].astype(jnp.float32)
            own = jnp.sum(q.astype(jnp.float32) * new_key, axis=1, keepdims=True) * scale
            top = jnp.maximum(jnp.max(scores, axis=1, keepdims=True), own)
            weights = jnp.exp(scores - top)
            own_weight = jnp.exp(own - top)
            total = jnp.sum(weights, axis=1, keepdims=True) + own_weight
            probs = pltpu.roll(weights / total, 1, 1).astype(jnp.bfloat16)
            own_prob = (own_weight / total).astype(jnp.bfloat16).astype(jnp.float32)
            context = jnp.dot(probs, stacked[:, cols], preferred_element_type=jnp.float32)
            context = context + own_prob * new_value
            context = context.astype(o_ref.dtype)
            for g in range(group_size):
                lanes = slice((h * group_size + g) * HEAD, (h * group_size + g + 1) * HEAD)
                o_ref[i:i + 1, lanes] = context[g:g + 1]


def attend(query, key_value_cache, new_kv, cached_length, kv_local, group_size):
    row_count = query.shape[0]
    cache_len = key_value_cache.shape[1]
    width = key_value_cache.shape[3]
    heads = kv_local * group_size
    rows = 8 if row_count % 8 == 0 else row_count
    query_heads = query.reshape(row_count, heads, HEAD)
    opts = dict(rows=rows, kv_local=kv_local, group_size=group_size)
    cache_spec = pl.BlockSpec((rows, cache_len, 2, width), lambda b, *_: (b, 0, 0, 0))
    head_spec = pl.BlockSpec((rows, heads, HEAD), lambda b, *_: (b, 0, 0))
    score_spec = pl.BlockSpec((rows, heads, 2 * cache_len), lambda b, *_: (b, 0, 0))
    scores = pl.pallas_call(
        functools.partial(score_kernel, **opts),
        out_shape=jax.ShapeDtypeStruct((row_count, heads, 2 * cache_len), jnp.float32),
        grid_spec=pltpu.PrefetchScalarGridSpec(
            num_scalar_prefetch=1,
            grid=(row_count // rows,),
            in_specs=[head_spec, cache_spec],
            out_specs=score_spec,
        ),
    )(cached_length, query_heads, key_value_cache)
    mix_rows = 8 if row_count % 8 == 0 else row_count
    out = pl.pallas_call(
        functools.partial(mix_kernel, rows=mix_rows, kv_local=kv_local, group_size=group_size),
        out_shape=jax.ShapeDtypeStruct((row_count, heads * HEAD), jnp.bfloat16),
        grid=(row_count // mix_rows,),
        in_specs=[
            pl.BlockSpec((mix_rows, heads, HEAD), lambda b: (b, 0, 0)),
            pl.BlockSpec((mix_rows, heads, 2 * cache_len), lambda b: (b, 0, 0)),
            pl.BlockSpec((mix_rows, cache_len, 2, width), lambda b: (b, 0, 0, 0)),
            pl.BlockSpec((mix_rows, 2, width), lambda b: (b, 0, 0)),
        ],
        out_specs=pl.BlockSpec((mix_rows, heads * HEAD), lambda b: (b, 0)),
    )(query_heads, scores, key_value_cache, new_kv)
    return out


def butterfly_sum(value, axis):
    size = lax.axis_size(axis)
    if size & (size - 1):
        return lax.psum(value, axis)
    stride = 1
    while stride < size:
        pairs = [(i, i ^ stride) for i in range(size)]
        value = value + lax.ppermute(value, axis, pairs)
        stride *= 2
    return value


def butterfly_gather(value, axis):
    size = lax.axis_size(axis)
    if size & (size - 1):
        return lax.all_gather(value, axis, axis=1, tiled=True)
    index = lax.axis_index(axis)
    stride = 1
    while stride < size:
        pairs = [(i, i ^ stride) for i in range(size)]
        other = lax.ppermute(value, axis, pairs)
        value = jnp.where(
            (index & stride) == 0,
            jnp.concatenate([value, other], axis=1),
            jnp.concatenate([other, value], axis=1),
        )
        stride *= 2
    return value


def body(
    hidden,
    input_norm_gain,
    key_value_weight,
    adapter_down,
    adapter_up,
    query,
    key_value_cache,
    segment_adapter,
    segment_sizes,
    cached_length,
):
    row_count = hidden.shape[0]
    part_width = hidden.shape[1]
    kv_width = key_value_weight.shape[2]
    kv_local = kv_width // HEAD
    cache_len = key_value_cache.shape[1]
    adapter_rank_size = adapter_up.shape[2]
    replicas = lax.axis_size("replica")
    segments = segment_sizes.shape[1]
    local = hidden.astype(jnp.float32)
    squares = butterfly_sum(jnp.sum(local * local, axis=1, keepdims=True), "tensor")
    row_scale = lax.rsqrt(squares / (part_width * lax.axis_size("tensor")) + EPSILON)
    own_gain = lax.dynamic_slice_in_dim(
        input_norm_gain, lax.axis_index("tensor") * part_width, part_width, 0
    )
    own_cols = (local * row_scale * own_gain).astype(jnp.bfloat16)
    gathered = lax.all_gather(hidden, "tensor", axis=1, tiled=True)
    normed = (gathered.astype(jnp.float32) * row_scale * input_norm_gain).astype(jnp.bfloat16)
    seg_counts = segment_sizes[0]
    adapters = segment_adapter[0]
    seg_ends = jnp.cumsum(seg_counts, dtype=jnp.int32)
    starts = seg_ends - seg_counts
    offsets = jnp.arange(SLOT, dtype=jnp.int32)
    row_ids = jnp.arange(row_count, dtype=jnp.int32)
    segment_index = jnp.sum((seg_ends[None, :] <= row_ids[:, None]).astype(jnp.int32), axis=1)
    token_position = row_ids - starts[segment_index]
    owners = adapters // ADP_DEV
    local_ids = adapters % ADP_DEV
    seg_ids = jnp.arange(segments, dtype=jnp.int32)
    slot_rank = jnp.sum(
        ((owners[None, :] == owners[:, None]) & (seg_ids[None, :] < seg_ids[:, None])).astype(
            jnp.int32
        ),
        axis=1,
    )
    owner_hit = (owners[None, None, :] == jnp.arange(replicas, dtype=jnp.int32)[:, None, None]) & (
        slot_rank[None, None, :] == jnp.arange(CAP, dtype=jnp.int32)[None, :, None]
    )
    wanted = jnp.sum(jnp.where(owner_hit, local_ids[None, None, :], 0), axis=2)
    fetch_slot = owners * CAP + slot_rank
    seg_at = jnp.sum(jnp.where(owner_hit, seg_ids[None, None, :], 0), axis=2)
    filled = jnp.any(owner_hit, axis=2)
    slot_counts = jnp.where(filled, seg_counts[seg_at], 0)
    slot_live = offsets[None, None, :] < slot_counts[:, :, None]
    source_row = jnp.where(slot_live, starts[seg_at][:, :, None] + offsets[None, None, :], 0)
    slot_rows = jnp.where(
        slot_live[:, :, :, None], own_cols[source_row], jnp.zeros((), jnp.bfloat16)
    )
    tags = jnp.broadcast_to(
        wanted.astype(jnp.bfloat16)[:, :, None, None], wanted.shape + (SLOT, HEAD)
    )
    payload = jnp.concatenate([slot_rows, tags], axis=3)
    got = lax.all_to_all(payload, "replica", split_axis=0, concat_axis=0, tiled=True)
    got_rows = got[..., :part_width]
    got_ids = got[:, :, 0, part_width].astype(jnp.int32)
    selected_up = adapter_up[got_ids]
    every_adapter = jnp.einsum(
        "oksd,adr->oksar", got_rows, adapter_down, preferred_element_type=jnp.float32
    )
    picked = got_ids[:, :, None] == jnp.arange(adapter_down.shape[0], dtype=jnp.int32)
    partial_value = jnp.sum(
        jnp.where(picked[:, :, None, :, None], every_adapter, 0.0), axis=3
    )
    summed = butterfly_sum(partial_value, "tensor").astype(jnp.bfloat16)
    summed = summed.reshape(summed.shape[:3] + (2, adapter_rank_size))
    owner_delta = (
        jnp.einsum("okscr,okcrw->okscw", summed, selected_up, preferred_element_type=jnp.float32)
        * ADAPTER_SCALE
    )
    slot_delta = lax.all_to_all(owner_delta, "replica", split_axis=0, concat_axis=0, tiled=True)
    flat_delta = slot_delta.reshape((replicas * CAP * SLOT,) + slot_delta.shape[3:])
    adapter_delta = flat_delta[fetch_slot[segment_index] * SLOT + token_position]
    base_projection = jnp.einsum(
        "jd,dcw->jcw", normed, key_value_weight, preferred_element_type=jnp.float32
    )
    current_key_value = base_projection + adapter_delta
    rotated = rotate(
        current_key_value[:, 0].reshape(row_count, kv_local, HEAD), cached_length
    ).reshape(row_count, kv_width)
    new_kv = jnp.stack([rotated, current_key_value[:, 1]], axis=1).astype(jnp.bfloat16)
    group_size = query.shape[1] // HEAD // kv_local
    attended = attend(query, key_value_cache, new_kv, cached_length, kv_local, group_size)
    return (new_kv, attended)


def solution(mesh):
    in_specs = (
        P("replica", "tensor"),
        P(),
        P(None, None, "tensor"),
        P("replica", "tensor", None),
        P("replica", None, None, "tensor"),
        P("replica", "tensor"),
        P("replica", None, None, "tensor"),
        P("replica", None),
        P("replica", None),
        P("replica"),
    )
    out_specs = (P("replica", None, "tensor"), P("replica", "tensor"))
    return jax.shard_map(body, mesh=mesh, in_specs=in_specs, out_specs=out_specs, check_vma=False)
```

```python
import functools

import jax
import jax.numpy as jnp
from jax import lax
from jax.experimental import pallas as pl
from jax.experimental.pallas import tpu as pltpu
from jax.sharding import PartitionSpec as P

HEAD = 128
ADP_DEV = 16
SLOT = 4
CAP = 2


ADAPTER_SCALE = 0.5
ROPE_BASE = 500000.0
EPSILON = 1e-05


def rotate(key_heads, token_position):
    half_size = key_heads.shape[-1] // 2
    inv_freq = ROPE_BASE ** (
        -(jnp.arange(half_size, dtype=jnp.float32) * 2.0) / key_heads.shape[-1]
    )
    angles = token_position.astype(jnp.float32)[:, None] * inv_freq[None, :]
    cosine_term = jnp.cos(angles)[:, None, :]
    sine_term = jnp.sin(angles)[:, None, :]
    first_half = key_heads[..., :half_size]
    second_half = key_heads[..., half_size:]
    return jnp.concatenate(
        [
            first_half * cosine_term - second_half * sine_term,
            second_half * cosine_term + first_half * sine_term,
        ],
        axis=-1,
    )


def head_rows(q_ref, i, h, group_size):
    return jnp.concatenate(
        [
            q_ref[i:i + 1, (h * group_size + g) * HEAD:(h * group_size + g + 1) * HEAD]
            for g in range(group_size)
        ],
        axis=0,
    )


def score_kernel(len_ref, q_ref, kv_ref, s_ref, *, rows, kv_local, group_size):
    scale = float(HEAD) ** (-0.5)
    step = pl.program_id(0)
    cache_len = kv_ref.shape[1]
    width = kv_ref.shape[3]
    pos = lax.broadcasted_iota(jnp.int32, (group_size, 2 * cache_len), 1)
    for i in range(rows):
        length = len_ref[step * rows + i]
        stacked = kv_ref[i].reshape(2 * cache_len, width)
        live = (pos % 2 == 0) & (pos < 2 * length)
        for h in range(kv_local):
            cols = slice(h * HEAD, (h + 1) * HEAD)
            qrows = slice(h * group_size, (h + 1) * group_size)
            scores = lax.dot_general(
                head_rows(q_ref, i, h, group_size), stacked[:, cols], (((1,), (1,)), ((), ())),
                preferred_element_type=jnp.float32,
            ) * scale
            s_ref[i, qrows, :] = jnp.where(live, scores, -jnp.inf)


def mix_kernel(q_ref, s_ref, kv_ref, nkv_ref, o_ref, *, rows, kv_local, group_size):
    scale = float(HEAD) ** (-0.5)
    cache_len = kv_ref.shape[1]
    width = kv_ref.shape[3]
    for i in range(rows):
        stacked = kv_ref[i].reshape(2 * cache_len, width)
        for h in range(kv_local):
            cols = slice(h * HEAD, (h + 1) * HEAD)
            qrows = slice(h * group_size, (h + 1) * group_size)
            q = head_rows(q_ref, i, h, group_size)
            scores = s_ref[i, qrows, :]
            new_key = nkv_ref[i, 0:1, cols].astype(jnp.float32)
            new_value = nkv_ref[i, 1:2, cols].astype(jnp.float32)
            own = jnp.sum(q.astype(jnp.float32) * new_key, axis=1, keepdims=True) * scale
            top = jnp.maximum(jnp.max(scores, axis=1, keepdims=True), own)
            weights = jnp.exp(scores - top)
            own_weight = jnp.exp(own - top)
            total = jnp.sum(weights, axis=1, keepdims=True) + own_weight
            probs = pltpu.roll(weights / total, 1, 1).astype(jnp.bfloat16)
            own_prob = (own_weight / total).astype(jnp.bfloat16).astype(jnp.float32)
            context = jnp.dot(probs, stacked[:, cols], preferred_element_type=jnp.float32)
            context = context + own_prob * new_value
            context = context.astype(o_ref.dtype)
            for g in range(group_size):
                lanes = slice((h * group_size + g) * HEAD, (h * group_size + g + 1) * HEAD)
                o_ref[i:i + 1, lanes] = context[g:g + 1]


def attend(query, key_value_cache, new_kv, cached_length, kv_local, group_size):
    row_count = query.shape[0]
    cache_len = key_value_cache.shape[1]
    width = key_value_cache.shape[3]
    heads = kv_local * group_size
    rows = 8 if row_count % 8 == 0 else row_count
    query_heads = query
    opts = dict(rows=rows, kv_local=kv_local, group_size=group_size)
    cache_spec = pl.BlockSpec((rows, cache_len, 2, width), lambda b, *_: (b, 0, 0, 0))
    head_spec = pl.BlockSpec((rows, heads * HEAD), lambda b, *_: (b, 0))
    score_spec = pl.BlockSpec((rows, heads, 2 * cache_len), lambda b, *_: (b, 0, 0))
    scores = pl.pallas_call(
        functools.partial(score_kernel, **opts),
        out_shape=jax.ShapeDtypeStruct((row_count, heads, 2 * cache_len), jnp.float32),
        grid_spec=pltpu.PrefetchScalarGridSpec(
            num_scalar_prefetch=1,
            grid=(row_count // rows,),
            in_specs=[head_spec, cache_spec],
            out_specs=score_spec,
        ),
    )(cached_length, query_heads, key_value_cache)
    mix_rows = 8 if row_count % 8 == 0 else row_count
    out = pl.pallas_call(
        functools.partial(mix_kernel, rows=mix_rows, kv_local=kv_local, group_size=group_size),
        out_shape=jax.ShapeDtypeStruct((row_count, heads * HEAD), jnp.bfloat16),
        grid=(row_count // mix_rows,),
        in_specs=[
            pl.BlockSpec((mix_rows, heads * HEAD), lambda b: (b, 0)),
            pl.BlockSpec((mix_rows, heads, 2 * cache_len), lambda b: (b, 0, 0)),
            pl.BlockSpec((mix_rows, cache_len, 2, width), lambda b: (b, 0, 0, 0)),
            pl.BlockSpec((mix_rows, 2, width), lambda b: (b, 0, 0)),
        ],
        out_specs=pl.BlockSpec((mix_rows, heads * HEAD), lambda b: (b, 0)),
    )(query_heads, scores, key_value_cache, new_kv)
    return out


def butterfly_sum(value, axis):
    size = lax.axis_size(axis)
    if size & (size - 1):
        return lax.psum(value, axis)
    stride = 1
    while stride < size:
        pairs = [(i, i ^ stride) for i in range(size)]
        value = value + lax.ppermute(value, axis, pairs)
        stride *= 2
    return value


def body(
    hidden,
    input_norm_gain,
    key_value_weight,
    adapter_down,
    adapter_up,
    query,
    key_value_cache,
    segment_adapter,
    segment_sizes,
    cached_length,
):
    row_count = hidden.shape[0]
    part_width = hidden.shape[1]
    kv_width = key_value_weight.shape[2]
    kv_local = kv_width // HEAD
    cache_len = key_value_cache.shape[1]
    adapter_rank_size = adapter_up.shape[2]
    replicas = lax.axis_size("replica")
    segments = segment_sizes.shape[1]
    gathered = lax.all_gather(hidden, "tensor", axis=1, tiled=True)
    widened = gathered.astype(jnp.float32)
    normed = (
        widened
        * lax.rsqrt(jnp.mean(widened * widened, axis=1, keepdims=True) + EPSILON)
        * input_norm_gain
    ).astype(jnp.bfloat16)
    own_cols = lax.dynamic_slice_in_dim(
        normed, lax.axis_index("tensor") * part_width, part_width, 1
    )
    seg_counts = segment_sizes[0]
    adapters = segment_adapter[0]
    seg_ends = jnp.cumsum(seg_counts, dtype=jnp.int32)
    starts = seg_ends - seg_counts
    offsets = jnp.arange(SLOT, dtype=jnp.int32)
    row_ids = jnp.arange(row_count, dtype=jnp.int32)
    segment_index = jnp.sum((seg_ends[None, :] <= row_ids[:, None]).astype(jnp.int32), axis=1)
    token_position = row_ids - starts[segment_index]
    owners = adapters // ADP_DEV
    local_ids = adapters % ADP_DEV
    seg_ids = jnp.arange(segments, dtype=jnp.int32)
    slot_rank = jnp.sum(
        ((owners[None, :] == owners[:, None]) & (seg_ids[None, :] < seg_ids[:, None])).astype(
            jnp.int32
        ),
        axis=1,
    )
    owner_hit = (owners[None, None, :] == jnp.arange(replicas, dtype=jnp.int32)[:, None, None]) & (
        slot_rank[None, None, :] == jnp.arange(CAP, dtype=jnp.int32)[None, :, None]
    )
    wanted = jnp.sum(jnp.where(owner_hit, local_ids[None, None, :], 0), axis=2)
    fetch_slot = owners * CAP + slot_rank
    seg_at = jnp.sum(jnp.where(owner_hit, seg_ids[None, None, :], 0), axis=2)
    filled = jnp.any(owner_hit, axis=2)
    slot_counts = jnp.where(filled, seg_counts[seg_at], 0)
    slot_live = offsets[None, None, :] < slot_counts[:, :, None]
    source_row = jnp.where(slot_live, starts[seg_at][:, :, None] + offsets[None, None, :], 0)
    slot_rows = jnp.where(
        slot_live[:, :, :, None], own_cols[source_row], jnp.zeros((), jnp.bfloat16)
    )
    tags = jnp.broadcast_to(
        wanted.astype(jnp.bfloat16)[:, :, None, None], wanted.shape + (SLOT, HEAD)
    )
    payload = jnp.concatenate([slot_rows, tags], axis=3)
    got = lax.all_to_all(payload, "replica", split_axis=0, concat_axis=0, tiled=True)
    got_rows = got[..., :part_width]
    got_ids = got[:, :, 0, part_width].astype(jnp.int32)
    selected_up = adapter_up[got_ids]
    every_adapter = jnp.einsum(
        "oksd,adr->oksar", got_rows, adapter_down, preferred_element_type=jnp.float32
    )
    picked = got_ids[:, :, None] == jnp.arange(adapter_down.shape[0], dtype=jnp.int32)
    partial_value = jnp.sum(
        jnp.where(picked[:, :, None, :, None], every_adapter, 0.0), axis=3
    )
    summed = butterfly_sum(partial_value, "tensor").astype(jnp.bfloat16)
    summed = summed.reshape(summed.shape[:3] + (2, adapter_rank_size))
    owner_delta = (
        jnp.einsum("okscr,okcrw->okscw", summed, selected_up, preferred_element_type=jnp.float32)
        * ADAPTER_SCALE
    )
    slot_delta = lax.all_to_all(owner_delta, "replica", split_axis=0, concat_axis=0, tiled=True)
    flat_delta = slot_delta.reshape((replicas * CAP * SLOT,) + slot_delta.shape[3:])
    adapter_delta = flat_delta[fetch_slot[segment_index] * SLOT + token_position]
    base_projection = jnp.einsum(
        "jd,dcw->jcw", normed, key_value_weight, preferred_element_type=jnp.float32
    )
    current_key_value = base_projection + adapter_delta
    rotated = rotate(
        current_key_value[:, 0].reshape(row_count, kv_local, HEAD), cached_length
    ).reshape(row_count, kv_width)
    new_kv = jnp.stack([rotated, current_key_value[:, 1]], axis=1).astype(jnp.bfloat16)
    group_size = query.shape[1] // HEAD // kv_local
    attended = attend(query, key_value_cache, new_kv, cached_length, kv_local, group_size)
    return (new_kv, attended)


def solution(mesh):
    in_specs = (
        P("replica", "tensor"),
        P(),
        P(None, None, "tensor"),
        P("replica", "tensor", None),
        P("replica", None, None, "tensor"),
        P("replica", "tensor"),
        P("replica", None, None, "tensor"),
        P("replica", None),
        P("replica", None),
        P("replica"),
    )
    out_specs = (P("replica", None, "tensor"), P("replica", "tensor"))
    return jax.shard_map(body, mesh=mesh, in_specs=in_specs, out_specs=out_specs, check_vma=False)
```

```python
import functools

import jax
import jax.numpy as jnp
from jax import lax
from jax.experimental import pallas as pl
from jax.experimental.pallas import tpu as pltpu
from jax.sharding import PartitionSpec as P

HEAD = 128
ADP_DEV = 16
SLOT = 4
CAP = 2


ADAPTER_SCALE = 0.5
ROPE_BASE = 500000.0
EPSILON = 1e-05


def rotate(key_heads, token_position):
    half_size = key_heads.shape[-1] // 2
    inv_freq = ROPE_BASE ** (
        -(jnp.arange(half_size, dtype=jnp.float32) * 2.0) / key_heads.shape[-1]
    )
    angles = token_position.astype(jnp.float32)[:, None] * inv_freq[None, :]
    cosine_term = jnp.cos(angles)[:, None, :]
    sine_term = jnp.sin(angles)[:, None, :]
    first_half = key_heads[..., :half_size]
    second_half = key_heads[..., half_size:]
    return jnp.concatenate(
        [
            first_half * cosine_term - second_half * sine_term,
            second_half * cosine_term + first_half * sine_term,
        ],
        axis=-1,
    )


def head_rows(q_ref, i, h, group_size):
    return jnp.concatenate(
        [
            q_ref[i:i + 1, (h * group_size + g) * HEAD:(h * group_size + g + 1) * HEAD]
            for g in range(group_size)
        ],
        axis=0,
    )


def score_kernel(len_ref, q_ref, kv_ref, s_ref, *, rows, kv_local, group_size):
    scale = float(HEAD) ** (-0.5)
    step = pl.program_id(0)
    cache_len = kv_ref.shape[1]
    width = kv_ref.shape[3]
    pos = lax.broadcasted_iota(jnp.int32, (group_size, 2 * cache_len), 1)
    for i in range(rows):
        length = len_ref[step * rows + i]
        stacked = kv_ref[i].reshape(2 * cache_len, width)
        live = (pos % 2 == 0) & (pos < 2 * length)
        for h in range(kv_local):
            cols = slice(h * HEAD, (h + 1) * HEAD)
            qrows = slice(h * group_size, (h + 1) * group_size)
            scores = lax.dot_general(
                head_rows(q_ref, i, h, group_size), stacked[:, cols], (((1,), (1,)), ((), ())),
                preferred_element_type=jnp.float32,
            ) * scale
            s_ref[i, qrows, :] = jnp.where(live, scores, -jnp.inf)


def mix_kernel(q_ref, s_ref, kv_ref, nkv_ref, o_ref, *, rows, kv_local, group_size):
    scale = float(HEAD) ** (-0.5)
    cache_len = kv_ref.shape[1]
    width = kv_ref.shape[3]
    for i in range(rows):
        stacked = kv_ref[i].reshape(2 * cache_len, width)
        for h in range(kv_local):
            cols = slice(h * HEAD, (h + 1) * HEAD)
            qrows = slice(h * group_size, (h + 1) * group_size)
            q = head_rows(q_ref, i, h, group_size)
            scores = s_ref[i, qrows, :]
            new_key = nkv_ref[i, 0:1, cols].astype(jnp.float32)
            new_value = nkv_ref[i, 1:2, cols].astype(jnp.float32)
            own = jnp.sum(q.astype(jnp.float32) * new_key, axis=1, keepdims=True) * scale
            top = jnp.maximum(jnp.max(scores, axis=1, keepdims=True), own)
            weights = jnp.exp(scores - top)
            own_weight = jnp.exp(own - top)
            total = jnp.sum(weights, axis=1, keepdims=True) + own_weight
            probs = pltpu.roll(weights / total, 1, 1).astype(jnp.bfloat16)
            own_prob = (own_weight / total).astype(jnp.bfloat16).astype(jnp.float32)
            context = jnp.dot(probs, stacked[:, cols], preferred_element_type=jnp.float32)
            context = context + own_prob * new_value
            context = context.astype(o_ref.dtype)
            for g in range(group_size):
                lanes = slice((h * group_size + g) * HEAD, (h * group_size + g + 1) * HEAD)
                o_ref[i:i + 1, lanes] = context[g:g + 1]


def attend(query, key_value_cache, new_kv, cached_length, kv_local, group_size):
    row_count = query.shape[0]
    cache_len = key_value_cache.shape[1]
    width = key_value_cache.shape[3]
    heads = kv_local * group_size
    rows = 16 if row_count % 16 == 0 else row_count
    query_heads = query
    opts = dict(rows=rows, kv_local=kv_local, group_size=group_size)
    cache_spec = pl.BlockSpec((rows, cache_len, 2, width), lambda b, *_: (b, 0, 0, 0))
    head_spec = pl.BlockSpec((rows, heads * HEAD), lambda b, *_: (b, 0))
    score_spec = pl.BlockSpec((rows, heads, 2 * cache_len), lambda b, *_: (b, 0, 0))
    scores = pl.pallas_call(
        functools.partial(score_kernel, **opts),
        out_shape=jax.ShapeDtypeStruct((row_count, heads, 2 * cache_len), jnp.float32),
        grid_spec=pltpu.PrefetchScalarGridSpec(
            num_scalar_prefetch=1,
            grid=(row_count // rows,),
            in_specs=[head_spec, cache_spec],
            out_specs=score_spec,
        ),
    )(cached_length, query_heads, key_value_cache)
    mix_rows = 8 if row_count % 8 == 0 else row_count
    out = pl.pallas_call(
        functools.partial(mix_kernel, rows=mix_rows, kv_local=kv_local, group_size=group_size),
        out_shape=jax.ShapeDtypeStruct((row_count, heads * HEAD), jnp.bfloat16),
        grid=(row_count // mix_rows,),
        in_specs=[
            pl.BlockSpec((mix_rows, heads * HEAD), lambda b: (b, 0)),
            pl.BlockSpec((mix_rows, heads, 2 * cache_len), lambda b: (b, 0, 0)),
            pl.BlockSpec((mix_rows, cache_len, 2, width), lambda b: (b, 0, 0, 0)),
            pl.BlockSpec((mix_rows, 2, width), lambda b: (b, 0, 0)),
        ],
        out_specs=pl.BlockSpec((mix_rows, heads * HEAD), lambda b: (b, 0)),
    )(query_heads, scores, key_value_cache, new_kv)
    return out


def butterfly_sum(value, axis):
    size = lax.axis_size(axis)
    if size & (size - 1):
        return lax.psum(value, axis)
    stride = 1
    while stride < size:
        pairs = [(i, i ^ stride) for i in range(size)]
        value = value + lax.ppermute(value, axis, pairs)
        stride *= 2
    return value


def body(
    hidden,
    input_norm_gain,
    key_value_weight,
    adapter_down,
    adapter_up,
    query,
    key_value_cache,
    segment_adapter,
    segment_sizes,
    cached_length,
):
    row_count = hidden.shape[0]
    part_width = hidden.shape[1]
    kv_width = key_value_weight.shape[2]
    kv_local = kv_width // HEAD
    cache_len = key_value_cache.shape[1]
    adapter_rank_size = adapter_up.shape[2]
    replicas = lax.axis_size("replica")
    segments = segment_sizes.shape[1]
    gathered = lax.all_gather(hidden, "tensor", axis=1, tiled=True)
    widened = gathered.astype(jnp.float32)
    normed = (
        widened
        * lax.rsqrt(jnp.mean(widened * widened, axis=1, keepdims=True) + EPSILON)
        * input_norm_gain
    ).astype(jnp.bfloat16)
    own_cols = lax.dynamic_slice_in_dim(
        normed, lax.axis_index("tensor") * part_width, part_width, 1
    )
    seg_counts = segment_sizes[0]
    adapters = segment_adapter[0]
    seg_ends = jnp.cumsum(seg_counts, dtype=jnp.int32)
    starts = seg_ends - seg_counts
    offsets = jnp.arange(SLOT, dtype=jnp.int32)
    row_ids = jnp.arange(row_count, dtype=jnp.int32)
    segment_index = jnp.sum((seg_ends[None, :] <= row_ids[:, None]).astype(jnp.int32), axis=1)
    token_position = row_ids - starts[segment_index]
    owners = adapters // ADP_DEV
    local_ids = adapters % ADP_DEV
    seg_ids = jnp.arange(segments, dtype=jnp.int32)
    slot_rank = jnp.sum(
        ((owners[None, :] == owners[:, None]) & (seg_ids[None, :] < seg_ids[:, None])).astype(
            jnp.int32
        ),
        axis=1,
    )
    owner_hit = (owners[None, None, :] == jnp.arange(replicas, dtype=jnp.int32)[:, None, None]) & (
        slot_rank[None, None, :] == jnp.arange(CAP, dtype=jnp.int32)[None, :, None]
    )
    wanted = jnp.sum(jnp.where(owner_hit, local_ids[None, None, :], 0), axis=2)
    fetch_slot = owners * CAP + slot_rank
    seg_at = jnp.sum(jnp.where(owner_hit, seg_ids[None, None, :], 0), axis=2)
    filled = jnp.any(owner_hit, axis=2)
    slot_counts = jnp.where(filled, seg_counts[seg_at], 0)
    slot_live = offsets[None, None, :] < slot_counts[:, :, None]
    source_row = jnp.where(slot_live, starts[seg_at][:, :, None] + offsets[None, None, :], 0)
    slot_rows = jnp.where(
        slot_live[:, :, :, None], own_cols[source_row], jnp.zeros((), jnp.bfloat16)
    )
    tags = jnp.broadcast_to(
        wanted.astype(jnp.bfloat16)[:, :, None, None], wanted.shape + (SLOT, HEAD)
    )
    payload = jnp.concatenate([slot_rows, tags], axis=3)
    got = lax.all_to_all(payload, "replica", split_axis=0, concat_axis=0, tiled=True)
    got_rows = got[..., :part_width]
    got_ids = got[:, :, 0, part_width].astype(jnp.int32)
    selected_up = adapter_up[got_ids]
    every_adapter = jnp.einsum(
        "oksd,adr->oksar", got_rows, adapter_down, preferred_element_type=jnp.float32
    )
    picked = got_ids[:, :, None] == jnp.arange(adapter_down.shape[0], dtype=jnp.int32)
    partial_value = jnp.sum(
        jnp.where(picked[:, :, None, :, None], every_adapter, 0.0), axis=3
    )
    summed = butterfly_sum(partial_value, "tensor").astype(jnp.bfloat16)
    summed = summed.reshape(summed.shape[:3] + (2, adapter_rank_size))
    owner_delta = (
        jnp.einsum("okscr,okcrw->okscw", summed, selected_up, preferred_element_type=jnp.float32)
        * ADAPTER_SCALE
    )
    slot_delta = lax.all_to_all(owner_delta, "replica", split_axis=0, concat_axis=0, tiled=True)
    flat_delta = slot_delta.reshape((replicas * CAP * SLOT,) + slot_delta.shape[3:])
    adapter_delta = flat_delta[fetch_slot[segment_index] * SLOT + token_position]
    base_projection = jnp.einsum(
        "jd,dcw->jcw", normed, key_value_weight, preferred_element_type=jnp.float32
    )
    current_key_value = base_projection + adapter_delta
    rotated = rotate(
        current_key_value[:, 0].reshape(row_count, kv_local, HEAD), cached_length
    ).reshape(row_count, kv_width)
    new_kv = jnp.stack([rotated, current_key_value[:, 1]], axis=1).astype(jnp.bfloat16)
    group_size = query.shape[1] // HEAD // kv_local
    attended = attend(query, key_value_cache, new_kv, cached_length, kv_local, group_size)
    return (new_kv, attended)


def solution(mesh):
    in_specs = (
        P("replica", "tensor"),
        P(),
        P(None, None, "tensor"),
        P("replica", "tensor", None),
        P("replica", None, None, "tensor"),
        P("replica", "tensor"),
        P("replica", None, None, "tensor"),
        P("replica", None),
        P("replica", None),
        P("replica"),
    )
    out_specs = (P("replica", None, "tensor"), P("replica", "tensor"))
    return jax.shard_map(body, mesh=mesh, in_specs=in_specs, out_specs=out_specs, check_vma=False)
```

```python
import functools

import jax
import jax.numpy as jnp
from jax import lax
from jax.experimental import pallas as pl
from jax.experimental.pallas import tpu as pltpu
from jax.sharding import PartitionSpec as P

HEAD = 128
ADP_DEV = 16
SLOT = 4
CAP = 2


ADAPTER_SCALE = 0.5
ROPE_BASE = 500000.0
EPSILON = 1e-05


def rotate(key_heads, token_position):
    half_size = key_heads.shape[-1] // 2
    inv_freq = ROPE_BASE ** (
        -(jnp.arange(half_size, dtype=jnp.float32) * 2.0) / key_heads.shape[-1]
    )
    angles = token_position.astype(jnp.float32)[:, None] * inv_freq[None, :]
    cosine_term = jnp.cos(angles)[:, None, :]
    sine_term = jnp.sin(angles)[:, None, :]
    first_half = key_heads[..., :half_size]
    second_half = key_heads[..., half_size:]
    return jnp.concatenate(
        [
            first_half * cosine_term - second_half * sine_term,
            second_half * cosine_term + first_half * sine_term,
        ],
        axis=-1,
    )


def head_rows(q_ref, i, h, group_size):
    return jnp.concatenate(
        [
            q_ref[i:i + 1, (h * group_size + g) * HEAD:(h * group_size + g + 1) * HEAD]
            for g in range(group_size)
        ],
        axis=0,
    )


def score_kernel(len_ref, q_ref, kv_ref, s_ref, *, rows, kv_local, group_size):
    scale = float(HEAD) ** (-0.5)
    step = pl.program_id(0)
    cache_len = kv_ref.shape[1]
    width = kv_ref.shape[3]
    pos = lax.broadcasted_iota(jnp.int32, (group_size, 2 * cache_len), 1)
    for i in range(rows):
        length = len_ref[step * rows + i]
        stacked = kv_ref[i].reshape(2 * cache_len, width)
        live = (pos % 2 == 0) & (pos < 2 * length)
        for h in range(kv_local):
            cols = slice(h * HEAD, (h + 1) * HEAD)
            qrows = slice(h * group_size, (h + 1) * group_size)
            scores = lax.dot_general(
                head_rows(q_ref, i, h, group_size), stacked[:, cols], (((1,), (1,)), ((), ())),
                preferred_element_type=jnp.float32,
            ) * scale
            s_ref[i, qrows, :] = jnp.where(live, scores, -jnp.inf)


def mix_kernel(q_ref, s_ref, kv_ref, nkv_ref, o_ref, *, rows, kv_local, group_size):
    scale = float(HEAD) ** (-0.5)
    cache_len = kv_ref.shape[1]
    width = kv_ref.shape[3]
    for i in range(rows):
        stacked = kv_ref[i].reshape(2 * cache_len, width)
        for h in range(kv_local):
            cols = slice(h * HEAD, (h + 1) * HEAD)
            qrows = slice(h * group_size, (h + 1) * group_size)
            q = head_rows(q_ref, i, h, group_size)
            scores = s_ref[i, qrows, :]
            new_key = nkv_ref[i, 0:1, cols].astype(jnp.float32)
            new_value = nkv_ref[i, 1:2, cols].astype(jnp.float32)
            own = jnp.sum(q.astype(jnp.float32) * new_key, axis=1, keepdims=True) * scale
            top = jnp.maximum(jnp.max(scores, axis=1, keepdims=True), own)
            weights = jnp.exp(scores - top)
            own_weight = jnp.exp(own - top)
            total = jnp.sum(weights, axis=1, keepdims=True) + own_weight
            probs = pltpu.roll(weights / total, 1, 1).astype(jnp.bfloat16)
            own_prob = (own_weight / total).astype(jnp.bfloat16).astype(jnp.float32)
            context = jnp.dot(probs, stacked[:, cols], preferred_element_type=jnp.float32)
            context = context + own_prob * new_value
            context = context.astype(o_ref.dtype)
            for g in range(group_size):
                lanes = slice((h * group_size + g) * HEAD, (h * group_size + g + 1) * HEAD)
                o_ref[i:i + 1, lanes] = context[g:g + 1]


def attend(query, key_value_cache, new_kv, cached_length, kv_local, group_size):
    row_count = query.shape[0]
    cache_len = key_value_cache.shape[1]
    width = key_value_cache.shape[3]
    heads = kv_local * group_size
    rows = 8 if row_count % 8 == 0 else row_count
    query_heads = query
    opts = dict(rows=rows, kv_local=kv_local, group_size=group_size)
    cache_spec = pl.BlockSpec((rows, cache_len, 2, width), lambda b, *_: (b, 0, 0, 0))
    head_spec = pl.BlockSpec((rows, heads * HEAD), lambda b, *_: (b, 0))
    score_spec = pl.BlockSpec((rows, heads, 2 * cache_len), lambda b, *_: (b, 0, 0))
    scores = pl.pallas_call(
        functools.partial(score_kernel, **opts),
        out_shape=jax.ShapeDtypeStruct((row_count, heads, 2 * cache_len), jnp.float32),
        grid_spec=pltpu.PrefetchScalarGridSpec(
            num_scalar_prefetch=1,
            grid=(row_count // rows,),
            in_specs=[head_spec, cache_spec],
            out_specs=score_spec,
        ),
    )(cached_length, query_heads, key_value_cache)
    mix_rows = 16 if row_count % 16 == 0 else row_count
    out = pl.pallas_call(
        functools.partial(mix_kernel, rows=mix_rows, kv_local=kv_local, group_size=group_size),
        out_shape=jax.ShapeDtypeStruct((row_count, heads * HEAD), jnp.bfloat16),
        grid=(row_count // mix_rows,),
        in_specs=[
            pl.BlockSpec((mix_rows, heads * HEAD), lambda b: (b, 0)),
            pl.BlockSpec((mix_rows, heads, 2 * cache_len), lambda b: (b, 0, 0)),
            pl.BlockSpec((mix_rows, cache_len, 2, width), lambda b: (b, 0, 0, 0)),
            pl.BlockSpec((mix_rows, 2, width), lambda b: (b, 0, 0)),
        ],
        out_specs=pl.BlockSpec((mix_rows, heads * HEAD), lambda b: (b, 0)),
    )(query_heads, scores, key_value_cache, new_kv)
    return out


def butterfly_sum(value, axis):
    size = lax.axis_size(axis)
    if size & (size - 1):
        return lax.psum(value, axis)
    stride = 1
    while stride < size:
        pairs = [(i, i ^ stride) for i in range(size)]
        value = value + lax.ppermute(value, axis, pairs)
        stride *= 2
    return value


def body(
    hidden,
    input_norm_gain,
    key_value_weight,
    adapter_down,
    adapter_up,
    query,
    key_value_cache,
    segment_adapter,
    segment_sizes,
    cached_length,
):
    row_count = hidden.shape[0]
    part_width = hidden.shape[1]
    kv_width = key_value_weight.shape[2]
    kv_local = kv_width // HEAD
    cache_len = key_value_cache.shape[1]
    adapter_rank_size = adapter_up.shape[2]
    replicas = lax.axis_size("replica")
    segments = segment_sizes.shape[1]
    gathered = lax.all_gather(hidden, "tensor", axis=1, tiled=True)
    widened = gathered.astype(jnp.float32)
    normed = (
        widened
        * lax.rsqrt(jnp.mean(widened * widened, axis=1, keepdims=True) + EPSILON)
        * input_norm_gain
    ).astype(jnp.bfloat16)
    own_cols = lax.dynamic_slice_in_dim(
        normed, lax.axis_index("tensor") * part_width, part_width, 1
    )
    seg_counts = segment_sizes[0]
    adapters = segment_adapter[0]
    seg_ends = jnp.cumsum(seg_counts, dtype=jnp.int32)
    starts = seg_ends - seg_counts
    offsets = jnp.arange(SLOT, dtype=jnp.int32)
    row_ids = jnp.arange(row_count, dtype=jnp.int32)
    segment_index = jnp.sum((seg_ends[None, :] <= row_ids[:, None]).astype(jnp.int32), axis=1)
    token_position = row_ids - starts[segment_index]
    owners = adapters // ADP_DEV
    local_ids = adapters % ADP_DEV
    seg_ids = jnp.arange(segments, dtype=jnp.int32)
    slot_rank = jnp.sum(
        ((owners[None, :] == owners[:, None]) & (seg_ids[None, :] < seg_ids[:, None])).astype(
            jnp.int32
        ),
        axis=1,
    )
    owner_hit = (owners[None, None, :] == jnp.arange(replicas, dtype=jnp.int32)[:, None, None]) & (
        slot_rank[None, None, :] == jnp.arange(CAP, dtype=jnp.int32)[None, :, None]
    )
    wanted = jnp.sum(jnp.where(owner_hit, local_ids[None, None, :], 0), axis=2)
    fetch_slot = owners * CAP + slot_rank
    seg_at = jnp.sum(jnp.where(owner_hit, seg_ids[None, None, :], 0), axis=2)
    filled = jnp.any(owner_hit, axis=2)
    slot_counts = jnp.where(filled, seg_counts[seg_at], 0)
    slot_live = offsets[None, None, :] < slot_counts[:, :, None]
    source_row = jnp.where(slot_live, starts[seg_at][:, :, None] + offsets[None, None, :], 0)
    slot_rows = jnp.where(
        slot_live[:, :, :, None], own_cols[source_row], jnp.zeros((), jnp.bfloat16)
    )
    tags = jnp.broadcast_to(
        wanted.astype(jnp.bfloat16)[:, :, None, None], wanted.shape + (SLOT, HEAD)
    )
    payload = jnp.concatenate([slot_rows, tags], axis=3)
    got = lax.all_to_all(payload, "replica", split_axis=0, concat_axis=0, tiled=True)
    got_rows = got[..., :part_width]
    got_ids = got[:, :, 0, part_width].astype(jnp.int32)
    selected_up = adapter_up[got_ids]
    every_adapter = jnp.einsum(
        "oksd,adr->oksar", got_rows, adapter_down, preferred_element_type=jnp.float32
    )
    picked = got_ids[:, :, None] == jnp.arange(adapter_down.shape[0], dtype=jnp.int32)
    partial_value = jnp.sum(
        jnp.where(picked[:, :, None, :, None], every_adapter, 0.0), axis=3
    )
    summed = butterfly_sum(partial_value, "tensor").astype(jnp.bfloat16)
    summed = summed.reshape(summed.shape[:3] + (2, adapter_rank_size))
    owner_delta = (
        jnp.einsum("okscr,okcrw->okscw", summed, selected_up, preferred_element_type=jnp.float32)
        * ADAPTER_SCALE
    )
    slot_delta = lax.all_to_all(owner_delta, "replica", split_axis=0, concat_axis=0, tiled=True)
    flat_delta = slot_delta.reshape((replicas * CAP * SLOT,) + slot_delta.shape[3:])
    adapter_delta = flat_delta[fetch_slot[segment_index] * SLOT + token_position]
    base_projection = jnp.einsum(
        "jd,dcw->jcw", normed, key_value_weight, preferred_element_type=jnp.float32
    )
    current_key_value = base_projection + adapter_delta
    rotated = rotate(
        current_key_value[:, 0].reshape(row_count, kv_local, HEAD), cached_length
    ).reshape(row_count, kv_width)
    new_kv = jnp.stack([rotated, current_key_value[:, 1]], axis=1).astype(jnp.bfloat16)
    group_size = query.shape[1] // HEAD // kv_local
    attended = attend(query, key_value_cache, new_kv, cached_length, kv_local, group_size)
    return (new_kv, attended)


def solution(mesh):
    in_specs = (
        P("replica", "tensor"),
        P(),
        P(None, None, "tensor"),
        P("replica", "tensor", None),
        P("replica", None, None, "tensor"),
        P("replica", "tensor"),
        P("replica", None, None, "tensor"),
        P("replica", None),
        P("replica", None),
        P("replica"),
    )
    out_specs = (P("replica", None, "tensor"), P("replica", "tensor"))
    return jax.shard_map(body, mesh=mesh, in_specs=in_specs, out_specs=out_specs, check_vma=False)
```
